128 devices in a mesh: ty: 8 (over y, core), tx: 16 (over z, x).
Axes of the slice: x: 4, y: 4, z: 4, core: 2. Of those that a mesh axis runs over, the one named last changes fastest.
Arguments:
- section_a: bfloat16 [4096, 8192], P('ty', 'tx'), may hold values from -6 to 6
- section_b: bfloat16 [4096, 8192], P('ty', 'tx'), may hold values from -6 to 6
- template_corner: int32 [2, 8, 128], P(None, 'ty', 'tx'), may hold values from 0 to 384
- template_slot: int32 [8, 128], P('ty', 'tx'), may hold values from 0 to 31, as said below
- window_corner: int32 [2, 8, 128], P(None, 'ty', 'tx'), may hold values from 0 to 384
- window_slot: int32 [8, 128], P('ty', 'tx'), may hold values from 0 to 31, as said below
- node_mask: int32 [256, 512], P('ty', 'tx'), may hold values 0 or 1
Outputs:
- owner_flow: float32 [2, 8, 128], P(None, 'ty', 'tx')
- source_flow: float32 [2, 8, 128], P(None, 'ty', 'tx')
- displacement: float32 [2, 256, 512], P(None, 'ty', 'tx')
The draws below stay inside these ranges and needn't reach their ends.
Inputs may be any that keep to these rules, and one draw needn't show every extreme that they name: `template_slot`: entry j of a row belongs to owner device j // 8 of that ty row; its value is s * 2 + k for the k-th pair that source device s sends to it; the values of one device's list are distinct; each owner gets exactly 2 pairs from each of 4 sources. `window_slot`: entry m of a row belongs to source device m // 8 of that ty row; its value is o * 2 + k for the k-th pair that it sends to owner device o; the values of one device's list are distinct; together with template_slot every pair of a row appears once on each side.
All inputs are finite; a program needn't handle non-finite values. No bound on the sum of `node_mask` on one device may be relied on, other than what follows from the above.
Results may differ from the reference program's by a relative error of at most 0.0003.
Values may be sent and summed in bfloat16 or wider, within the bound.
No kernel may reach another device: no remote copies, remote signals or barrier semaphores. Data moves between devices by JAX's collectives and lax.ppermute only.
A program may use at most 64 MiB of HBM per device.

```python
import jax
import jax.numpy as jnp
from jax import lax

TILE = 512
PATCH = 128
SHIFTS = 65
RADIUS = 32
WIN = 192
ITEMS_DEV = 8
CAP = 2
ITEMS = 128
MY = 32
MX = 32
ITERS_R = 3
ROWS = 4096
COLS = 8192
NODE_ROWS = 256
NODE_COLS = 512
N_TY = 8
N_TX = 16


def image_draw(key):
    keys = jax.random.split(key, 3)
    image = jnp.clip(jax.random.normal(keys[2], (ROWS, COLS), jnp.float32), -6.0, 6.0)
    return image.astype(jnp.bfloat16)


def draw_section_a(key, part):
    return image_draw(jax.random.fold_in(key, 11))


def draw_section_b(key, part):
    return image_draw(jax.random.fold_in(key, 23))


def item_tables(key):
    groups = ITEMS_DEV // CAP
    span = TILE - PATCH + 1

    def arrange(values, order):
        flat = values.reshape(values.shape[:-3] + (N_TX, ITEMS_DEV))
        picked = jnp.take_along_axis(flat, jnp.broadcast_to(order, flat.shape), axis=-1)
        return picked.reshape(values.shape[:-3] + (N_TX * ITEMS_DEV,))

    def one_row(row_key):
        keys = jax.random.split(row_key, 5)
        shifts = jax.random.permutation(keys[0], N_TX)[:groups]
        sigma = jax.random.permutation(keys[1], N_TX)
        inverse = jnp.argsort(sigma)
        corners = jax.random.randint(keys[2], (4, N_TX, groups, CAP), 0, span)
        corners = corners.at[0:2, 0, 0, 0].set(jnp.array([0, span - 1], dtype=jnp.int32))
        corners = corners.at[2:4, :, 0, 0].set(span - 1)
        corners = corners.at[2:4, :, 0, CAP - 1].set(0)
        device_ids = jnp.arange(N_TX)[:, None, None]
        group_ids = jnp.broadcast_to(jnp.arange(groups)[None, :, None], (N_TX, groups, CAP))
        rank_ids = jnp.broadcast_to(jnp.arange(CAP)[None, None, :], (N_TX, groups, CAP))
        owners = jnp.broadcast_to(sigma[(device_ids + shifts[group_ids[:, :, :1]]) % N_TX], (N_TX, groups, CAP))
        send_slot = owners * CAP + rank_ids
        sources = jnp.broadcast_to((inverse[device_ids] - shifts[group_ids[:, :, :1]]) % N_TX, (N_TX, groups, CAP))
        recv_slot = sources * CAP + rank_ids
        a_corner = corners[0:2][:, sources, group_ids, rank_ids]
        b_corner = corners[2:4]
        order_a = jax.vmap(lambda sub_key: jax.random.permutation(sub_key, ITEMS_DEV))(jax.random.split(keys[3], N_TX))
        order_b = jax.vmap(lambda sub_key: jax.random.permutation(sub_key, ITEMS_DEV))(jax.random.split(keys[4], N_TX))
        return (arrange(a_corner, order_a), arrange(recv_slot, order_a), arrange(b_corner, order_b), arrange(send_slot, order_b))
    return jax.vmap(one_row)(jax.random.split(key, N_TY))


def draw_template_corner(key, part):
    tables = item_tables(jax.random.fold_in(key, 7))
    return jnp.transpose(tables[0], (1, 0, 2)).astype(jnp.int32)


def draw_template_slot(key, part):
    return item_tables(jax.random.fold_in(key, 7))[1].astype(jnp.int32)


def draw_window_corner(key, part):
    tables = item_tables(jax.random.fold_in(key, 7))
    return jnp.transpose(tables[2], (1, 0, 2)).astype(jnp.int32)


def draw_window_slot(key, part):
    return item_tables(jax.random.fold_in(key, 7))[3].astype(jnp.int32)


def touch_ends(drawn, stream_key, least, high):
    index_at = [jax.random.randint(jax.random.fold_in(stream_key, axis), (), 0, length) for axis, length in enumerate(drawn.shape)]
    main_axis = drawn.shape.index(max(drawn.shape))
    neighbour = index_at[:main_axis] + [(index_at[main_axis] + 1) % drawn.shape[main_axis]] + index_at[main_axis + 1:]
    return drawn.at[tuple(index_at)].set(least).at[tuple(neighbour)].set(high)


def setup_inputs(seed: int = 0) -> dict:
    key_of = jax.random.split(jax.random.key(seed), 8)
    return {
        "section_a": draw_section_a(jax.random.fold_in(key_of[7], 71), 0),
        "section_b": draw_section_b(jax.random.fold_in(key_of[7], 71), 0),
        "template_corner": draw_template_corner(jax.random.fold_in(key_of[7], 71), 0),
        "template_slot": draw_template_slot(jax.random.fold_in(key_of[7], 71), 0),
        "window_corner": draw_window_corner(jax.random.fold_in(key_of[7], 71), 0),
        "window_slot": draw_window_slot(jax.random.fold_in(key_of[7], 71), 0),
        "node_mask": touch_ends((jax.random.randint(key_of[6], (NODE_ROWS, NODE_COLS), 0, 8) < 7).astype(jnp.int32), jax.random.fold_in(key_of[6], 1), 0, 1),
    }


SHARPNESS = 256.0
SPRING_RATE = 0.25
FLOW_RATE = 0.5
FLOW_UNIT = 8.0
EPSILON = 1e-05

def block_flow(template, window):
    temp_f = template.astype(jnp.float32)
    wind_f = window.astype(jnp.float32)
    stacked = jnp.stack([wind_f[offset:offset + PATCH] for offset in range(SHIFTS)])
    products = jnp.einsum('ij,dik->djk', temp_f, stacked, precision=lax.Precision.HIGHEST)
    padded = jnp.pad(products, ((0, 0), (0, 0), (0, 1)))
    flat = padded.reshape(SHIFTS, PATCH * (WIN + 1))
    flat = jnp.pad(flat, ((0, 0), (0, PATCH)))
    skewed = flat.reshape(SHIFTS, PATCH, WIN + 2)[:, :, :SHIFTS]
    corr = lax.optimization_barrier(jnp.sum(skewed, axis=1))
    energy_t = jnp.mean(temp_f * temp_f)
    energy_w = jnp.mean(wind_f * wind_f)
    scores = SHARPNESS * corr / (PATCH * PATCH * jnp.sqrt((energy_t + EPSILON) * (energy_w + EPSILON)))
    weights = jnp.exp(scores - jnp.max(scores))
    weights = weights / jnp.sum(weights)
    shift_vals = (jnp.arange(SHIFTS) - RADIUS).astype(jnp.float32)
    flow_y = jnp.sum(weights * shift_vals[:, None]) / FLOW_UNIT
    flow_x = jnp.sum(weights * shift_vals[None, :]) / FLOW_UNIT
    return jnp.stack([flow_y, flow_x])

def relax_sweep(padded, mask_pad, target, count):
    centre = padded[:, 1:-1, 1:-1]
    mask_c = mask_pad[1:-1, 1:-1]
    height = centre.shape[1]
    width = centre.shape[2]
    spring = jnp.zeros_like(centre)
    for row_step, col_step in ((0, 1), (2, 1), (1, 0), (1, 2)):
        nearby = padded[:, row_step:row_step + height, col_step:col_step + width]
        mask_n = mask_pad[row_step:row_step + height, col_step:col_step + width]
        spring = spring + mask_c * mask_n * (nearby - centre)
    return centre + SPRING_RATE * spring + FLOW_RATE * (target - count * centre)

def reference(section_a, section_b, template_corner, template_slot, window_corner, window_slot, node_mask):
    slot_count = N_TX * CAP
    entry_ids = jnp.arange(ITEMS, dtype=jnp.int32)
    device_of = entry_ids // ITEMS_DEV
    row_ids = jnp.broadcast_to(jnp.arange(N_TY, dtype=jnp.int32)[:, None], (N_TY, ITEMS))
    keys_b = device_of[None, :] * slot_count + window_slot
    table = jnp.zeros((N_TY, N_TX * slot_count), jnp.int32)
    table = table.at[row_ids, keys_b].set(jnp.broadcast_to(entry_ids[None, :], (N_TY, ITEMS)))
    source_a = template_slot // CAP
    rank_a = template_slot % CAP
    keys_a = source_a * slot_count + device_of[None, :] * CAP + rank_a
    partner = jnp.take_along_axis(table, keys_a, axis=1).astype(jnp.int32)
    padded_b = jnp.pad(section_b, RADIUS)
    a_top = row_ids * TILE + template_corner[0]
    a_left = device_of[None, :] * TILE + template_corner[1]
    b_top = row_ids * TILE + jnp.take_along_axis(window_corner[0], partner, axis=1)
    b_left = source_a * TILE + jnp.take_along_axis(window_corner[1], partner, axis=1)
    corners = jnp.stack([a_top.reshape(-1), a_left.reshape(-1), b_top.reshape(-1), b_left.reshape(-1)], axis=1).astype(jnp.int32)

    def one_pair(corner):
        template = lax.dynamic_slice(section_a, (corner[0], corner[1]), (PATCH, PATCH))
        window = lax.dynamic_slice(padded_b, (corner[2], corner[3]), (WIN, WIN))
        return block_flow(template, window)
    flows = lax.map(one_pair, corners)
    owner_flow = flows.T.reshape(2, N_TY, ITEMS)
    source_flow = jnp.zeros((2, N_TY, ITEMS), jnp.float32).at[:, row_ids, partner].set(-owner_flow)
    node_y = row_ids * MY + (window_corner[0] + PATCH // 2) * MY // TILE
    node_x = device_of[None, :] * MX + (window_corner[1] + PATCH // 2) * MX // TILE
    target = jnp.zeros((2, NODE_ROWS, NODE_COLS), jnp.float32).at[:, node_y, node_x].add(source_flow)
    count = jnp.zeros((NODE_ROWS, NODE_COLS), jnp.float32).at[node_y, node_x].add(jnp.ones((N_TY, ITEMS), jnp.float32))
    mask_pad = jnp.pad(node_mask.astype(jnp.float32), 1)
    displace = jnp.zeros((2, NODE_ROWS, NODE_COLS), jnp.float32)
    for sweep in range(ITERS_R):
        displace = relax_sweep(jnp.pad(displace, ((0, 0), (1, 1), (1, 1))), mask_pad, target, count)
    return (owner_flow, source_flow, displace)
```

```python
import jax
import jax.numpy as jnp
from jax import lax
from jax.sharding import PartitionSpec as P
from jax.experimental import pallas as pl
from jax.experimental.pallas import tpu as pltpu

PATCH = 128
SHIFTS = 65
RADIUS = 32
WIN = 192
CAP = 2
ITERS_R = 3


SHARPNESS = 256.0
SPRING_RATE = 0.25
FLOW_RATE = 0.5
FLOW_UNIT = 8.0
EPSILON = 1e-05

from jax.experimental import pallas as pl
from jax.experimental.pallas import tpu as pltpu


def flow_kernel(tf_ref, w_ref, out_ref, wpad, tpad, corr):
    wpad[...] = jnp.zeros(wpad.shape, jnp.float32)
    wf = w_ref[0].astype(jnp.float32)
    wpad[0:WIN, 0:WIN] = wf
    tfv = tf_ref[0].astype(jnp.float32)
    tpad[...] = jnp.zeros(tpad.shape, jnp.float32)
    tpad[:, 0:PATCH] = tfv
    wb = wpad[...].astype(jnp.bfloat16)
    tp = tpad[...]
    corr[...] = jnp.zeros(corr.shape, jnp.float32)

    def step(dy, carry):
        lhs = pltpu.roll(tp, dy, axis=1).astype(jnp.bfloat16)
        m = jnp.dot(lhs, wb, preferred_element_type=jnp.float32)
        r = pltpu.roll(m, 0, axis=1, stride=1, stride_axis=0)
        corr[pl.ds(dy, 1), :] = jnp.sum(r, axis=0, keepdims=True)
        return carry
    lax.fori_loop(0, SHIFTS, step, 0, unroll=5)

    c = corr[...]
    rows = lax.broadcasted_iota(jnp.int32, c.shape, 0)
    lanes = lax.broadcasted_iota(jnp.int32, c.shape, 1)
    valid = (rows < SHIFTS) & (lanes >= PATCH - 1) & (lanes < PATCH - 1 + SHIFTS)
    e_t = jnp.sum(tfv * tfv, keepdims=True) / float(PATCH * PATCH)
    e_w = jnp.sum(wf * wf, keepdims=True) / float(WIN * WIN)
    denom = float(PATCH * PATCH) * jnp.sqrt((e_t + EPSILON) * (e_w + EPSILON))
    scores = SHARPNESS * c / denom
    scores = jnp.where(valid, scores, -jnp.inf)
    mx = jnp.max(scores, keepdims=True)
    e = jnp.where(valid, jnp.exp(scores - mx), 0.0)
    w = e / jnp.sum(e, keepdims=True)
    sy = (rows - RADIUS).astype(jnp.float32)
    sx = (lanes - (PATCH - 1) - RADIUS).astype(jnp.float32)
    fy = jnp.sum(w * sy, keepdims=True) / FLOW_UNIT
    fx = jnp.sum(w * sx, keepdims=True) / FLOW_UNIT
    orow = lax.broadcasted_iota(jnp.int32, (8, 128), 0)
    out_ref[0] = jnp.where(orow == 0, fy, jnp.where(orow == 1, fx, 0.0))

def flows_of(templates, windows):
    n = templates.shape[0]
    tf = jnp.flip(templates, axis=2).transpose(0, 2, 1)
    out = pl.pallas_call(
        flow_kernel,
        grid=(n,),
        in_specs=[pl.BlockSpec((1, PATCH, PATCH), lambda i: (i, 0, 0)),
                  pl.BlockSpec((1, WIN, WIN), lambda i: (i, 0, 0))],
        out_specs=pl.BlockSpec((1, 8, 128), lambda i: (i, 0, 0)),
        out_shape=jax.ShapeDtypeStruct((n, 8, 128), jnp.float32),
        scratch_shapes=[pltpu.VMEM((256, 256), jnp.float32),
                        pltpu.VMEM((PATCH, 256), jnp.float32),
                        pltpu.VMEM((72, 256), jnp.float32)],
    )(tf, windows)
    return out[:, 0:2, 0].T


def padded_2(cells, sides, width):
    for axis, dim in sides:
        count = lax.axis_size(axis)
        ends = count - 1
        head = lax.slice_in_dim(cells, 0, width, axis=dim)
        tail = lax.slice_in_dim(cells, cells.shape[dim] - width, cells.shape[dim], axis=dim)
        cells = jnp.concatenate(
            [
                lax.ppermute(tail, axis, [(i, (i + 1) % count) for i in range(ends)]),
                cells,
                lax.ppermute(head, axis, [((i + 1) % count, i) for i in range(ends)]),
            ],
            axis=dim,
        )
    return cells


def shift_tables():
    rows_out = jnp.arange(SHIFTS * PATCH, dtype=jnp.int32)
    wanted = rows_out // PATCH + rows_out % PATCH
    row_shift = (wanted[:, None] == jnp.arange(WIN, dtype=jnp.int32)[None, :]).astype(jnp.bfloat16)
    cols_out = jnp.arange(SHIFTS * WIN, dtype=jnp.int32)
    source_col = cols_out % WIN - cols_out // WIN
    col_shift = (jnp.arange(PATCH, dtype=jnp.int32)[:, None] == source_col[None, :]).astype(
        jnp.bfloat16
    )
    return (row_shift, col_shift)


def make_block_flow(row_shift, col_shift):

    def block_flow(pair):
        template, window = pair
        moved_rows = jnp.dot(row_shift, window, preferred_element_type=jnp.float32).astype(
            jnp.bfloat16
        )
        moved_rows = moved_rows.reshape(SHIFTS, PATCH, WIN)
        placed = jnp.dot(template, col_shift, preferred_element_type=jnp.float32).astype(
            jnp.bfloat16
        )
        placed = placed.reshape(PATCH, SHIFTS, WIN)
        corr = jnp.einsum("dia,ixa->dx", moved_rows, placed, preferred_element_type=jnp.float32)
        temp_f = template.astype(jnp.float32)
        wind_f = window.astype(jnp.float32)
        energy_t = jnp.mean(temp_f * temp_f)
        energy_w = jnp.mean(wind_f * wind_f)
        scores = (
            SHARPNESS
            * corr
            / (PATCH * PATCH * jnp.sqrt((energy_t + EPSILON) * (energy_w + EPSILON)))
        )
        weights = jnp.exp(scores - jnp.max(scores))
        weights = weights / jnp.sum(weights)
        shift_vals = (jnp.arange(SHIFTS) - RADIUS).astype(jnp.float32)
        flow_y = jnp.sum(weights * shift_vals[:, None]) / FLOW_UNIT
        flow_x = jnp.sum(weights * shift_vals[None, :]) / FLOW_UNIT
        return jnp.stack([flow_y, flow_x])

    return block_flow


def relax_sweep(padded, mask_pad, target, count):
    centre = padded[:, 1:-1, 1:-1]
    mask_c = mask_pad[1:-1, 1:-1]
    height = centre.shape[1]
    width = centre.shape[2]
    spring = jnp.zeros_like(centre)
    for row_step, col_step in ((0, 1), (2, 1), (1, 0), (1, 2)):
        nearby = padded[:, row_step : row_step + height, col_step : col_step + width]
        mask_n = mask_pad[row_step : row_step + height, col_step : col_step + width]
        spring = spring + mask_c * mask_n * (nearby - centre)
    return centre + SPRING_RATE * spring + FLOW_RATE * (target - count * centre)


def cut_blocks(image, tops, lefts, extent):
    return jax.vmap(
        lambda top_row, left_col: lax.dynamic_slice(image, (top_row, left_col), (extent, extent))
    )(tops, lefts)


def select_rows(picker, values):
    flat = values.reshape(values.shape[0], -1)
    chosen = jnp.dot(picker, flat, preferred_element_type=jnp.float32).astype(jnp.bfloat16)
    return chosen.reshape((picker.shape[0],) + values.shape[1:])


def shards(
    section_a, section_b, template_corner, template_slot, window_corner, window_slot, node_mask
):
    tile_size = section_a.shape[0]
    slot_count = lax.axis_size("tx") * CAP
    slot_ids = jnp.arange(slot_count, dtype=jnp.int32)
    owner_picker = template_slot[0][:, None] == slot_ids[None, :]
    source_picker = window_slot[0][:, None] == slot_ids[None, :]
    row_shift, col_shift = shift_tables()
    block_flow = make_block_flow(row_shift, col_shift)
    b_wide = padded_2(section_b, (("ty", 0), ("tx", 1)), RADIUS)
    templates = cut_blocks(section_a, template_corner[0, 0], template_corner[1, 0], PATCH)
    windows = cut_blocks(b_wide, window_corner[0, 0], window_corner[1, 0], WIN)
    highest = lax.Precision.HIGHEST
    outgoing = select_rows(source_picker.T.astype(jnp.bfloat16), windows)
    arrived = lax.all_to_all(outgoing, "tx", split_axis=0, concat_axis=0, tiled=True)
    matched = select_rows(owner_picker.astype(jnp.bfloat16), arrived)
    flows = flows_of(templates, matched)
    returned = jnp.dot(flows, owner_picker.astype(jnp.float32), precision=highest)
    landed = lax.all_to_all(returned, "tx", split_axis=1, concat_axis=1, tiled=True)
    source_flow = -jnp.dot(landed, source_picker.T.astype(jnp.float32), precision=highest)
    node_rows, node_cols = node_mask.shape
    centre_y = (window_corner[0, 0] + PATCH // 2) * node_rows // tile_size
    centre_x = (window_corner[1, 0] + PATCH // 2) * node_cols // tile_size
    node_ids = centre_y * node_cols + centre_x
    node_picker = (
        node_ids[:, None] == jnp.arange(node_rows * node_cols, dtype=jnp.int32)[None, :]
    ).astype(jnp.float32)
    target = jnp.dot(source_flow, node_picker, precision=highest).reshape(2, node_rows, node_cols)
    count = jnp.sum(node_picker, axis=0).reshape(node_rows, node_cols)
    mask = node_mask.astype(jnp.float32)
    mask_wide = padded_2(mask, (("ty", 0), ("tx", 1)), 1)
    displace = jnp.zeros((2, node_rows, node_cols), jnp.float32)
    for sweep in range(ITERS_R):
        padded = padded_2(displace, (("ty", 1), ("tx", 2)), 1)
        displace = relax_sweep(padded, mask_wide, target, count)
    return (flows[:, None, :], source_flow[:, None, :], displace)


def solution(mesh):
    placed = (
        P("ty", "tx"),
        P("ty", "tx"),
        P(None, "ty", "tx"),
        P("ty", "tx"),
        P(None, "ty", "tx"),
        P("ty", "tx"),
        P("ty", "tx"),
    )
    return jax.shard_map(
        shards,
        mesh=mesh,
        in_specs=placed,
        out_specs=(P(None, "ty", "tx"), P(None, "ty", "tx"), P(None, "ty", "tx")),
        check_vma=False,
    )
```

```python
import jax
import jax.numpy as jnp
from jax import lax
from jax.sharding import PartitionSpec as P
from jax.experimental import pallas as pl
from jax.experimental.pallas import tpu as pltpu

PATCH = 128
SHIFTS = 65
RADIUS = 32
WIN = 192
CAP = 2
ITERS_R = 3


SHARPNESS = 256.0
SPRING_RATE = 0.25
FLOW_RATE = 0.5
FLOW_UNIT = 8.0
EPSILON = 1e-05

LANES = 256


def flow_kernel(tf_ref, w_ref, out_ref, wpad, tpad, corr):
    wpad[...] = jnp.zeros(wpad.shape, jnp.float32)
    wf = w_ref[0].astype(jnp.float32)
    wpad[0:WIN, 0:WIN] = wf
    tfv = tf_ref[0].astype(jnp.float32)
    tpad[...] = jnp.zeros(tpad.shape, jnp.float32)
    tpad[:, 0:PATCH] = tfv
    wb = wpad[...].astype(jnp.bfloat16)
    tp = tpad[...]
    corr[...] = jnp.zeros(corr.shape, jnp.float32)

    def step(dy, carry):
        lhs = pltpu.roll(tp, dy, axis=1).astype(jnp.bfloat16)
        m = jnp.dot(lhs, wb, preferred_element_type=jnp.float32)
        r = pltpu.roll(m, 0, axis=1, stride=1, stride_axis=0)
        corr[pl.ds(dy, 1), :] = jnp.sum(r, axis=0, keepdims=True)
        return carry

    lax.fori_loop(0, SHIFTS, step, 0, unroll=5)

    c = corr[...]
    rows = lax.broadcasted_iota(jnp.int32, c.shape, 0)
    lanes = lax.broadcasted_iota(jnp.int32, c.shape, 1)
    valid = (rows < SHIFTS) & (lanes >= PATCH - 1) & (lanes < PATCH - 1 + SHIFTS)
    e_t = jnp.sum(tfv * tfv, keepdims=True) / float(PATCH * PATCH)
    e_w = jnp.sum(wf * wf, keepdims=True) / float(WIN * WIN)
    denom = float(PATCH * PATCH) * jnp.sqrt((e_t + EPSILON) * (e_w + EPSILON))
    scores = SHARPNESS * c / denom
    scores = jnp.where(valid, scores, -jnp.inf)
    mx = jnp.max(scores, keepdims=True)
    e = jnp.where(valid, jnp.exp(scores - mx), 0.0)
    w = e / jnp.sum(e, keepdims=True)
    sy = (rows - RADIUS).astype(jnp.float32)
    sx = (lanes - (PATCH - 1) - RADIUS).astype(jnp.float32)
    fy = jnp.sum(w * sy, keepdims=True) / FLOW_UNIT
    fx = jnp.sum(w * sx, keepdims=True) / FLOW_UNIT
    orow = lax.broadcasted_iota(jnp.int32, (8, 128), 0)
    out_ref[0] = jnp.where(orow == 0, fy, jnp.where(orow == 1, fx, 0.0))


def flows_of(tflipped, windows):
    n = tflipped.shape[0]
    out = pl.pallas_call(
        flow_kernel,
        grid=(n,),
        in_specs=[
            pl.BlockSpec((1, PATCH, PATCH), lambda i: (i, 0, 0)),
            pl.BlockSpec((1, WIN, WIN), lambda i: (i, 0, 0)),
        ],
        out_specs=pl.BlockSpec((1, 8, 128), lambda i: (i, 0, 0)),
        out_shape=jax.ShapeDtypeStruct((n, 8, 128), jnp.float32),
        scratch_shapes=[
            pltpu.VMEM((LANES, LANES), jnp.float32),
            pltpu.VMEM((PATCH, LANES), jnp.float32),
            pltpu.VMEM((72, LANES), jnp.float32),
        ],
    )(tflipped, windows)
    return out[:, 0:2, 0].T


def halo(cells, width):
    n_ty = lax.axis_size("ty")
    n_tx = lax.axis_size("tx")
    height, breadth = cells.shape[-2], cells.shape[-1]
    pieces = {}
    for dy in (-1, 0, 1):
        for dx in (-1, 0, 1):
            if dy == 0 and dx == 0:
                pieces[(dy, dx)] = cells
                continue
            rows = {-1: (height - width, height), 0: (0, height), 1: (0, width)}[dy]
            cols = {-1: (breadth - width, breadth), 0: (0, breadth), 1: (0, width)}[dx]
            part = cells[..., rows[0] : rows[1], cols[0] : cols[1]]
            pairs = []
            for i in range(n_ty):
                for j in range(n_tx):
                    si, sj = i + dy, j + dx
                    if 0 <= si < n_ty and 0 <= sj < n_tx:
                        pairs.append((si * n_tx + sj, i * n_tx + j))
            pieces[(dy, dx)] = lax.ppermute(part, ("ty", "tx"), pairs)
    bands = [
        jnp.concatenate([pieces[(dy, -1)], pieces[(dy, 0)], pieces[(dy, 1)]], axis=-1)
        for dy in (-1, 0, 1)
    ]
    return jnp.concatenate(bands, axis=-2)


def relax_sweep(padded, mask_pad, target, count):
    centre = padded[:, 1:-1, 1:-1]
    mask_c = mask_pad[1:-1, 1:-1]
    height = centre.shape[1]
    width = centre.shape[2]
    spring = jnp.zeros_like(centre)
    for row_step, col_step in ((0, 1), (2, 1), (1, 0), (1, 2)):
        nearby = padded[:, row_step : row_step + height, col_step : col_step + width]
        mask_n = mask_pad[row_step : row_step + height, col_step : col_step + width]
        spring = spring + mask_c * mask_n * (nearby - centre)
    return centre + SPRING_RATE * spring + FLOW_RATE * (target - count * centre)


def one_hot(starts, size, extent, flip=False):
    offs = jnp.arange(size, dtype=jnp.int32)
    if flip:
        offs = size - 1 - offs
    want = starts[:, None, None] + offs[None, :, None]
    return (want == jnp.arange(extent, dtype=jnp.int32)[None, None, :]).astype(jnp.bfloat16)


def shards(
    section_a, section_b, template_corner, template_slot, window_corner, window_slot, node_mask
):
    tile_size = section_a.shape[0]
    slot_count = lax.axis_size("tx") * CAP
    slot_ids = jnp.arange(slot_count, dtype=jnp.int32)
    owner_picker = template_slot[0][:, None] == slot_ids[None, :]
    source_picker = window_slot[0][:, None] == slot_ids[None, :]
    f32 = jnp.float32

    col_pick = one_hot(template_corner[1, 0], PATCH, section_a.shape[1], flip=True)
    row_pick = one_hot(template_corner[0, 0], PATCH, section_a.shape[0])
    by_col = jnp.einsum("krc,ac->kra", col_pick, section_a, preferred_element_type=f32)
    tflipped = jnp.einsum(
        "kra,kia->kri", by_col.astype(jnp.bfloat16), row_pick, preferred_element_type=f32
    ).astype(jnp.bfloat16)
    outgoing = jnp.einsum(
        "ks,kri->sri", owner_picker.astype(jnp.bfloat16), tflipped, preferred_element_type=f32
    ).astype(jnp.bfloat16)
    arrived = lax.all_to_all(outgoing, "tx", split_axis=0, concat_axis=0, tiled=True)

    b_wide = halo(section_b, RADIUS)
    wrow_pick = one_hot(window_corner[0, 0], WIN, b_wide.shape[0])
    wcol_pick = one_hot(window_corner[1, 0], WIN, b_wide.shape[1])
    by_row = jnp.einsum("mra,ac->mrc", wrow_pick, b_wide, preferred_element_type=f32)
    windows = jnp.einsum(
        "mrc,msc->mrs", by_row.astype(jnp.bfloat16), wcol_pick, preferred_element_type=f32
    ).astype(jnp.bfloat16)
    matched = jnp.einsum(
        "ms,sri->mri", source_picker.astype(jnp.bfloat16), arrived, preferred_element_type=f32
    ).astype(jnp.bfloat16)

    flows = flows_of(matched, windows)
    source_flow = -flows

    returned = jnp.sum(jnp.where(source_picker[None], flows[:, :, None], 0.0), axis=1)
    landed = lax.all_to_all(returned, "tx", split_axis=1, concat_axis=1, tiled=True)
    owner_flow = jnp.sum(jnp.where(owner_picker[None], landed[:, None, :], 0.0), axis=2)

    node_rows, node_cols = node_mask.shape
    centre_y = (window_corner[0, 0] + PATCH // 2) * node_rows // tile_size
    centre_x = (window_corner[1, 0] + PATCH // 2) * node_cols // tile_size
    attach = (centre_y[:, None, None] == jnp.arange(node_rows, dtype=jnp.int32)[None, :, None]) & (
        centre_x[:, None, None] == jnp.arange(node_cols, dtype=jnp.int32)[None, None, :]
    )
    target = jnp.sum(jnp.where(attach[None], source_flow[:, :, None, None], 0.0), axis=1)
    count = jnp.sum(attach.astype(f32), axis=0)
    mask = node_mask.astype(f32)
    fields = jnp.concatenate([target, count[None], mask[None]], axis=0)
    wide = halo(fields, ITERS_R)
    displace = jnp.zeros((2,) + wide.shape[1:], f32)
    for sweep in range(ITERS_R):
        lo_m, hi_m = sweep, wide.shape[1] - sweep
        lo_t, hi_t = sweep + 1, wide.shape[1] - sweep - 1
        displace = relax_sweep(
            displace,
            wide[3, lo_m:hi_m, lo_m:hi_m],
            wide[0:2, lo_t:hi_t, lo_t:hi_t],
            wide[2, lo_t:hi_t, lo_t:hi_t],
        )
    return (owner_flow[:, None, :], source_flow[:, None, :], displace)


def solution(mesh):
    placed = (
        P("ty", "tx"),
        P("ty", "tx"),
        P(None, "ty", "tx"),
        P("ty", "tx"),
        P(None, "ty", "tx"),
        P("ty", "tx"),
        P("ty", "tx"),
    )
    return jax.shard_map(
        shards,
        mesh=mesh,
        in_specs=placed,
        out_specs=(P(None, "ty", "tx"), P(None, "ty", "tx"), P(None, "ty", "tx")),
        check_vma=False,
    )
```

```python
import jax
import jax.numpy as jnp
from jax import lax
from jax.sharding import PartitionSpec as P
from jax.experimental import pallas as pl
from jax.experimental.pallas import tpu as pltpu

PATCH = 128
SHIFTS = 65
RADIUS = 32
WIN = 192
CAP = 2
ITERS_R = 3


SHARPNESS = 256.0
SPRING_RATE = 0.25
FLOW_RATE = 0.5
FLOW_UNIT = 8.0
EPSILON = 1e-05

HALF = PATCH // 2


def flow_kernel(tf_ref, w_ref, out_ref, wlo, whi, corr):
    wf = w_ref[0].astype(jnp.float32)
    wlo[...] = wf[:, 0:PATCH]
    whi[...] = jnp.zeros(whi.shape, jnp.float32)
    whi[:, 0:WIN - HALF] = wf[:, HALF:WIN]
    tfv = tf_ref[0].astype(jnp.float32)
    t_top = tf_ref[0, 0:HALF, :]
    t_bot = tf_ref[0, HALF:PATCH, :]
    corr[...] = jnp.zeros(corr.shape, jnp.float32)

    def step(dy, carry):
        w_lo = wlo[pl.ds(dy, PATCH), :].astype(jnp.bfloat16)
        w_hi = whi[pl.ds(dy, PATCH), :].astype(jnp.bfloat16)
        m_top = jnp.dot(t_top, w_hi, preferred_element_type=jnp.float32)
        m_bot = jnp.dot(t_bot, w_lo, preferred_element_type=jnp.float32)
        r_top = pltpu.roll(m_top, 0, axis=1, stride=1, stride_axis=0)
        r_bot = pltpu.roll(m_bot, 0, axis=1, stride=1, stride_axis=0)
        corr[pl.ds(dy, 1), :] = jnp.sum(r_top + r_bot, axis=0, keepdims=True)
        return carry

    lax.fori_loop(0, SHIFTS, step, 0, unroll=SHIFTS)

    c = corr[...]
    rows = lax.broadcasted_iota(jnp.int32, c.shape, 0)
    lanes = lax.broadcasted_iota(jnp.int32, c.shape, 1)
    valid = (rows < SHIFTS) & (lanes >= HALF - 1)
    e_t = jnp.sum(tfv * tfv, keepdims=True) / float(PATCH * PATCH)
    e_w = jnp.sum(wf * wf, keepdims=True) / float(WIN * WIN)
    denom = float(PATCH * PATCH) * jnp.sqrt((e_t + EPSILON) * (e_w + EPSILON))
    scores = SHARPNESS * c / denom
    scores = jnp.where(valid, scores, -jnp.inf)
    mx = jnp.max(scores, keepdims=True)
    e = jnp.where(valid, jnp.exp(scores - mx), 0.0)
    w = e / jnp.sum(e, keepdims=True)
    sy = (rows - RADIUS).astype(jnp.float32)
    sx = (lanes - (HALF - 1) - RADIUS).astype(jnp.float32)
    fy = jnp.sum(w * sy, keepdims=True) / FLOW_UNIT
    fx = jnp.sum(w * sx, keepdims=True) / FLOW_UNIT
    orow = lax.broadcasted_iota(jnp.int32, (8, 128), 0)
    out_ref[0] = jnp.where(orow == 0, fy, jnp.where(orow == 1, fx, 0.0))

def flows_of(tflipped, windows):
    n = tflipped.shape[0]
    out = pl.pallas_call(
        flow_kernel,
        grid=(n,),
        in_specs=[pl.BlockSpec((1, PATCH, PATCH), lambda i: (i, 0, 0)),
                  pl.BlockSpec((1, WIN, WIN), lambda i: (i, 0, 0))],
        out_specs=pl.BlockSpec((1, 8, 128), lambda i: (i, 0, 0)),
        out_shape=jax.ShapeDtypeStruct((n, 8, 128), jnp.float32),
        scratch_shapes=[pltpu.VMEM((WIN, PATCH), jnp.float32),
                        pltpu.VMEM((WIN, PATCH), jnp.float32),
                        pltpu.VMEM((72, PATCH), jnp.float32)],
    )(tflipped, windows)
    return out[:, 0:2, 0].T


def halo(cells, width):
    n_ty = lax.axis_size("ty")
    n_tx = lax.axis_size("tx")
    height, breadth = cells.shape[-2], cells.shape[-1]
    pieces = {}
    for dy in (-1, 0, 1):
        for dx in (-1, 0, 1):
            if dy == 0 and dx == 0:
                pieces[(dy, dx)] = cells
                continue
            rows = {-1: (height - width, height), 0: (0, height), 1: (0, width)}[dy]
            cols = {-1: (breadth - width, breadth), 0: (0, breadth), 1: (0, width)}[dx]
            part = cells[..., rows[0] : rows[1], cols[0] : cols[1]]
            pairs = []
            for i in range(n_ty):
                for j in range(n_tx):
                    si, sj = i + dy, j + dx
                    if 0 <= si < n_ty and 0 <= sj < n_tx:
                        pairs.append((si * n_tx + sj, i * n_tx + j))
            pieces[(dy, dx)] = lax.ppermute(part, ("ty", "tx"), pairs)
    bands = [
        jnp.concatenate([pieces[(dy, -1)], pieces[(dy, 0)], pieces[(dy, 1)]], axis=-1)
        for dy in (-1, 0, 1)
    ]
    return jnp.concatenate(bands, axis=-2)


def relax_sweep(padded, mask_pad, target, count):
    centre = padded[:, 1:-1, 1:-1]
    mask_c = mask_pad[1:-1, 1:-1]
    height = centre.shape[1]
    width = centre.shape[2]
    spring = jnp.zeros_like(centre)
    for row_step, col_step in ((0, 1), (2, 1), (1, 0), (1, 2)):
        nearby = padded[:, row_step : row_step + height, col_step : col_step + width]
        mask_n = mask_pad[row_step : row_step + height, col_step : col_step + width]
        spring = spring + mask_c * mask_n * (nearby - centre)
    return centre + SPRING_RATE * spring + FLOW_RATE * (target - count * centre)


def one_hot(starts, size, extent, flip=False):
    offs = jnp.arange(size, dtype=jnp.int32)
    if flip:
        offs = size - 1 - offs
    want = starts[:, None, None] + offs[None, :, None]
    return (want == jnp.arange(extent, dtype=jnp.int32)[None, None, :]).astype(jnp.bfloat16)


def shards(
    section_a, section_b, template_corner, template_slot, window_corner, window_slot, node_mask
):
    tile_size = section_a.shape[0]
    slot_count = lax.axis_size("tx") * CAP
    slot_ids = jnp.arange(slot_count, dtype=jnp.int32)
    owner_picker = template_slot[0][:, None] == slot_ids[None, :]
    source_picker = window_slot[0][:, None] == slot_ids[None, :]
    f32 = jnp.float32

    col_pick = one_hot(template_corner[1, 0], PATCH, section_a.shape[1], flip=True)
    row_pick = one_hot(template_corner[0, 0], PATCH, section_a.shape[0])
    by_col = jnp.einsum("krc,ac->kra", col_pick, section_a, preferred_element_type=f32)
    tflipped = jnp.einsum(
        "kra,kia->kri", by_col.astype(jnp.bfloat16), row_pick, preferred_element_type=f32
    ).astype(jnp.bfloat16)
    outgoing = jnp.einsum(
        "ks,kri->sri", owner_picker.astype(jnp.bfloat16), tflipped, preferred_element_type=f32
    ).astype(jnp.bfloat16)
    arrived = lax.all_to_all(outgoing, "tx", split_axis=0, concat_axis=0, tiled=True)

    b_wide = halo(section_b, RADIUS)
    wrow_pick = one_hot(window_corner[0, 0], WIN, b_wide.shape[0])
    wcol_pick = one_hot(window_corner[1, 0], WIN, b_wide.shape[1])
    by_row = jnp.einsum("mra,ac->mrc", wrow_pick, b_wide, preferred_element_type=f32)
    windows = jnp.einsum(
        "mrc,msc->mrs", by_row.astype(jnp.bfloat16), wcol_pick, preferred_element_type=f32
    ).astype(jnp.bfloat16)
    matched = jnp.einsum(
        "ms,sri->mri", source_picker.astype(jnp.bfloat16), arrived, preferred_element_type=f32
    ).astype(jnp.bfloat16)

    flows = flows_of(matched, windows)
    source_flow = -flows

    returned = jnp.sum(jnp.where(source_picker[None], flows[:, :, None], 0.0), axis=1)
    landed = lax.all_to_all(returned, "tx", split_axis=1, concat_axis=1, tiled=True)
    owner_flow = jnp.sum(jnp.where(owner_picker[None], landed[:, None, :], 0.0), axis=2)

    node_rows, node_cols = node_mask.shape
    centre_y = (window_corner[0, 0] + PATCH // 2) * node_rows // tile_size
    centre_x = (window_corner[1, 0] + PATCH // 2) * node_cols // tile_size
    attach = (centre_y[:, None, None] == jnp.arange(node_rows, dtype=jnp.int32)[None, :, None]) & (
        centre_x[:, None, None] == jnp.arange(node_cols, dtype=jnp.int32)[None, None, :]
    )
    target = jnp.sum(jnp.where(attach[None], source_flow[:, :, None, None], 0.0), axis=1)
    count = jnp.sum(attach.astype(f32), axis=0)
    mask = node_mask.astype(f32)
    fields = jnp.concatenate([target, count[None], mask[None]], axis=0)
    wide = halo(fields, ITERS_R)
    displace = jnp.zeros((2,) + wide.shape[1:], f32)
    for sweep in range(ITERS_R):
        lo_m, hi_m = sweep, wide.shape[1] - sweep
        lo_t, hi_t = sweep + 1, wide.shape[1] - sweep - 1
        displace = relax_sweep(
            displace,
            wide[3, lo_m:hi_m, lo_m:hi_m],
            wide[0:2, lo_t:hi_t, lo_t:hi_t],
            wide[2, lo_t:hi_t, lo_t:hi_t],
        )
    return (owner_flow[:, None, :], source_flow[:, None, :], displace)


def solution(mesh):
    placed = (
        P("ty", "tx"),
        P("ty", "tx"),
        P(None, "ty", "tx"),
        P("ty", "tx"),
        P(None, "ty", "tx"),
        P("ty", "tx"),
        P("ty", "tx"),
    )
    return jax.shard_map(
        shards,
        mesh=mesh,
        in_specs=placed,
        out_specs=(P(None, "ty", "tx"), P(None, "ty", "tx"), P(None, "ty", "tx")),
        check_vma=False,
    )
```

```python
import jax
import jax.numpy as jnp
from jax import lax
from jax.sharding import PartitionSpec as P
from jax.experimental import pallas as pl
from jax.experimental.pallas import tpu as pltpu

PATCH = 128
SHIFTS = 65
RADIUS = 32
WIN = 192
CAP = 2
ITERS_R = 3


SHARPNESS = 256.0
SPRING_RATE = 0.25
FLOW_RATE = 0.5
FLOW_UNIT = 8.0
EPSILON = 1e-05

HALF = PATCH // 2


def flow_kernel(tf_ref, w_ref, out_ref, wlo, whi, corr):
    wf = w_ref[0].astype(jnp.float32)
    wlo[...] = wf[:, 0:PATCH]
    whi[...] = jnp.zeros(whi.shape, jnp.float32)
    whi[:, 0:WIN - HALF] = wf[:, HALF:WIN]
    tfv = tf_ref[0].astype(jnp.float32)
    t_top = tf_ref[0, 0:HALF, :]
    t_bot = tf_ref[0, HALF:PATCH, :]
    corr[...] = jnp.zeros(corr.shape, jnp.float32)

    def step(dy, carry):
        w_lo = wlo[pl.ds(dy, PATCH), :].astype(jnp.bfloat16)
        w_hi = whi[pl.ds(dy, PATCH), :].astype(jnp.bfloat16)
        m_top = jnp.dot(t_top, w_hi, preferred_element_type=jnp.float32)
        m_bot = jnp.dot(t_bot, w_lo, preferred_element_type=jnp.float32)
        r_top = pltpu.roll(m_top, 0, axis=1, stride=1, stride_axis=0)
        r_bot = pltpu.roll(m_bot, 0, axis=1, stride=1, stride_axis=0)
        corr[pl.ds(dy, 1), :] = jnp.sum(r_top + r_bot, axis=0, keepdims=True)
        return carry

    lax.fori_loop(0, SHIFTS, step, 0, unroll=SHIFTS)

    c = corr[...]
    rows = lax.broadcasted_iota(jnp.int32, c.shape, 0)
    lanes = lax.broadcasted_iota(jnp.int32, c.shape, 1)
    valid = (rows < SHIFTS) & (lanes >= HALF - 1)
    e_t = jnp.sum(tfv * tfv, keepdims=True) / float(PATCH * PATCH)
    e_w = jnp.sum(wf * wf, keepdims=True) / float(WIN * WIN)
    denom = float(PATCH * PATCH) * jnp.sqrt((e_t + EPSILON) * (e_w + EPSILON))
    scores = SHARPNESS * c / denom
    scores = jnp.where(valid, scores, -jnp.inf)
    mx = jnp.max(scores, keepdims=True)
    e = jnp.where(valid, jnp.exp(scores - mx), 0.0)
    w = e / jnp.sum(e, keepdims=True)
    sy = (rows - RADIUS).astype(jnp.float32)
    sx = (lanes - (HALF - 1) - RADIUS).astype(jnp.float32)
    fy = jnp.sum(w * sy, keepdims=True) / FLOW_UNIT
    fx = jnp.sum(w * sx, keepdims=True) / FLOW_UNIT
    orow = lax.broadcasted_iota(jnp.int32, (8, 128), 0)
    out_ref[0] = jnp.where(orow == 0, fy, jnp.where(orow == 1, fx, 0.0))

def flows_of(tflipped, windows):
    n = tflipped.shape[0]
    out = pl.pallas_call(
        flow_kernel,
        grid=(n,),
        in_specs=[pl.BlockSpec((1, PATCH, PATCH), lambda i: (i, 0, 0)),
                  pl.BlockSpec((1, WIN, WIN), lambda i: (i, 0, 0))],
        out_specs=pl.BlockSpec((1, 8, 128), lambda i: (i, 0, 0)),
        out_shape=jax.ShapeDtypeStruct((n, 8, 128), jnp.float32),
        scratch_shapes=[pltpu.VMEM((WIN, PATCH), jnp.float32),
                        pltpu.VMEM((WIN, PATCH), jnp.float32),
                        pltpu.VMEM((72, PATCH), jnp.float32)],
    )(tflipped, windows)
    return out[:, 0:2, 0].T


def halo(cells, width):
    n_ty = lax.axis_size("ty")
    n_tx = lax.axis_size("tx")
    height, breadth = cells.shape[-2], cells.shape[-1]
    pieces = {}
    for dy in (-1, 0, 1):
        for dx in (-1, 0, 1):
            if dy == 0 and dx == 0:
                pieces[(dy, dx)] = cells
                continue
            rows = {-1: (height - width, height), 0: (0, height), 1: (0, width)}[dy]
            cols = {-1: (breadth - width, breadth), 0: (0, breadth), 1: (0, width)}[dx]
            part = cells[..., rows[0] : rows[1], cols[0] : cols[1]]
            pairs = []
            for i in range(n_ty):
                for j in range(n_tx):
                    si, sj = i + dy, j + dx
                    if 0 <= si < n_ty and 0 <= sj < n_tx:
                        pairs.append((si * n_tx + sj, i * n_tx + j))
            pieces[(dy, dx)] = lax.ppermute(part, ("ty", "tx"), pairs)
    bands = [
        jnp.concatenate([pieces[(dy, -1)], pieces[(dy, 0)], pieces[(dy, 1)]], axis=-1)
        for dy in (-1, 0, 1)
    ]
    return jnp.concatenate(bands, axis=-2)


def relax_sweep(padded, mask_pad, target, count):
    centre = padded[:, 1:-1, 1:-1]
    mask_c = mask_pad[1:-1, 1:-1]
    height = centre.shape[1]
    width = centre.shape[2]
    spring = jnp.zeros_like(centre)
    for row_step, col_step in ((0, 1), (2, 1), (1, 0), (1, 2)):
        nearby = padded[:, row_step : row_step + height, col_step : col_step + width]
        mask_n = mask_pad[row_step : row_step + height, col_step : col_step + width]
        spring = spring + mask_c * mask_n * (nearby - centre)
    return centre + SPRING_RATE * spring + FLOW_RATE * (target - count * centre)


def one_hot(starts, size, extent, flip=False):
    offs = jnp.arange(size, dtype=jnp.int32)
    if flip:
        offs = size - 1 - offs
    want = starts[:, None, None] + offs[None, :, None]
    return (want == jnp.arange(extent, dtype=jnp.int32)[None, None, :]).astype(jnp.bfloat16)


def shards(
    section_a, section_b, template_corner, template_slot, window_corner, window_slot, node_mask
):
    tile_size = section_a.shape[0]
    slot_count = lax.axis_size("tx") * CAP
    slot_ids = jnp.arange(slot_count, dtype=jnp.int32)
    owner_picker = template_slot[0][:, None] == slot_ids[None, :]
    source_picker = window_slot[0][:, None] == slot_ids[None, :]
    f32 = jnp.float32

    col_pick = one_hot(template_corner[1, 0], PATCH, section_a.shape[1], flip=True)
    row_pick = one_hot(template_corner[0, 0], PATCH, section_a.shape[0])
    by_col = jnp.einsum("krc,ac->kra", col_pick, section_a, preferred_element_type=f32)
    tflipped = jnp.einsum(
        "kra,kia->kri", by_col.astype(jnp.bfloat16), row_pick, preferred_element_type=f32
    ).astype(jnp.bfloat16)
    outgoing = jnp.einsum(
        "ks,kri->sri", owner_picker.astype(jnp.bfloat16), tflipped, preferred_element_type=f32
    ).astype(jnp.bfloat16)
    arrived = lax.all_to_all(outgoing, "tx", split_axis=0, concat_axis=0, tiled=True)

    b_wide = halo(section_b, RADIUS)
    wrow_pick = one_hot(window_corner[0, 0], WIN, b_wide.shape[0])
    wcol_pick = one_hot(window_corner[1, 0], WIN, b_wide.shape[1])
    by_row = jnp.einsum("mra,ac->mrc", wrow_pick, b_wide, preferred_element_type=f32)
    windows = jnp.einsum(
        "mrc,msc->mrs", by_row.astype(jnp.bfloat16), wcol_pick, preferred_element_type=f32
    ).astype(jnp.bfloat16)
    matched = jnp.einsum(
        "ms,sri->mri", source_picker.astype(jnp.bfloat16), arrived, preferred_element_type=f32
    ).astype(jnp.bfloat16)

    flows = flows_of(matched, windows)
    source_flow = -flows

    n_ty = lax.axis_size("ty")
    n_tx = lax.axis_size("tx")
    me_y = lax.axis_index("ty")
    me_x = lax.axis_index("tx")
    node_rows, node_cols = node_mask.shape
    w = ITERS_R
    strips = jnp.concatenate(
        [
            node_mask[0:w, :].reshape(-1),
            node_mask[node_rows - w :, :].reshape(-1),
            node_mask[:, 0:w].reshape(-1),
            node_mask[:, node_cols - w :].reshape(-1),
        ]
    )
    facts = jnp.concatenate(
        [window_slot[0], window_corner[0, 0], window_corner[1, 0], strips]
    ).astype(f32)
    all_facts = lax.all_gather(facts, ("ty", "tx")).astype(jnp.int32)
    all_flows = lax.all_gather(flows.reshape(-1), ("ty", "tx"))
    items = flows.shape[1]

    row_flows = lax.dynamic_slice_in_dim(all_flows, me_y * n_tx, n_tx, axis=0).reshape(n_tx, 2, items)
    row_slots = lax.dynamic_slice_in_dim(all_facts, me_y * n_tx, n_tx, axis=0)[:, 0:items]
    src = template_slot[0] // CAP
    rank = template_slot[0] % CAP
    match = (jnp.arange(n_tx, dtype=jnp.int32)[None, :, None] == src[:, None, None]) & (
        row_slots[None, :, :] == (me_x * CAP + rank)[:, None, None]
    )
    owner_flow = jnp.sum(
        jnp.where(match[None], jnp.transpose(row_flows, (1, 0, 2))[:, None, :, :], 0.0), axis=(2, 3)
    )

    ext_r = node_rows + 2 * w
    ext_c = node_cols + 2 * w
    ids_r = jnp.arange(ext_r, dtype=jnp.int32)
    ids_c = jnp.arange(ext_c, dtype=jnp.int32)
    target = jnp.zeros((2, ext_r, ext_c), f32)
    count = jnp.zeros((ext_r, ext_c), f32)
    mask_rows = []
    for dy in (-1, 0, 1):
        mask_band = []
        for dx in (-1, 0, 1):
            ny = me_y + dy
            nx = me_x + dx
            inside = (ny >= 0) & (ny < n_ty) & (nx >= 0) & (nx < n_tx)
            who = jnp.clip(ny, 0, n_ty - 1) * n_tx + jnp.clip(nx, 0, n_tx - 1)
            fact = lax.dynamic_index_in_dim(all_facts, who, axis=0, keepdims=False)
            flow = lax.dynamic_index_in_dim(all_flows, who, axis=0, keepdims=False).reshape(2, items)
            corner_y = fact[items : 2 * items]
            corner_x = fact[2 * items : 3 * items]
            at_y = dy * node_rows + w + (corner_y + PATCH // 2) * node_rows // tile_size
            at_x = dx * node_cols + w + (corner_x + PATCH // 2) * node_cols // tile_size
            hit = (
                inside
                & (at_y[:, None, None] == ids_r[None, :, None])
                & (at_x[:, None, None] == ids_c[None, None, :])
            )
            target = target + jnp.sum(jnp.where(hit[None], -flow[:, :, None, None], 0.0), axis=1)
            count = count + jnp.sum(hit.astype(f32), axis=0)
            base = 3 * items
            top = fact[base : base + w * node_cols].reshape(w, node_cols)
            bottom = fact[base + w * node_cols : base + 2 * w * node_cols].reshape(w, node_cols)
            left = fact[base + 2 * w * node_cols : base + 2 * w * node_cols + node_rows * w].reshape(node_rows, w)
            right = fact[base + 2 * w * node_cols + node_rows * w :].reshape(node_rows, w)
            if dy == 0 and dx == 0:
                piece = node_mask
            elif dy == 0:
                piece = right if dx == -1 else left
            else:
                band = bottom if dy == -1 else top
                piece = {-1: band[:, node_cols - w :], 0: band, 1: band[:, 0:w]}[dx]
            mask_band.append(jnp.where(inside, piece, 0).astype(f32))
        mask_rows.append(jnp.concatenate(mask_band, axis=1))
    mask_wide = jnp.concatenate(mask_rows, axis=0)

    displace = jnp.zeros((2, ext_r, ext_c), f32)
    for sweep in range(ITERS_R):
        lo_m, hi_m = sweep, ext_r - sweep
        lo_c, hi_c = sweep, ext_c - sweep
        displace = relax_sweep(
            displace,
            mask_wide[lo_m:hi_m, lo_c:hi_c],
            target[:, lo_m + 1 : hi_m - 1, lo_c + 1 : hi_c - 1],
            count[lo_m + 1 : hi_m - 1, lo_c + 1 : hi_c - 1],
        )
    return (owner_flow[:, None, :], source_flow[:, None, :], displace)


def solution(mesh):
    placed = (
        P("ty", "tx"),
        P("ty", "tx"),
        P(None, "ty", "tx"),
        P("ty", "tx"),
        P(None, "ty", "tx"),
        P("ty", "tx"),
        P("ty", "tx"),
    )
    return jax.shard_map(
        shards,
        mesh=mesh,
        in_specs=placed,
        out_specs=(P(None, "ty", "tx"), P(None, "ty", "tx"), P(None, "ty", "tx")),
        check_vma=False,
    )
```

```python
import jax
import jax.numpy as jnp
from jax import lax
from jax.sharding import PartitionSpec as P
from jax.experimental import pallas as pl
from jax.experimental.pallas import tpu as pltpu

PATCH = 128
SHIFTS = 65
RADIUS = 32
WIN = 192
CAP = 2
ITERS_R = 3


SHARPNESS = 256.0
SPRING_RATE = 0.25
FLOW_RATE = 0.5
FLOW_UNIT = 8.0
EPSILON = 1e-05

HALF = PATCH // 2


def flow_kernel(tf_ref, w_ref, out_ref, wlo, whi, corr):
    wf = w_ref[0].astype(jnp.float32)
    wlo[...] = wf[:, 0:PATCH]
    whi[...] = jnp.zeros(whi.shape, jnp.float32)
    whi[:, 0:WIN - HALF] = wf[:, HALF:WIN]
    tfv = tf_ref[0].astype(jnp.float32)
    t_top = tf_ref[0, 0:HALF, :]
    t_bot = tf_ref[0, HALF:PATCH, :]
    corr[...] = jnp.zeros(corr.shape, jnp.float32)

    def step(dy, carry):
        w_lo = wlo[pl.ds(dy, PATCH), :].astype(jnp.bfloat16)
        w_hi = whi[pl.ds(dy, PATCH), :].astype(jnp.bfloat16)
        m_top = jnp.dot(t_top, w_hi, preferred_element_type=jnp.float32)
        m_bot = jnp.dot(t_bot, w_lo, preferred_element_type=jnp.float32)
        r_top = pltpu.roll(m_top, 0, axis=1, stride=1, stride_axis=0)
        r_bot = pltpu.roll(m_bot, 0, axis=1, stride=1, stride_axis=0)
        corr[pl.ds(dy, 1), :] = jnp.sum(r_top + r_bot, axis=0, keepdims=True)
        return carry

    lax.fori_loop(0, SHIFTS, step, 0, unroll=SHIFTS)

    c = corr[...]
    rows = lax.broadcasted_iota(jnp.int32, c.shape, 0)
    lanes = lax.broadcasted_iota(jnp.int32, c.shape, 1)
    valid = (rows < SHIFTS) & (lanes >= HALF - 1)
    e_t = jnp.sum(tfv * tfv, keepdims=True) / float(PATCH * PATCH)
    e_w = jnp.sum(wf * wf, keepdims=True) / float(WIN * WIN)
    denom = float(PATCH * PATCH) * jnp.sqrt((e_t + EPSILON) * (e_w + EPSILON))
    scores = SHARPNESS * c / denom
    scores = jnp.where(valid, scores, -jnp.inf)
    mx = jnp.max(scores, keepdims=True)
    e = jnp.where(valid, jnp.exp(scores - mx), 0.0)
    w = e / jnp.sum(e, keepdims=True)
    sy = (rows - RADIUS).astype(jnp.float32)
    sx = (lanes - (HALF - 1) - RADIUS).astype(jnp.float32)
    fy = jnp.sum(w * sy, keepdims=True) / FLOW_UNIT
    fx = jnp.sum(w * sx, keepdims=True) / FLOW_UNIT
    orow = lax.broadcasted_iota(jnp.int32, (8, 128), 0)
    out_ref[0] = jnp.where(orow == 0, fy, jnp.where(orow == 1, fx, 0.0))

def flows_of(tflipped, windows):
    n = tflipped.shape[0]
    out = pl.pallas_call(
        flow_kernel,
        grid=(n,),
        in_specs=[pl.BlockSpec((1, PATCH, PATCH), lambda i: (i, 0, 0)),
                  pl.BlockSpec((1, WIN, WIN), lambda i: (i, 0, 0))],
        out_specs=pl.BlockSpec((1, 8, 128), lambda i: (i, 0, 0)),
        out_shape=jax.ShapeDtypeStruct((n, 8, 128), jnp.float32),
        scratch_shapes=[pltpu.VMEM((WIN, PATCH), jnp.float32),
                        pltpu.VMEM((WIN, PATCH), jnp.float32),
                        pltpu.VMEM((72, PATCH), jnp.float32)],
    )(tflipped, windows)
    return out[:, 0:2, 0].T


def halo(cells, width):
    n_ty = lax.axis_size("ty")
    n_tx = lax.axis_size("tx")
    height, breadth = cells.shape[-2], cells.shape[-1]
    pieces = {}
    for dy in (-1, 0, 1):
        for dx in (-1, 0, 1):
            if dy == 0 and dx == 0:
                pieces[(dy, dx)] = cells
                continue
            rows = {-1: (height - width, height), 0: (0, height), 1: (0, width)}[dy]
            cols = {-1: (breadth - width, breadth), 0: (0, breadth), 1: (0, width)}[dx]
            part = cells[..., rows[0] : rows[1], cols[0] : cols[1]]
            pairs = []
            for i in range(n_ty):
                for j in range(n_tx):
                    si, sj = i + dy, j + dx
                    if 0 <= si < n_ty and 0 <= sj < n_tx:
                        pairs.append((si * n_tx + sj, i * n_tx + j))
            pieces[(dy, dx)] = lax.ppermute(part, ("ty", "tx"), pairs)
    bands = [
        jnp.concatenate([pieces[(dy, -1)], pieces[(dy, 0)], pieces[(dy, 1)]], axis=-1)
        for dy in (-1, 0, 1)
    ]
    return jnp.concatenate(bands, axis=-2)


def relax_sweep(padded, mask_pad, target, count):
    centre = padded[:, 1:-1, 1:-1]
    mask_c = mask_pad[1:-1, 1:-1]
    height = centre.shape[1]
    width = centre.shape[2]
    spring = jnp.zeros_like(centre)
    for row_step, col_step in ((0, 1), (2, 1), (1, 0), (1, 2)):
        nearby = padded[:, row_step : row_step + height, col_step : col_step + width]
        mask_n = mask_pad[row_step : row_step + height, col_step : col_step + width]
        spring = spring + mask_c * mask_n * (nearby - centre)
    return centre + SPRING_RATE * spring + FLOW_RATE * (target - count * centre)


def one_hot(starts, size, extent, flip=False):
    offs = jnp.arange(size, dtype=jnp.int32)
    if flip:
        offs = size - 1 - offs
    want = starts[:, None, None] + offs[None, :, None]
    return (want == jnp.arange(extent, dtype=jnp.int32)[None, None, :]).astype(jnp.bfloat16)


def shards(
    section_a, section_b, template_corner, template_slot, window_corner, window_slot, node_mask
):
    tile_size = section_a.shape[0]
    slot_count = lax.axis_size("tx") * CAP
    slot_ids = jnp.arange(slot_count, dtype=jnp.int32)
    owner_picker = template_slot[0][:, None] == slot_ids[None, :]
    source_picker = window_slot[0][:, None] == slot_ids[None, :]
    f32 = jnp.float32

    col_pick = one_hot(template_corner[1, 0], PATCH, section_a.shape[1], flip=True)
    row_pick = one_hot(template_corner[0, 0], PATCH, section_a.shape[0])
    by_col = jnp.einsum("krc,ac->kra", col_pick, section_a, preferred_element_type=f32)
    tflipped = jnp.einsum(
        "kra,kia->kri", by_col.astype(jnp.bfloat16), row_pick, preferred_element_type=f32
    ).astype(jnp.bfloat16)
    outgoing = jnp.einsum(
        "ks,kri->sri", owner_picker.astype(jnp.bfloat16), tflipped, preferred_element_type=f32
    ).astype(jnp.bfloat16)

    n_tx = lax.axis_size("tx")
    n_ty = lax.axis_size("ty")
    me_x = lax.axis_index("tx")
    tx_ids = jnp.arange(n_tx, dtype=jnp.int32)
    to_left = (tx_ids == me_x - 1)[:, None]
    to_right = (tx_ids == me_x + 1)[:, None]

    def side_payload(left, right):
        lf = left.reshape(1, -1)
        rf = right.reshape(1, -1)
        return jnp.where(to_left, lf, jnp.where(to_right, rf, jnp.zeros_like(lf)))

    def side_arrivals(got, shape):
        left = lax.dynamic_index_in_dim(got, jnp.maximum(me_x - 1, 0), axis=0, keepdims=False)
        right = lax.dynamic_index_in_dim(got, jnp.minimum(me_x + 1, n_tx - 1), axis=0, keepdims=False)
        left = jnp.where(me_x >= 1, left, jnp.zeros_like(left)).reshape(shape)
        right = jnp.where(me_x + 1 < n_tx, right, jnp.zeros_like(right)).reshape(shape)
        return left, right

    def rows_exchange(cells, width):
        count = n_ty
        height = cells.shape[-2]
        head = cells[..., 0:width, :]
        tail = cells[..., height - width : height, :]
        above = lax.ppermute(tail, "ty", [(i, i + 1) for i in range(count - 1)])
        below = lax.ppermute(head, "ty", [(i + 1, i) for i in range(count - 1)])
        return above, below

    node_rows, node_cols = node_mask.shape
    centre_y = (window_corner[0, 0] + PATCH // 2) * node_rows // tile_size
    centre_x = (window_corner[1, 0] + PATCH // 2) * node_cols // tile_size
    attach = (centre_y[:, None, None] == jnp.arange(node_rows, dtype=jnp.int32)[None, :, None]) & (
        centre_x[:, None, None] == jnp.arange(node_cols, dtype=jnp.int32)[None, None, :]
    )
    count = jnp.sum(attach.astype(f32), axis=0)
    mask = node_mask.astype(f32)
    fixed = jnp.stack([count, mask]).astype(jnp.bfloat16)
    w = ITERS_R
    b_cols = section_b.shape[1]
    send = jnp.concatenate(
        [
            outgoing.reshape(n_tx, -1),
            side_payload(section_b[:, 0:RADIUS], section_b[:, b_cols - RADIUS :]),
            side_payload(fixed[:, :, 0:w], fixed[:, :, node_cols - w :]),
        ],
        axis=1,
    )
    got = lax.all_to_all(send, "tx", split_axis=0, concat_axis=0, tiled=True)
    t_len = outgoing.size // n_tx
    b_len = section_b.shape[0] * RADIUS
    arrived = got[:, 0:t_len].reshape(outgoing.shape)
    b_left, b_right = side_arrivals(got[:, t_len : t_len + b_len], (section_b.shape[0], RADIUS))
    f_left, f_right = side_arrivals(got[:, t_len + b_len :], (2, node_rows, w))
    b_tx = jnp.concatenate([b_left, section_b, b_right], axis=1)
    fixed_tx = jnp.concatenate([f_left, fixed, f_right], axis=2)

    b_len_row = RADIUS * b_tx.shape[1]
    stacked_head = jnp.concatenate(
        [b_tx[0:RADIUS].reshape(-1), fixed_tx[:, 0:w].reshape(-1)]
    )
    stacked_tail = jnp.concatenate(
        [b_tx[b_tx.shape[0] - RADIUS :].reshape(-1), fixed_tx[:, node_rows - w :].reshape(-1)]
    )
    above = lax.ppermute(stacked_tail, "ty", [(i, i + 1) for i in range(n_ty - 1)])
    below = lax.ppermute(stacked_head, "ty", [(i + 1, i) for i in range(n_ty - 1)])
    b_wide = jnp.concatenate(
        [
            above[0:b_len_row].reshape(RADIUS, -1),
            b_tx,
            below[0:b_len_row].reshape(RADIUS, -1),
        ],
        axis=0,
    )
    fixed_wide = jnp.concatenate(
        [
            above[b_len_row:].reshape(2, w, -1),
            fixed_tx,
            below[b_len_row:].reshape(2, w, -1),
        ],
        axis=1,
    ).astype(f32)

    wrow_pick = one_hot(window_corner[0, 0], WIN, b_wide.shape[0])
    wcol_pick = one_hot(window_corner[1, 0], WIN, b_wide.shape[1])
    by_row = jnp.einsum("mra,ac->mrc", wrow_pick, b_wide, preferred_element_type=f32)
    windows = jnp.einsum(
        "mrc,msc->mrs", by_row.astype(jnp.bfloat16), wcol_pick, preferred_element_type=f32
    ).astype(jnp.bfloat16)
    matched = jnp.einsum(
        "ms,sri->mri", source_picker.astype(jnp.bfloat16), arrived, preferred_element_type=f32
    ).astype(jnp.bfloat16)

    flows = flows_of(matched, windows)
    source_flow = -flows

    target = jnp.sum(jnp.where(attach[None], source_flow[:, :, None, None], 0.0), axis=1)
    returned = jnp.sum(jnp.where(source_picker[None], flows[:, :, None], 0.0), axis=1)
    back = jnp.concatenate(
        [
            returned.reshape(2, n_tx, CAP).transpose(1, 0, 2).reshape(n_tx, -1),
            side_payload(target[:, :, 0:w], target[:, :, node_cols - w :]),
        ],
        axis=1,
    )
    came = lax.all_to_all(back, "tx", split_axis=0, concat_axis=0, tiled=True)
    landed = came[:, 0 : 2 * CAP].reshape(n_tx, 2, CAP).transpose(1, 0, 2).reshape(2, -1)
    owner_flow = jnp.sum(jnp.where(owner_picker[None], landed[:, None, :], 0.0), axis=2)
    t_left, t_right = side_arrivals(came[:, 2 * CAP :], (2, node_rows, w))
    target_tx = jnp.concatenate([t_left, target, t_right], axis=2)
    t_above, t_below = rows_exchange(target_tx, w)
    target_wide = jnp.concatenate([t_above, target_tx, t_below], axis=1)

    wide = jnp.concatenate([target_wide, fixed_wide], axis=0)
    displace = jnp.zeros((2,) + wide.shape[1:], f32)
    for sweep in range(ITERS_R):
        lo_m, hi_m = sweep, wide.shape[1] - sweep
        lo_t, hi_t = sweep + 1, wide.shape[1] - sweep - 1
        displace = relax_sweep(
            displace,
            wide[3, lo_m:hi_m, lo_m:hi_m],
            wide[0:2, lo_t:hi_t, lo_t:hi_t],
            wide[2, lo_t:hi_t, lo_t:hi_t],
        )
    return (owner_flow[:, None, :], source_flow[:, None, :], displace)


def solution(mesh):
    placed = (
        P("ty", "tx"),
        P("ty", "tx"),
        P(None, "ty", "tx"),
        P("ty", "tx"),
        P(None, "ty", "tx"),
        P("ty", "tx"),
        P("ty", "tx"),
    )
    return jax.shard_map(
        shards,
        mesh=mesh,
        in_specs=placed,
        out_specs=(P(None, "ty", "tx"), P(None, "ty", "tx"), P(None, "ty", "tx")),
        check_vma=False,
    )
```

```python
import jax
import jax.numpy as jnp
from jax import lax
from jax.sharding import PartitionSpec as P
from jax.experimental import pallas as pl
from jax.experimental.pallas import tpu as pltpu

PATCH = 128
SHIFTS = 65
RADIUS = 32
WIN = 192
CAP = 2
ITERS_R = 3


SHARPNESS = 256.0
SPRING_RATE = 0.25
FLOW_RATE = 0.5
FLOW_UNIT = 8.0
EPSILON = 1e-05

HALF = PATCH // 2


def flow_kernel(tf_ref, w_ref, out_ref, wlo, whi, corr):
    wf = w_ref[0].astype(jnp.float32)
    wlo[...] = wf[:, 0:PATCH]
    whi[...] = jnp.zeros(whi.shape, jnp.float32)
    whi[:, 0:WIN - HALF] = wf[:, HALF:WIN]
    tfv = tf_ref[0].astype(jnp.float32)
    t_top = tf_ref[0, 0:HALF, :]
    t_bot = tf_ref[0, HALF:PATCH, :]
    corr[...] = jnp.zeros(corr.shape, jnp.float32)

    def step(dy, carry):
        w_lo = wlo[pl.ds(dy, PATCH), :].astype(jnp.bfloat16)
        w_hi = whi[pl.ds(dy, PATCH), :].astype(jnp.bfloat16)
        m_top = jnp.dot(t_top, w_hi, preferred_element_type=jnp.float32)
        m_bot = jnp.dot(t_bot, w_lo, preferred_element_type=jnp.float32)
        r_top = pltpu.roll(m_top, 0, axis=1, stride=1, stride_axis=0)
        r_bot = pltpu.roll(m_bot, 0, axis=1, stride=1, stride_axis=0)
        corr[pl.ds(dy, 1), :] = jnp.sum(r_top + r_bot, axis=0, keepdims=True)
        return carry

    lax.fori_loop(0, SHIFTS, step, 0, unroll=SHIFTS)

    c = corr[...]
    rows = lax.broadcasted_iota(jnp.int32, c.shape, 0)
    lanes = lax.broadcasted_iota(jnp.int32, c.shape, 1)
    valid = (rows < SHIFTS) & (lanes >= HALF - 1)
    e_t = jnp.sum(tfv * tfv, keepdims=True) / float(PATCH * PATCH)
    e_w = jnp.sum(wf * wf, keepdims=True) / float(WIN * WIN)
    denom = float(PATCH * PATCH) * jnp.sqrt((e_t + EPSILON) * (e_w + EPSILON))
    scores = SHARPNESS * c / denom
    scores = jnp.where(valid, scores, -jnp.inf)
    mx = jnp.max(scores, keepdims=True)
    e = jnp.where(valid, jnp.exp(scores - mx), 0.0)
    w = e / jnp.sum(e, keepdims=True)
    sy = (rows - RADIUS).astype(jnp.float32)
    sx = (lanes - (HALF - 1) - RADIUS).astype(jnp.float32)
    fy = jnp.sum(w * sy, keepdims=True) / FLOW_UNIT
    fx = jnp.sum(w * sx, keepdims=True) / FLOW_UNIT
    orow = lax.broadcasted_iota(jnp.int32, (8, 128), 0)
    out_ref[0] = jnp.where(orow == 0, fy, jnp.where(orow == 1, fx, 0.0))

def flows_of(tflipped, windows):
    n = tflipped.shape[0]
    out = pl.pallas_call(
        flow_kernel,
        grid=(n,),
        in_specs=[pl.BlockSpec((1, PATCH, PATCH), lambda i: (i, 0, 0)),
                  pl.BlockSpec((1, WIN, WIN), lambda i: (i, 0, 0))],
        out_specs=pl.BlockSpec((1, 8, 128), lambda i: (i, 0, 0)),
        out_shape=jax.ShapeDtypeStruct((n, 8, 128), jnp.float32),
        scratch_shapes=[pltpu.VMEM((WIN, PATCH), jnp.float32),
                        pltpu.VMEM((WIN, PATCH), jnp.float32),
                        pltpu.VMEM((72, PATCH), jnp.float32)],
    )(tflipped, windows)
    return out[:, 0:2, 0].T


def halo(cells, width):
    n_ty = lax.axis_size("ty")
    n_tx = lax.axis_size("tx")
    height, breadth = cells.shape[-2], cells.shape[-1]
    pieces = {}
    for dy in (-1, 0, 1):
        for dx in (-1, 0, 1):
            if dy == 0 and dx == 0:
                pieces[(dy, dx)] = cells
                continue
            rows = {-1: (height - width, height), 0: (0, height), 1: (0, width)}[dy]
            cols = {-1: (breadth - width, breadth), 0: (0, breadth), 1: (0, width)}[dx]
            part = cells[..., rows[0] : rows[1], cols[0] : cols[1]]
            pairs = []
            for i in range(n_ty):
                for j in range(n_tx):
                    si, sj = i + dy, j + dx
                    if 0 <= si < n_ty and 0 <= sj < n_tx:
                        pairs.append((si * n_tx + sj, i * n_tx + j))
            pieces[(dy, dx)] = lax.ppermute(part, ("ty", "tx"), pairs)
    bands = [
        jnp.concatenate([pieces[(dy, -1)], pieces[(dy, 0)], pieces[(dy, 1)]], axis=-1)
        for dy in (-1, 0, 1)
    ]
    return jnp.concatenate(bands, axis=-2)


def relax_sweep(padded, mask_pad, target, count):
    centre = padded[:, 1:-1, 1:-1]
    mask_c = mask_pad[1:-1, 1:-1]
    height = centre.shape[1]
    width = centre.shape[2]
    spring = jnp.zeros_like(centre)
    for row_step, col_step in ((0, 1), (2, 1), (1, 0), (1, 2)):
        nearby = padded[:, row_step : row_step + height, col_step : col_step + width]
        mask_n = mask_pad[row_step : row_step + height, col_step : col_step + width]
        spring = spring + mask_c * mask_n * (nearby - centre)
    return centre + SPRING_RATE * spring + FLOW_RATE * (target - count * centre)


def one_hot(starts, size, extent, flip=False):
    offs = jnp.arange(size, dtype=jnp.int32)
    if flip:
        offs = size - 1 - offs
    want = starts[:, None, None] + offs[None, :, None]
    return (want == jnp.arange(extent, dtype=jnp.int32)[None, None, :]).astype(jnp.bfloat16)


def shards(
    section_a, section_b, template_corner, template_slot, window_corner, window_slot, node_mask
):
    tile_size = section_a.shape[0]
    slot_count = lax.axis_size("tx") * CAP
    slot_ids = jnp.arange(slot_count, dtype=jnp.int32)
    owner_picker = template_slot[0][:, None] == slot_ids[None, :]
    source_picker = window_slot[0][:, None] == slot_ids[None, :]
    f32 = jnp.float32

    col_pick = one_hot(template_corner[1, 0], PATCH, section_a.shape[1], flip=True)
    row_pick = one_hot(template_corner[0, 0], PATCH, section_a.shape[0])
    by_col = jnp.einsum("krc,ac->kra", col_pick, section_a, preferred_element_type=f32)
    tflipped = jnp.einsum(
        "kra,kia->kri", by_col.astype(jnp.bfloat16), row_pick, preferred_element_type=f32
    ).astype(jnp.bfloat16)
    outgoing = jnp.einsum(
        "ks,kri->sri", owner_picker.astype(jnp.bfloat16), tflipped, preferred_element_type=f32
    ).astype(jnp.bfloat16)

    n_tx = lax.axis_size("tx")
    n_ty = lax.axis_size("ty")
    me_x = lax.axis_index("tx")
    tx_ids = jnp.arange(n_tx, dtype=jnp.int32)
    to_left = (tx_ids == me_x - 1)[:, None]
    to_right = (tx_ids == me_x + 1)[:, None]

    def side_payload(left, right):
        lf = left.reshape(1, -1)
        rf = right.reshape(1, -1)
        return jnp.where(to_left, lf, jnp.where(to_right, rf, jnp.zeros_like(lf)))

    def side_arrivals(got, shape):
        left = lax.dynamic_index_in_dim(got, jnp.maximum(me_x - 1, 0), axis=0, keepdims=False)
        right = lax.dynamic_index_in_dim(got, jnp.minimum(me_x + 1, n_tx - 1), axis=0, keepdims=False)
        left = jnp.where(me_x >= 1, left, jnp.zeros_like(left)).reshape(shape)
        right = jnp.where(me_x + 1 < n_tx, right, jnp.zeros_like(right)).reshape(shape)
        return left, right

    def rows_exchange(cells, width):
        count = n_ty
        height = cells.shape[-2]
        head = cells[..., 0:width, :]
        tail = cells[..., height - width : height, :]
        above = lax.ppermute(tail, "ty", [(i, i + 1) for i in range(count - 1)])
        below = lax.ppermute(head, "ty", [(i + 1, i) for i in range(count - 1)])
        return above, below

    node_rows, node_cols = node_mask.shape
    centre_y = (window_corner[0, 0] + PATCH // 2) * node_rows // tile_size
    centre_x = (window_corner[1, 0] + PATCH // 2) * node_cols // tile_size
    attach = (centre_y[:, None, None] == jnp.arange(node_rows, dtype=jnp.int32)[None, :, None]) & (
        centre_x[:, None, None] == jnp.arange(node_cols, dtype=jnp.int32)[None, None, :]
    )
    count = jnp.sum(attach.astype(f32), axis=0)
    mask = node_mask.astype(f32)
    w = ITERS_R
    arrived = lax.all_to_all(outgoing, "tx", split_axis=0, concat_axis=0, tiled=True)
    b_wide = halo(section_b, RADIUS)

    wrow_pick = one_hot(window_corner[0, 0], WIN, b_wide.shape[0])
    wcol_pick = one_hot(window_corner[1, 0], WIN, b_wide.shape[1])
    by_row = jnp.einsum("mra,ac->mrc", wrow_pick, b_wide, preferred_element_type=f32)
    windows = jnp.einsum(
        "mrc,msc->mrs", by_row.astype(jnp.bfloat16), wcol_pick, preferred_element_type=f32
    ).astype(jnp.bfloat16)
    matched = jnp.einsum(
        "ms,sri->mri", source_picker.astype(jnp.bfloat16), arrived, preferred_element_type=f32
    ).astype(jnp.bfloat16)

    flows = flows_of(matched, windows)
    source_flow = -flows

    target = jnp.sum(jnp.where(attach[None], source_flow[:, :, None, None], 0.0), axis=1)
    fields = jnp.concatenate([target, count[None], mask[None]], axis=0)
    returned = jnp.sum(jnp.where(source_picker[None], flows[:, :, None], 0.0), axis=1)
    back = jnp.concatenate(
        [
            returned.reshape(2, n_tx, CAP).transpose(1, 0, 2).reshape(n_tx, -1),
            side_payload(fields[:, :, 0:w], fields[:, :, node_cols - w :]),
        ],
        axis=1,
    )
    came = lax.all_to_all(back, "tx", split_axis=0, concat_axis=0, tiled=True)
    landed = came[:, 0 : 2 * CAP].reshape(n_tx, 2, CAP).transpose(1, 0, 2).reshape(2, -1)
    owner_flow = jnp.sum(jnp.where(owner_picker[None], landed[:, None, :], 0.0), axis=2)
    f_left, f_right = side_arrivals(came[:, 2 * CAP :], (fields.shape[0], node_rows, w))
    fields_tx = jnp.concatenate([f_left, fields, f_right], axis=2)
    f_above, f_below = rows_exchange(fields_tx, w)
    wide = jnp.concatenate([f_above, fields_tx, f_below], axis=1)

    displace = jnp.zeros((2,) + wide.shape[1:], f32)
    for sweep in range(ITERS_R):
        lo_m, hi_m = sweep, wide.shape[1] - sweep
        lo_t, hi_t = sweep + 1, wide.shape[1] - sweep - 1
        displace = relax_sweep(
            displace,
            wide[3, lo_m:hi_m, lo_m:hi_m],
            wide[0:2, lo_t:hi_t, lo_t:hi_t],
            wide[2, lo_t:hi_t, lo_t:hi_t],
        )
    return (owner_flow[:, None, :], source_flow[:, None, :], displace)


def solution(mesh):
    placed = (
        P("ty", "tx"),
        P("ty", "tx"),
        P(None, "ty", "tx"),
        P("ty", "tx"),
        P(None, "ty", "tx"),
        P("ty", "tx"),
        P("ty", "tx"),
    )
    return jax.shard_map(
        shards,
        mesh=mesh,
        in_specs=placed,
        out_specs=(P(None, "ty", "tx"), P(None, "ty", "tx"), P(None, "ty", "tx")),
        check_vma=False,
    )
```

```python
import jax
import jax.numpy as jnp
from jax import lax
from jax.sharding import PartitionSpec as P
from jax.experimental import pallas as pl
from jax.experimental.pallas import tpu as pltpu

PATCH = 128
SHIFTS = 65
RADIUS = 32
WIN = 192
CAP = 2
ITERS_R = 3


SHARPNESS = 256.0
SPRING_RATE = 0.25
FLOW_RATE = 0.5
FLOW_UNIT = 8.0
EPSILON = 1e-05

HALF = PATCH // 2


def flow_kernel(tf_ref, w_ref, out_ref, wlo, whi, corr):
    wf = w_ref[0].astype(jnp.float32)
    wlo[...] = wf[:, 0:PATCH]
    whi[...] = jnp.zeros(whi.shape, jnp.float32)
    whi[:, 0:WIN - HALF] = wf[:, HALF:WIN]
    tfv = tf_ref[0].astype(jnp.float32)
    t_top = tf_ref[0, 0:HALF, :]
    t_bot = tf_ref[0, HALF:PATCH, :]
    corr[...] = jnp.zeros(corr.shape, jnp.float32)

    def step(dy, carry):
        w_lo = wlo[pl.ds(dy, PATCH), :].astype(jnp.bfloat16)
        w_hi = whi[pl.ds(dy, PATCH), :].astype(jnp.bfloat16)
        m_top = jnp.dot(t_top, w_hi, preferred_element_type=jnp.float32)
        m_bot = jnp.dot(t_bot, w_lo, preferred_element_type=jnp.float32)
        r_top = pltpu.roll(m_top, 0, axis=1, stride=1, stride_axis=0)
        r_bot = pltpu.roll(m_bot, 0, axis=1, stride=1, stride_axis=0)
        corr[pl.ds(dy, 1), :] = jnp.sum(r_top + r_bot, axis=0, keepdims=True)
        return carry

    lax.fori_loop(0, SHIFTS, step, 0, unroll=SHIFTS)

    c = corr[...]
    rows = lax.broadcasted_iota(jnp.int32, c.shape, 0)
    lanes = lax.broadcasted_iota(jnp.int32, c.shape, 1)
    valid = (rows < SHIFTS) & (lanes >= HALF - 1)
    e_t = jnp.sum(tfv * tfv, keepdims=True) / float(PATCH * PATCH)
    e_w = jnp.sum(wf * wf, keepdims=True) / float(WIN * WIN)
    denom = float(PATCH * PATCH) * jnp.sqrt((e_t + EPSILON) * (e_w + EPSILON))
    scores = SHARPNESS * c / denom
    scores = jnp.where(valid, scores, -jnp.inf)
    mx = jnp.max(scores, keepdims=True)
    e = jnp.where(valid, jnp.exp(scores - mx), 0.0)
    w = e / jnp.sum(e, keepdims=True)
    sy = (rows - RADIUS).astype(jnp.float32)
    sx = (lanes - (HALF - 1) - RADIUS).astype(jnp.float32)
    fy = jnp.sum(w * sy, keepdims=True) / FLOW_UNIT
    fx = jnp.sum(w * sx, keepdims=True) / FLOW_UNIT
    orow = lax.broadcasted_iota(jnp.int32, (8, 128), 0)
    out_ref[0] = jnp.where(orow == 0, fy, jnp.where(orow == 1, fx, 0.0))

def flows_of(tflipped, windows):
    n = tflipped.shape[0]
    out = pl.pallas_call(
        flow_kernel,
        grid=(n,),
        in_specs=[pl.BlockSpec((1, PATCH, PATCH), lambda i: (i, 0, 0)),
                  pl.BlockSpec((1, WIN, WIN), lambda i: (i, 0, 0))],
        out_specs=pl.BlockSpec((1, 8, 128), lambda i: (i, 0, 0)),
        out_shape=jax.ShapeDtypeStruct((n, 8, 128), jnp.float32),
        scratch_shapes=[pltpu.VMEM((WIN, PATCH), jnp.float32),
                        pltpu.VMEM((WIN, PATCH), jnp.float32),
                        pltpu.VMEM((72, PATCH), jnp.float32)],
    )(tflipped, windows)
    return out[:, 0:2, 0].T


def halo(cells, width):
    n_ty = lax.axis_size("ty")
    n_tx = lax.axis_size("tx")
    height, breadth = cells.shape[-2], cells.shape[-1]
    pieces = {}
    for dy in (-1, 0, 1):
        for dx in (-1, 0, 1):
            if dy == 0 and dx == 0:
                pieces[(dy, dx)] = cells
                continue
            rows = {-1: (height - width, height), 0: (0, height), 1: (0, width)}[dy]
            cols = {-1: (breadth - width, breadth), 0: (0, breadth), 1: (0, width)}[dx]
            part = cells[..., rows[0] : rows[1], cols[0] : cols[1]]
            pairs = []
            for i in range(n_ty):
                for j in range(n_tx):
                    si, sj = i + dy, j + dx
                    if 0 <= si < n_ty and 0 <= sj < n_tx:
                        pairs.append((si * n_tx + sj, i * n_tx + j))
            pieces[(dy, dx)] = lax.ppermute(part, ("ty", "tx"), pairs)
    bands = [
        jnp.concatenate([pieces[(dy, -1)], pieces[(dy, 0)], pieces[(dy, 1)]], axis=-1)
        for dy in (-1, 0, 1)
    ]
    return jnp.concatenate(bands, axis=-2)


def relax_sweep(padded, mask_pad, target, count):
    centre = padded[:, 1:-1, 1:-1]
    mask_c = mask_pad[1:-1, 1:-1]
    height = centre.shape[1]
    width = centre.shape[2]
    spring = jnp.zeros_like(centre)
    for row_step, col_step in ((0, 1), (2, 1), (1, 0), (1, 2)):
        nearby = padded[:, row_step : row_step + height, col_step : col_step + width]
        mask_n = mask_pad[row_step : row_step + height, col_step : col_step + width]
        spring = spring + mask_c * mask_n * (nearby - centre)
    return centre + SPRING_RATE * spring + FLOW_RATE * (target - count * centre)


def one_hot(starts, size, extent, flip=False):
    offs = jnp.arange(size, dtype=jnp.int32)
    if flip:
        offs = size - 1 - offs
    want = starts[:, None, None] + offs[None, :, None]
    return (want == jnp.arange(extent, dtype=jnp.int32)[None, None, :]).astype(jnp.bfloat16)


def shards(
    section_a, section_b, template_corner, template_slot, window_corner, window_slot, node_mask
):
    tile_size = section_a.shape[0]
    slot_count = lax.axis_size("tx") * CAP
    slot_ids = jnp.arange(slot_count, dtype=jnp.int32)
    owner_picker = template_slot[0][:, None] == slot_ids[None, :]
    source_picker = window_slot[0][:, None] == slot_ids[None, :]
    f32 = jnp.float32

    col_pick = one_hot(template_corner[1, 0], PATCH, section_a.shape[1], flip=True)
    row_pick = one_hot(template_corner[0, 0], PATCH, section_a.shape[0])
    by_col = jnp.einsum("krc,ac->kra", col_pick, section_a, preferred_element_type=f32)
    tflipped = jnp.einsum(
        "kra,kia->kri", by_col.astype(jnp.bfloat16), row_pick, preferred_element_type=f32
    ).astype(jnp.bfloat16)
    outgoing = jnp.einsum(
        "ks,kri->sri", owner_picker.astype(jnp.bfloat16), tflipped, preferred_element_type=f32
    ).astype(jnp.bfloat16)

    n_tx = lax.axis_size("tx")
    n_ty = lax.axis_size("ty")
    me_x = lax.axis_index("tx")
    tx_ids = jnp.arange(n_tx, dtype=jnp.int32)
    to_left = (tx_ids == me_x - 1)[:, None]
    to_right = (tx_ids == me_x + 1)[:, None]

    def side_payload(left, right):
        lf = left.reshape(1, -1)
        rf = right.reshape(1, -1)
        return jnp.where(to_left, lf, jnp.where(to_right, rf, jnp.zeros_like(lf)))

    def side_arrivals(got, shape):
        left = lax.dynamic_index_in_dim(got, jnp.maximum(me_x - 1, 0), axis=0, keepdims=False)
        right = lax.dynamic_index_in_dim(got, jnp.minimum(me_x + 1, n_tx - 1), axis=0, keepdims=False)
        left = jnp.where(me_x >= 1, left, jnp.zeros_like(left)).reshape(shape)
        right = jnp.where(me_x + 1 < n_tx, right, jnp.zeros_like(right)).reshape(shape)
        return left, right

    def rows_exchange(cells, width):
        count = n_ty
        height = cells.shape[-2]
        head = cells[..., 0:width, :]
        tail = cells[..., height - width : height, :]
        above = lax.ppermute(tail, "ty", [(i, i + 1) for i in range(count - 1)])
        below = lax.ppermute(head, "ty", [(i + 1, i) for i in range(count - 1)])
        return above, below

    node_rows, node_cols = node_mask.shape
    centre_y = (window_corner[0, 0] + PATCH // 2) * node_rows // tile_size
    centre_x = (window_corner[1, 0] + PATCH // 2) * node_cols // tile_size
    attach = (centre_y[:, None, None] == jnp.arange(node_rows, dtype=jnp.int32)[None, :, None]) & (
        centre_x[:, None, None] == jnp.arange(node_cols, dtype=jnp.int32)[None, None, :]
    )
    count = jnp.sum(attach.astype(f32), axis=0)
    mask = node_mask.astype(f32)
    w = ITERS_R
    b_rows, b_cols = section_b.shape
    rim_send = side_payload(section_b[:, 0:RADIUS], section_b[:, b_cols - RADIUS :])
    slot_shape = outgoing.shape[1:]
    send = jnp.concatenate(
        [outgoing.reshape((n_tx, CAP) + slot_shape), rim_send.reshape((n_tx, 1) + slot_shape)], axis=1
    )
    got = lax.all_to_all(send, "tx", split_axis=0, concat_axis=0, tiled=True)
    arrived = got[:, 0:CAP].reshape(outgoing.shape)
    b_left, b_right = side_arrivals(got[:, CAP].reshape(n_tx, -1), (b_rows, RADIUS))
    b_tx = jnp.concatenate([b_left, section_b, b_right], axis=1)
    b_above, b_below = rows_exchange(b_tx, RADIUS)
    b_wide = jnp.concatenate([b_above, b_tx, b_below], axis=0)

    wrow_pick = one_hot(window_corner[0, 0], WIN, b_wide.shape[0])
    wcol_pick = one_hot(window_corner[1, 0], WIN, b_wide.shape[1])
    by_row = jnp.einsum("mra,ac->mrc", wrow_pick, b_wide, preferred_element_type=f32)
    windows = jnp.einsum(
        "mrc,msc->mrs", by_row.astype(jnp.bfloat16), wcol_pick, preferred_element_type=f32
    ).astype(jnp.bfloat16)
    matched = jnp.einsum(
        "ms,sri->mri", source_picker.astype(jnp.bfloat16), arrived, preferred_element_type=f32
    ).astype(jnp.bfloat16)

    flows = flows_of(matched, windows)
    source_flow = -flows

    target = jnp.sum(jnp.where(attach[None], source_flow[:, :, None, None], 0.0), axis=1)
    fields = jnp.concatenate([target, count[None], mask[None]], axis=0)
    returned = jnp.sum(jnp.where(source_picker[None], flows[:, :, None], 0.0), axis=1)
    back = jnp.concatenate(
        [
            returned.reshape(2, n_tx, CAP).transpose(1, 0, 2).reshape(n_tx, -1),
            side_payload(fields[:, :, 0:w], fields[:, :, node_cols - w :]),
        ],
        axis=1,
    )
    came = lax.all_to_all(back, "tx", split_axis=0, concat_axis=0, tiled=True)
    landed = came[:, 0 : 2 * CAP].reshape(n_tx, 2, CAP).transpose(1, 0, 2).reshape(2, -1)
    owner_flow = jnp.sum(jnp.where(owner_picker[None], landed[:, None, :], 0.0), axis=2)
    f_left, f_right = side_arrivals(came[:, 2 * CAP :], (fields.shape[0], node_rows, w))
    fields_tx = jnp.concatenate([f_left, fields, f_right], axis=2)
    f_above, f_below = rows_exchange(fields_tx, w)
    wide = jnp.concatenate([f_above, fields_tx, f_below], axis=1)

    displace = jnp.zeros((2,) + wide.shape[1:], f32)
    for sweep in range(ITERS_R):
        lo_m, hi_m = sweep, wide.shape[1] - sweep
        lo_t, hi_t = sweep + 1, wide.shape[1] - sweep - 1
        displace = relax_sweep(
            displace,
            wide[3, lo_m:hi_m, lo_m:hi_m],
            wide[0:2, lo_t:hi_t, lo_t:hi_t],
            wide[2, lo_t:hi_t, lo_t:hi_t],
        )
    return (owner_flow[:, None, :], source_flow[:, None, :], displace)


def solution(mesh):
    placed = (
        P("ty", "tx"),
        P("ty", "tx"),
        P(None, "ty", "tx"),
        P("ty", "tx"),
        P(None, "ty", "tx"),
        P("ty", "tx"),
        P("ty", "tx"),
    )
    return jax.shard_map(
        shards,
        mesh=mesh,
        in_specs=placed,
        out_specs=(P(None, "ty", "tx"), P(None, "ty", "tx"), P(None, "ty", "tx")),
        check_vma=False,
    )
```

```python
import jax
import jax.numpy as jnp
from jax import lax
from jax.sharding import PartitionSpec as P
from jax.experimental import pallas as pl
from jax.experimental.pallas import tpu as pltpu

PATCH = 128
SHIFTS = 65
RADIUS = 32
WIN = 192
CAP = 2
ITERS_R = 3


SHARPNESS = 256.0
SPRING_RATE = 0.25
FLOW_RATE = 0.5
FLOW_UNIT = 8.0
EPSILON = 1e-05

HALF = PATCH // 2


def flow_kernel(tf_ref, w_ref, out_ref, wlo, whi, corr):
    wf = w_ref[0].astype(jnp.float32)
    wlo[...] = wf[:, 0:PATCH]
    whi[...] = jnp.zeros(whi.shape, jnp.float32)
    whi[:, 0:WIN - HALF] = wf[:, HALF:WIN]
    tfv = tf_ref[0].astype(jnp.float32)
    t_top = tf_ref[0, 0:HALF, :]
    t_bot = tf_ref[0, HALF:PATCH, :]
    corr[...] = jnp.zeros(corr.shape, jnp.float32)

    def step(dy, carry):
        w_lo = wlo[pl.ds(dy, PATCH), :].astype(jnp.bfloat16)
        w_hi = whi[pl.ds(dy, PATCH), :].astype(jnp.bfloat16)
        m_top = jnp.dot(t_top, w_hi, preferred_element_type=jnp.float32)
        m_bot = jnp.dot(t_bot, w_lo, preferred_element_type=jnp.float32)
        r_top = pltpu.roll(m_top, 0, axis=1, stride=1, stride_axis=0)
        r_bot = pltpu.roll(m_bot, 0, axis=1, stride=1, stride_axis=0)
        corr[pl.ds(dy, 1), :] = jnp.sum(r_top + r_bot, axis=0, keepdims=True)
        return carry

    lax.fori_loop(0, SHIFTS, step, 0, unroll=SHIFTS)

    c = corr[...]
    rows = lax.broadcasted_iota(jnp.int32, c.shape, 0)
    lanes = lax.broadcasted_iota(jnp.int32, c.shape, 1)
    valid = (rows < SHIFTS) & (lanes >= HALF - 1)
    e_t = jnp.sum(tfv * tfv, keepdims=True) / float(PATCH * PATCH)
    e_w = jnp.sum(wf * wf, keepdims=True) / float(WIN * WIN)
    denom = float(PATCH * PATCH) * jnp.sqrt((e_t + EPSILON) * (e_w + EPSILON))
    scores = SHARPNESS * c / denom
    scores = jnp.where(valid, scores, -jnp.inf)
    mx = jnp.max(scores, keepdims=True)
    e = jnp.where(valid, jnp.exp(scores - mx), 0.0)
    w = e / jnp.sum(e, keepdims=True)
    sy = (rows - RADIUS).astype(jnp.float32)
    sx = (lanes - (HALF - 1) - RADIUS).astype(jnp.float32)
    fy = jnp.sum(w * sy, keepdims=True) / FLOW_UNIT
    fx = jnp.sum(w * sx, keepdims=True) / FLOW_UNIT
    orow = lax.broadcasted_iota(jnp.int32, (8, 128), 0)
    out_ref[0] = jnp.where(orow == 0, fy, jnp.where(orow == 1, fx, 0.0))

def flows_of(tflipped, windows):
    n = tflipped.shape[0]
    out = pl.pallas_call(
        flow_kernel,
        grid=(n,),
        in_specs=[pl.BlockSpec((1, PATCH, PATCH), lambda i: (i, 0, 0)),
                  pl.BlockSpec((1, WIN, WIN), lambda i: (i, 0, 0))],
        out_specs=pl.BlockSpec((1, 8, 128), lambda i: (i, 0, 0)),
        out_shape=jax.ShapeDtypeStruct((n, 8, 128), jnp.float32),
        scratch_shapes=[pltpu.VMEM((WIN, PATCH), jnp.float32),
                        pltpu.VMEM((WIN, PATCH), jnp.float32),
                        pltpu.VMEM((72, PATCH), jnp.float32)],
    )(tflipped, windows)
    return out[:, 0:2, 0].T


def halo(cells, width):
    n_ty = lax.axis_size("ty")
    n_tx = lax.axis_size("tx")
    height, breadth = cells.shape[-2], cells.shape[-1]
    pieces = {}
    for dy in (-1, 0, 1):
        for dx in (-1, 0, 1):
            if dy == 0 and dx == 0:
                pieces[(dy, dx)] = cells
                continue
            rows = {-1: (height - width, height), 0: (0, height), 1: (0, width)}[dy]
            cols = {-1: (breadth - width, breadth), 0: (0, breadth), 1: (0, width)}[dx]
            part = cells[..., rows[0] : rows[1], cols[0] : cols[1]]
            pairs = []
            for i in range(n_ty):
                for j in range(n_tx):
                    si, sj = i + dy, j + dx
                    if 0 <= si < n_ty and 0 <= sj < n_tx:
                        pairs.append((si * n_tx + sj, i * n_tx + j))
            pieces[(dy, dx)] = lax.ppermute(part, ("ty", "tx"), pairs)
    bands = [
        jnp.concatenate([pieces[(dy, -1)], pieces[(dy, 0)], pieces[(dy, 1)]], axis=-1)
        for dy in (-1, 0, 1)
    ]
    return jnp.concatenate(bands, axis=-2)


def relax_sweep(padded, mask_pad, target, count):
    centre = padded[:, 1:-1, 1:-1]
    mask_c = mask_pad[1:-1, 1:-1]
    height = centre.shape[1]
    width = centre.shape[2]
    spring = jnp.zeros_like(centre)
    for row_step, col_step in ((0, 1), (2, 1), (1, 0), (1, 2)):
        nearby = padded[:, row_step : row_step + height, col_step : col_step + width]
        mask_n = mask_pad[row_step : row_step + height, col_step : col_step + width]
        spring = spring + mask_c * mask_n * (nearby - centre)
    return centre + SPRING_RATE * spring + FLOW_RATE * (target - count * centre)


def one_hot(starts, size, extent, flip=False):
    offs = jnp.arange(size, dtype=jnp.int32)
    if flip:
        offs = size - 1 - offs
    want = starts[:, None, None] + offs[None, :, None]
    return (want == jnp.arange(extent, dtype=jnp.int32)[None, None, :]).astype(jnp.bfloat16)


def shards(
    section_a, section_b, template_corner, template_slot, window_corner, window_slot, node_mask
):
    tile_size = section_a.shape[0]
    slot_count = lax.axis_size("tx") * CAP
    slot_ids = jnp.arange(slot_count, dtype=jnp.int32)
    owner_picker = template_slot[0][:, None] == slot_ids[None, :]
    source_picker = window_slot[0][:, None] == slot_ids[None, :]
    f32 = jnp.float32

    col_pick = one_hot(template_corner[1, 0], PATCH, section_a.shape[1], flip=True)
    row_pick = one_hot(template_corner[0, 0], PATCH, section_a.shape[0])
    by_col = jnp.einsum("krc,ac->kra", col_pick, section_a, preferred_element_type=f32)
    tflipped = jnp.einsum(
        "kra,kia->kri", by_col.astype(jnp.bfloat16), row_pick, preferred_element_type=f32
    ).astype(jnp.bfloat16)
    outgoing = jnp.einsum(
        "ks,kri->sri", owner_picker.astype(jnp.bfloat16), tflipped, preferred_element_type=f32
    ).astype(jnp.bfloat16)

    n_tx = lax.axis_size("tx")
    n_ty = lax.axis_size("ty")
    me_x = lax.axis_index("tx")
    tx_ids = jnp.arange(n_tx, dtype=jnp.int32)
    to_left = (tx_ids == me_x - 1)[:, None]
    to_right = (tx_ids == me_x + 1)[:, None]

    def side_payload(left, right):
        lf = left.reshape(1, -1)
        rf = right.reshape(1, -1)
        return jnp.where(to_left, lf, jnp.where(to_right, rf, jnp.zeros_like(lf)))

    def side_arrivals(got, shape):
        left = lax.dynamic_index_in_dim(got, jnp.maximum(me_x - 1, 0), axis=0, keepdims=False)
        right = lax.dynamic_index_in_dim(got, jnp.minimum(me_x + 1, n_tx - 1), axis=0, keepdims=False)
        left = jnp.where(me_x >= 1, left, jnp.zeros_like(left)).reshape(shape)
        right = jnp.where(me_x + 1 < n_tx, right, jnp.zeros_like(right)).reshape(shape)
        return left, right

    def rows_exchange(cells, width):
        count = n_ty
        height = cells.shape[-2]
        head = cells[..., 0:width, :]
        tail = cells[..., height - width : height, :]
        above = lax.ppermute(tail, "ty", [(i, i + 1) for i in range(count - 1)])
        below = lax.ppermute(head, "ty", [(i + 1, i) for i in range(count - 1)])
        return above, below

    node_rows, node_cols = node_mask.shape
    centre_y = (window_corner[0, 0] + PATCH // 2) * node_rows // tile_size
    centre_x = (window_corner[1, 0] + PATCH // 2) * node_cols // tile_size
    attach = (centre_y[:, None, None] == jnp.arange(node_rows, dtype=jnp.int32)[None, :, None]) & (
        centre_x[:, None, None] == jnp.arange(node_cols, dtype=jnp.int32)[None, None, :]
    )
    count = jnp.sum(attach.astype(f32), axis=0)
    mask = node_mask.astype(f32)
    w = ITERS_R
    arrived = lax.all_to_all(outgoing, "tx", split_axis=0, concat_axis=0, tiled=True)
    b_wide = halo(section_b, RADIUS)

    wrow_pick = one_hot(window_corner[0, 0], WIN, b_wide.shape[0])
    wcol_pick = one_hot(window_corner[1, 0], WIN, b_wide.shape[1])
    by_row = jnp.einsum("mra,ac->mrc", wrow_pick, b_wide, preferred_element_type=f32)
    windows = jnp.einsum(
        "mrc,msc->mrs", by_row.astype(jnp.bfloat16), wcol_pick, preferred_element_type=f32
    ).astype(jnp.bfloat16)
    matched = jnp.einsum(
        "ms,sri->mri", source_picker.astype(jnp.bfloat16), arrived, preferred_element_type=f32
    ).astype(jnp.bfloat16)

    flows = flows_of(matched, windows)
    source_flow = -flows

    target = jnp.sum(jnp.where(attach[None], source_flow[:, :, None, None], 0.0), axis=1)
    fields = jnp.concatenate([target, count[None], mask[None]], axis=0)
    returned = jnp.sum(jnp.where(source_picker[None], flows[:, :, None], 0.0), axis=1)
    lane = 128
    sides = side_payload(fields[:, :, 0:w], fields[:, :, node_cols - w :])
    flows_out = returned.reshape(2, n_tx, CAP).transpose(1, 0, 2).reshape(n_tx, -1)
    side_len = sides.shape[1]
    chunk = -(-(side_len + flows_out.shape[1]) // lane) * lane
    back = jnp.concatenate(
        [sides, flows_out, jnp.zeros((n_tx, chunk - side_len - flows_out.shape[1]), f32)], axis=1
    ).reshape(n_tx, chunk // lane, lane)
    came = lax.all_to_all(back, "tx", split_axis=0, concat_axis=0, tiled=True).reshape(n_tx, chunk)
    landed = came[:, side_len : side_len + 2 * CAP].reshape(n_tx, 2, CAP).transpose(1, 0, 2).reshape(2, -1)
    owner_flow = jnp.sum(jnp.where(owner_picker[None], landed[:, None, :], 0.0), axis=2)
    f_left, f_right = side_arrivals(came[:, 0:side_len], (fields.shape[0], node_rows, w))
    fields_tx = jnp.concatenate([f_left, fields, f_right], axis=2)
    f_above, f_below = rows_exchange(fields_tx, w)
    wide = jnp.concatenate([f_above, fields_tx, f_below], axis=1)

    displace = jnp.zeros((2,) + wide.shape[1:], f32)
    for sweep in range(ITERS_R):
        lo_m, hi_m = sweep, wide.shape[1] - sweep
        lo_t, hi_t = sweep + 1, wide.shape[1] - sweep - 1
        displace = relax_sweep(
            displace,
            wide[3, lo_m:hi_m, lo_m:hi_m],
            wide[0:2, lo_t:hi_t, lo_t:hi_t],
            wide[2, lo_t:hi_t, lo_t:hi_t],
        )
    return (owner_flow[:, None, :], source_flow[:, None, :], displace)


def solution(mesh):
    placed = (
        P("ty", "tx"),
        P("ty", "tx"),
        P(None, "ty", "tx"),
        P("ty", "tx"),
        P(None, "ty", "tx"),
        P("ty", "tx"),
        P("ty", "tx"),
    )
    return jax.shard_map(
        shards,
        mesh=mesh,
        in_specs=placed,
        out_specs=(P(None, "ty", "tx"), P(None, "ty", "tx"), P(None, "ty", "tx")),
        check_vma=False,
    )
```

```python
import jax
import jax.numpy as jnp
from jax import lax
from jax.sharding import PartitionSpec as P
from jax.experimental import pallas as pl
from jax.experimental.pallas import tpu as pltpu

PATCH = 128
SHIFTS = 65
RADIUS = 32
WIN = 192
CAP = 2
ITERS_R = 3


SHARPNESS = 256.0
SPRING_RATE = 0.25
FLOW_RATE = 0.5
FLOW_UNIT = 8.0
EPSILON = 1e-05

HALF = PATCH // 2


def flow_kernel(tf_ref, w_ref, out_ref, wlo, whi, corr):
    wf = w_ref[0].astype(jnp.float32)
    wlo[...] = wf[:, 0:PATCH]
    whi[...] = jnp.zeros(whi.shape, jnp.float32)
    whi[:, 0:WIN - HALF] = wf[:, HALF:WIN]
    tfv = tf_ref[0].astype(jnp.float32)
    t_cat = jnp.concatenate([tf_ref[0, 0:HALF, :], tf_ref[0, HALF:PATCH, :]], axis=1)
    corr[...] = jnp.zeros(corr.shape, jnp.float32)

    def step(dy, carry):
        w_cat = jnp.concatenate(
            [whi[pl.ds(dy, PATCH), :], wlo[pl.ds(dy, PATCH), :]], axis=0
        ).astype(jnp.bfloat16)
        m = jnp.dot(t_cat, w_cat, preferred_element_type=jnp.float32)
        r = pltpu.roll(m, 0, axis=1, stride=1, stride_axis=0)
        corr[pl.ds(dy, 1), :] = jnp.sum(r, axis=0, keepdims=True)
        return carry

    lax.fori_loop(0, SHIFTS, step, 0, unroll=SHIFTS)

    c = corr[...]
    rows = lax.broadcasted_iota(jnp.int32, c.shape, 0)
    lanes = lax.broadcasted_iota(jnp.int32, c.shape, 1)
    valid = (rows < SHIFTS) & (lanes >= HALF - 1)
    e_t = jnp.sum(tfv * tfv, keepdims=True) / float(PATCH * PATCH)
    e_w = jnp.sum(wf * wf, keepdims=True) / float(WIN * WIN)
    denom = float(PATCH * PATCH) * jnp.sqrt((e_t + EPSILON) * (e_w + EPSILON))
    scores = SHARPNESS * c / denom
    scores = jnp.where(valid, scores, -jnp.inf)
    mx = jnp.max(scores, keepdims=True)
    e = jnp.where(valid, jnp.exp(scores - mx), 0.0)
    w = e / jnp.sum(e, keepdims=True)
    sy = (rows - RADIUS).astype(jnp.float32)
    sx = (lanes - (HALF - 1) - RADIUS).astype(jnp.float32)
    fy = jnp.sum(w * sy, keepdims=True) / FLOW_UNIT
    fx = jnp.sum(w * sx, keepdims=True) / FLOW_UNIT
    orow = lax.broadcasted_iota(jnp.int32, (8, 128), 0)
    out_ref[0] = jnp.where(orow == 0, fy, jnp.where(orow == 1, fx, 0.0))

def flows_of(tflipped, windows):
    n = tflipped.shape[0]
    out = pl.pallas_call(
        flow_kernel,
        grid=(n,),
        in_specs=[pl.BlockSpec((1, PATCH, PATCH), lambda i: (i, 0, 0)),
                  pl.BlockSpec((1, WIN, WIN), lambda i: (i, 0, 0))],
        out_specs=pl.BlockSpec((1, 8, 128), lambda i: (i, 0, 0)),
        out_shape=jax.ShapeDtypeStruct((n, 8, 128), jnp.float32),
        scratch_shapes=[pltpu.VMEM((WIN, PATCH), jnp.float32),
                        pltpu.VMEM((WIN, PATCH), jnp.float32),
                        pltpu.VMEM((72, PATCH), jnp.float32)],
    )(tflipped, windows)
    return out[:, 0:2, 0].T


def halo(cells, width):
    n_ty = lax.axis_size("ty")
    n_tx = lax.axis_size("tx")
    height, breadth = cells.shape[-2], cells.shape[-1]
    pieces = {}
    for dy in (-1, 0, 1):
        for dx in (-1, 0, 1):
            if dy == 0 and dx == 0:
                pieces[(dy, dx)] = cells
                continue
            rows = {-1: (height - width, height), 0: (0, height), 1: (0, width)}[dy]
            cols = {-1: (breadth - width, breadth), 0: (0, breadth), 1: (0, width)}[dx]
            part = cells[..., rows[0] : rows[1], cols[0] : cols[1]]
            pairs = []
            for i in range(n_ty):
                for j in range(n_tx):
                    si, sj = i + dy, j + dx
                    if 0 <= si < n_ty and 0 <= sj < n_tx:
                        pairs.append((si * n_tx + sj, i * n_tx + j))
            pieces[(dy, dx)] = lax.ppermute(part, ("ty", "tx"), pairs)
    bands = [
        jnp.concatenate([pieces[(dy, -1)], pieces[(dy, 0)], pieces[(dy, 1)]], axis=-1)
        for dy in (-1, 0, 1)
    ]
    return jnp.concatenate(bands, axis=-2)


def relax_sweep(padded, mask_pad, target, count):
    centre = padded[:, 1:-1, 1:-1]
    mask_c = mask_pad[1:-1, 1:-1]
    height = centre.shape[1]
    width = centre.shape[2]
    spring = jnp.zeros_like(centre)
    for row_step, col_step in ((0, 1), (2, 1), (1, 0), (1, 2)):
        nearby = padded[:, row_step : row_step + height, col_step : col_step + width]
        mask_n = mask_pad[row_step : row_step + height, col_step : col_step + width]
        spring = spring + mask_c * mask_n * (nearby - centre)
    return centre + SPRING_RATE * spring + FLOW_RATE * (target - count * centre)


def one_hot(starts, size, extent, flip=False):
    offs = jnp.arange(size, dtype=jnp.int32)
    if flip:
        offs = size - 1 - offs
    want = starts[:, None, None] + offs[None, :, None]
    return (want == jnp.arange(extent, dtype=jnp.int32)[None, None, :]).astype(jnp.bfloat16)


def shards(
    section_a, section_b, template_corner, template_slot, window_corner, window_slot, node_mask
):
    tile_size = section_a.shape[0]
    slot_count = lax.axis_size("tx") * CAP
    slot_ids = jnp.arange(slot_count, dtype=jnp.int32)
    owner_picker = template_slot[0][:, None] == slot_ids[None, :]
    source_picker = window_slot[0][:, None] == slot_ids[None, :]
    f32 = jnp.float32

    col_pick = one_hot(template_corner[1, 0], PATCH, section_a.shape[1], flip=True)
    row_pick = one_hot(template_corner[0, 0], PATCH, section_a.shape[0])
    by_col = jnp.einsum("krc,ac->kra", col_pick, section_a, preferred_element_type=f32)
    tflipped = jnp.einsum(
        "kra,kia->kri", by_col.astype(jnp.bfloat16), row_pick, preferred_element_type=f32
    ).astype(jnp.bfloat16)
    outgoing = jnp.einsum(
        "ks,kri->sri", owner_picker.astype(jnp.bfloat16), tflipped, preferred_element_type=f32
    ).astype(jnp.bfloat16)

    n_tx = lax.axis_size("tx")
    n_ty = lax.axis_size("ty")
    me_x = lax.axis_index("tx")
    tx_ids = jnp.arange(n_tx, dtype=jnp.int32)
    to_left = (tx_ids == me_x - 1)[:, None]
    to_right = (tx_ids == me_x + 1)[:, None]

    def side_payload(left, right):
        lf = left.reshape(1, -1)
        rf = right.reshape(1, -1)
        return jnp.where(to_left, lf, jnp.where(to_right, rf, jnp.zeros_like(lf)))

    def side_arrivals(got, shape):
        left = lax.dynamic_index_in_dim(got, jnp.maximum(me_x - 1, 0), axis=0, keepdims=False)
        right = lax.dynamic_index_in_dim(got, jnp.minimum(me_x + 1, n_tx - 1), axis=0, keepdims=False)
        left = jnp.where(me_x >= 1, left, jnp.zeros_like(left)).reshape(shape)
        right = jnp.where(me_x + 1 < n_tx, right, jnp.zeros_like(right)).reshape(shape)
        return left, right

    def rows_exchange(cells, width):
        count = n_ty
        height = cells.shape[-2]
        head = cells[..., 0:width, :]
        tail = cells[..., height - width : height, :]
        above = lax.ppermute(tail, "ty", [(i, i + 1) for i in range(count - 1)])
        below = lax.ppermute(head, "ty", [(i + 1, i) for i in range(count - 1)])
        return above, below

    node_rows, node_cols = node_mask.shape
    centre_y = (window_corner[0, 0] + PATCH // 2) * node_rows // tile_size
    centre_x = (window_corner[1, 0] + PATCH // 2) * node_cols // tile_size
    attach = (centre_y[:, None, None] == jnp.arange(node_rows, dtype=jnp.int32)[None, :, None]) & (
        centre_x[:, None, None] == jnp.arange(node_cols, dtype=jnp.int32)[None, None, :]
    )
    count = jnp.sum(attach.astype(f32), axis=0)
    mask = node_mask.astype(f32)
    w = ITERS_R
    arrived = lax.all_to_all(outgoing, "tx", split_axis=0, concat_axis=0, tiled=True)
    b_wide = halo(section_b, RADIUS)

    wrow_pick = one_hot(window_corner[0, 0], WIN, b_wide.shape[0])
    wcol_pick = one_hot(window_corner[1, 0], WIN, b_wide.shape[1])
    by_row = jnp.einsum("mra,ac->mrc", wrow_pick, b_wide, preferred_element_type=f32)
    windows = jnp.einsum(
        "mrc,msc->mrs", by_row.astype(jnp.bfloat16), wcol_pick, preferred_element_type=f32
    ).astype(jnp.bfloat16)
    matched = jnp.einsum(
        "ms,sri->mri", source_picker.astype(jnp.bfloat16), arrived, preferred_element_type=f32
    ).astype(jnp.bfloat16)

    flows = flows_of(matched, windows)
    source_flow = -flows

    target = jnp.sum(jnp.where(attach[None], source_flow[:, :, None, None], 0.0), axis=1)
    fields = jnp.concatenate([target, count[None], mask[None]], axis=0)
    returned = jnp.sum(jnp.where(source_picker[None], flows[:, :, None], 0.0), axis=1)
    lane = 128
    sides = side_payload(fields[:, :, 0:w], fields[:, :, node_cols - w :])
    flows_out = returned.reshape(2, n_tx, CAP).transpose(1, 0, 2).reshape(n_tx, -1)
    side_len = sides.shape[1]
    chunk = -(-(side_len + flows_out.shape[1]) // lane) * lane
    back = jnp.concatenate(
        [sides, flows_out, jnp.zeros((n_tx, chunk - side_len - flows_out.shape[1]), f32)], axis=1
    ).reshape(n_tx, chunk // lane, lane)
    came = lax.all_to_all(back, "tx", split_axis=0, concat_axis=0, tiled=True).reshape(n_tx, chunk)
    landed = came[:, side_len : side_len + 2 * CAP].reshape(n_tx, 2, CAP).transpose(1, 0, 2).reshape(2, -1)
    owner_flow = jnp.sum(jnp.where(owner_picker[None], landed[:, None, :], 0.0), axis=2)
    f_left, f_right = side_arrivals(came[:, 0:side_len], (fields.shape[0], node_rows, w))
    fields_tx = jnp.concatenate([f_left, fields, f_right], axis=2)
    f_above, f_below = rows_exchange(fields_tx, w)
    wide = jnp.concatenate([f_above, fields_tx, f_below], axis=1)

    displace = jnp.zeros((2,) + wide.shape[1:], f32)
    for sweep in range(ITERS_R):
        lo_m, hi_m = sweep, wide.shape[1] - sweep
        lo_t, hi_t = sweep + 1, wide.shape[1] - sweep - 1
        displace = relax_sweep(
            displace,
            wide[3, lo_m:hi_m, lo_m:hi_m],
            wide[0:2, lo_t:hi_t, lo_t:hi_t],
            wide[2, lo_t:hi_t, lo_t:hi_t],
        )
    return (owner_flow[:, None, :], source_flow[:, None, :], displace)


def solution(mesh):
    placed = (
        P("ty", "tx"),
        P("ty", "tx"),
        P(None, "ty", "tx"),
        P("ty", "tx"),
        P(None, "ty", "tx"),
        P("ty", "tx"),
        P("ty", "tx"),
    )
    return jax.shard_map(
        shards,
        mesh=mesh,
        in_specs=placed,
        out_specs=(P(None, "ty", "tx"), P(None, "ty", "tx"), P(None, "ty", "tx")),
        check_vma=False,
    )
```

```python
import jax
import jax.numpy as jnp
from jax import lax
from jax.sharding import PartitionSpec as P
from jax.experimental import pallas as pl
from jax.experimental.pallas import tpu as pltpu

PATCH = 128
SHIFTS = 65
RADIUS = 32
WIN = 192
CAP = 2
ITERS_R = 3


SHARPNESS = 256.0
SPRING_RATE = 0.25
FLOW_RATE = 0.5
FLOW_UNIT = 8.0
EPSILON = 1e-05

HALF = PATCH // 2


def flow_kernel(tf_ref, w_ref, out_ref, wlo, whi, corr):
    wf = w_ref[0].astype(jnp.float32)
    wlo[...] = wf[:, 0:PATCH]
    whi[...] = jnp.zeros(whi.shape, jnp.float32)
    whi[:, 0:WIN - HALF] = wf[:, HALF:WIN]
    tfv = tf_ref[0].astype(jnp.float32)
    t_cat = jnp.concatenate([tf_ref[0, 0:HALF, :], tf_ref[0, HALF:PATCH, :]], axis=1)
    corr[...] = jnp.zeros(corr.shape, jnp.float32)

    def step(dy, carry):
        w_cat = jnp.concatenate(
            [whi[pl.ds(dy, PATCH), :], wlo[pl.ds(dy, PATCH), :]], axis=0
        ).astype(jnp.bfloat16)
        m = jnp.dot(t_cat, w_cat, preferred_element_type=jnp.float32)
        r = pltpu.roll(m, 0, axis=1, stride=1, stride_axis=0)
        corr[pl.ds(dy, 1), :] = jnp.sum(r, axis=0, keepdims=True)
        return carry

    lax.fori_loop(0, SHIFTS, step, 0, unroll=SHIFTS)

    c = corr[...]
    rows = lax.broadcasted_iota(jnp.int32, c.shape, 0)
    lanes = lax.broadcasted_iota(jnp.int32, c.shape, 1)
    valid = (rows < SHIFTS) & (lanes >= HALF - 1)
    e_t = jnp.sum(tfv * tfv, keepdims=True) / float(PATCH * PATCH)
    e_w = jnp.sum(wf * wf, keepdims=True) / float(WIN * WIN)
    denom = float(PATCH * PATCH) * jnp.sqrt((e_t + EPSILON) * (e_w + EPSILON))
    scores = SHARPNESS * c / denom
    scores = jnp.where(valid, scores, -jnp.inf)
    mx = jnp.max(scores, keepdims=True)
    e = jnp.where(valid, jnp.exp(scores - mx), 0.0)
    w = e / jnp.sum(e, keepdims=True)
    sy = (rows - RADIUS).astype(jnp.float32)
    sx = (lanes - (HALF - 1) - RADIUS).astype(jnp.float32)
    fy = jnp.sum(w * sy, keepdims=True) / FLOW_UNIT
    fx = jnp.sum(w * sx, keepdims=True) / FLOW_UNIT
    orow = lax.broadcasted_iota(jnp.int32, (8, 128), 0)
    out_ref[0] = jnp.where(orow == 0, fy, jnp.where(orow == 1, fx, 0.0))

def flows_of(tflipped, windows):
    n = tflipped.shape[0]
    out = pl.pallas_call(
        flow_kernel,
        grid=(n,),
        in_specs=[pl.BlockSpec((1, PATCH, PATCH), lambda i: (i, 0, 0)),
                  pl.BlockSpec((1, WIN, WIN), lambda i: (i, 0, 0))],
        out_specs=pl.BlockSpec((1, 8, 128), lambda i: (i, 0, 0)),
        out_shape=jax.ShapeDtypeStruct((n, 8, 128), jnp.float32),
        scratch_shapes=[pltpu.VMEM((WIN, PATCH), jnp.float32),
                        pltpu.VMEM((WIN, PATCH), jnp.float32),
                        pltpu.VMEM((72, PATCH), jnp.float32)],
    )(tflipped, windows)
    return out[:, 0:2, 0].T


def padded_2(cells, sides, width):
    for axis, dim in sides:
        count = lax.axis_size(axis)
        ends = count - 1
        head = lax.slice_in_dim(cells, 0, width, axis=dim)
        tail = lax.slice_in_dim(cells, cells.shape[dim] - width, cells.shape[dim], axis=dim)
        cells = jnp.concatenate(
            [
                lax.ppermute(tail, axis, [(i, (i + 1) % count) for i in range(ends)]),
                cells,
                lax.ppermute(head, axis, [((i + 1) % count, i) for i in range(ends)]),
            ],
            axis=dim,
        )
    return cells


def halo(cells, width):
    n_ty = lax.axis_size("ty")
    n_tx = lax.axis_size("tx")
    height, breadth = cells.shape[-2], cells.shape[-1]
    pieces = {}
    for dy in (-1, 0, 1):
        for dx in (-1, 0, 1):
            if dy == 0 and dx == 0:
                pieces[(dy, dx)] = cells
                continue
            rows = {-1: (height - width, height), 0: (0, height), 1: (0, width)}[dy]
            cols = {-1: (breadth - width, breadth), 0: (0, breadth), 1: (0, width)}[dx]
            part = cells[..., rows[0] : rows[1], cols[0] : cols[1]]
            pairs = []
            for i in range(n_ty):
                for j in range(n_tx):
                    si, sj = i + dy, j + dx
                    if 0 <= si < n_ty and 0 <= sj < n_tx:
                        pairs.append((si * n_tx + sj, i * n_tx + j))
            pieces[(dy, dx)] = lax.ppermute(part, ("ty", "tx"), pairs)
    bands = [
        jnp.concatenate([pieces[(dy, -1)], pieces[(dy, 0)], pieces[(dy, 1)]], axis=-1)
        for dy in (-1, 0, 1)
    ]
    return jnp.concatenate(bands, axis=-2)


def relax_sweep(padded, mask_pad, target, count):
    centre = padded[:, 1:-1, 1:-1]
    mask_c = mask_pad[1:-1, 1:-1]
    height = centre.shape[1]
    width = centre.shape[2]
    spring = jnp.zeros_like(centre)
    for row_step, col_step in ((0, 1), (2, 1), (1, 0), (1, 2)):
        nearby = padded[:, row_step : row_step + height, col_step : col_step + width]
        mask_n = mask_pad[row_step : row_step + height, col_step : col_step + width]
        spring = spring + mask_c * mask_n * (nearby - centre)
    return centre + SPRING_RATE * spring + FLOW_RATE * (target - count * centre)


def one_hot(starts, size, extent, flip=False):
    offs = jnp.arange(size, dtype=jnp.int32)
    if flip:
        offs = size - 1 - offs
    want = starts[:, None, None] + offs[None, :, None]
    return (want == jnp.arange(extent, dtype=jnp.int32)[None, None, :]).astype(jnp.bfloat16)


def shards(
    section_a, section_b, template_corner, template_slot, window_corner, window_slot, node_mask
):
    tile_size = section_a.shape[0]
    slot_count = lax.axis_size("tx") * CAP
    slot_ids = jnp.arange(slot_count, dtype=jnp.int32)
    owner_picker = template_slot[0][:, None] == slot_ids[None, :]
    source_picker = window_slot[0][:, None] == slot_ids[None, :]
    f32 = jnp.float32

    col_pick = one_hot(template_corner[1, 0], PATCH, section_a.shape[1], flip=True)
    row_pick = one_hot(template_corner[0, 0], PATCH, section_a.shape[0])
    by_col = jnp.einsum("krc,ac->kra", col_pick, section_a, preferred_element_type=f32)
    tflipped = jnp.einsum(
        "kra,kia->kri", by_col.astype(jnp.bfloat16), row_pick, preferred_element_type=f32
    ).astype(jnp.bfloat16)
    outgoing = jnp.einsum(
        "ks,kri->sri", owner_picker.astype(jnp.bfloat16), tflipped, preferred_element_type=f32
    ).astype(jnp.bfloat16)

    n_tx = lax.axis_size("tx")
    n_ty = lax.axis_size("ty")
    me_x = lax.axis_index("tx")
    tx_ids = jnp.arange(n_tx, dtype=jnp.int32)
    to_left = (tx_ids == me_x - 1)[:, None]
    to_right = (tx_ids == me_x + 1)[:, None]

    def side_payload(left, right):
        lf = left.reshape(1, -1)
        rf = right.reshape(1, -1)
        return jnp.where(to_left, lf, jnp.where(to_right, rf, jnp.zeros_like(lf)))

    def side_arrivals(got, shape):
        left = lax.dynamic_index_in_dim(got, jnp.maximum(me_x - 1, 0), axis=0, keepdims=False)
        right = lax.dynamic_index_in_dim(got, jnp.minimum(me_x + 1, n_tx - 1), axis=0, keepdims=False)
        left = jnp.where(me_x >= 1, left, jnp.zeros_like(left)).reshape(shape)
        right = jnp.where(me_x + 1 < n_tx, right, jnp.zeros_like(right)).reshape(shape)
        return left, right

    def rows_exchange(cells, width):
        count = n_ty
        height = cells.shape[-2]
        head = cells[..., 0:width, :]
        tail = cells[..., height - width : height, :]
        above = lax.ppermute(tail, "ty", [(i, i + 1) for i in range(count - 1)])
        below = lax.ppermute(head, "ty", [(i + 1, i) for i in range(count - 1)])
        return above, below

    node_rows, node_cols = node_mask.shape
    centre_y = (window_corner[0, 0] + PATCH // 2) * node_rows // tile_size
    centre_x = (window_corner[1, 0] + PATCH // 2) * node_cols // tile_size
    attach = (centre_y[:, None, None] == jnp.arange(node_rows, dtype=jnp.int32)[None, :, None]) & (
        centre_x[:, None, None] == jnp.arange(node_cols, dtype=jnp.int32)[None, None, :]
    )
    count = jnp.sum(attach.astype(f32), axis=0)
    mask = node_mask.astype(f32)
    w = ITERS_R
    arrived = lax.all_to_all(outgoing, "tx", split_axis=0, concat_axis=0, tiled=True)
    b_wide = padded_2(section_b, (("ty", 0), ("tx", 1)), RADIUS)

    wrow_pick = one_hot(window_corner[0, 0], WIN, b_wide.shape[0])
    wcol_pick = one_hot(window_corner[1, 0], WIN, b_wide.shape[1])
    by_row = jnp.einsum("mra,ac->mrc", wrow_pick, b_wide, preferred_element_type=f32)
    windows = jnp.einsum(
        "mrc,msc->mrs", by_row.astype(jnp.bfloat16), wcol_pick, preferred_element_type=f32
    ).astype(jnp.bfloat16)
    matched = jnp.einsum(
        "ms,sri->mri", source_picker.astype(jnp.bfloat16), arrived, preferred_element_type=f32
    ).astype(jnp.bfloat16)

    flows = flows_of(matched, windows)
    source_flow = -flows

    target = jnp.sum(jnp.where(attach[None], source_flow[:, :, None, None], 0.0), axis=1)
    fields = jnp.concatenate([target, count[None], mask[None]], axis=0)
    returned = jnp.sum(jnp.where(source_picker[None], flows[:, :, None], 0.0), axis=1)
    lane = 128
    sides = side_payload(fields[:, :, 0:w], fields[:, :, node_cols - w :])
    flows_out = returned.reshape(2, n_tx, CAP).transpose(1, 0, 2).reshape(n_tx, -1)
    side_len = sides.shape[1]
    chunk = -(-(side_len + flows_out.shape[1]) // lane) * lane
    back = jnp.concatenate(
        [sides, flows_out, jnp.zeros((n_tx, chunk - side_len - flows_out.shape[1]), f32)], axis=1
    ).reshape(n_tx, chunk // lane, lane)
    came = lax.all_to_all(back, "tx", split_axis=0, concat_axis=0, tiled=True).reshape(n_tx, chunk)
    landed = came[:, side_len : side_len + 2 * CAP].reshape(n_tx, 2, CAP).transpose(1, 0, 2).reshape(2, -1)
    owner_flow = jnp.sum(jnp.where(owner_picker[None], landed[:, None, :], 0.0), axis=2)
    f_left, f_right = side_arrivals(came[:, 0:side_len], (fields.shape[0], node_rows, w))
    fields_tx = jnp.concatenate([f_left, fields, f_right], axis=2)
    f_above, f_below = rows_exchange(fields_tx, w)
    wide = jnp.concatenate([f_above, fields_tx, f_below], axis=1)

    displace = jnp.zeros((2,) + wide.shape[1:], f32)
    for sweep in range(ITERS_R):
        lo_m, hi_m = sweep, wide.shape[1] - sweep
        lo_t, hi_t = sweep + 1, wide.shape[1] - sweep - 1
        displace = relax_sweep(
            displace,
            wide[3, lo_m:hi_m, lo_m:hi_m],
            wide[0:2, lo_t:hi_t, lo_t:hi_t],
            wide[2, lo_t:hi_t, lo_t:hi_t],
        )
    return (owner_flow[:, None, :], source_flow[:, None, :], displace)


def solution(mesh):
    placed = (
        P("ty", "tx"),
        P("ty", "tx"),
        P(None, "ty", "tx"),
        P("ty", "tx"),
        P(None, "ty", "tx"),
        P("ty", "tx"),
        P("ty", "tx"),
    )
    return jax.shard_map(
        shards,
        mesh=mesh,
        in_specs=placed,
        out_specs=(P(None, "ty", "tx"), P(None, "ty", "tx"), P(None, "ty", "tx")),
        check_vma=False,
    )
```

```python
import jax
import jax.numpy as jnp
from jax import lax
from jax.sharding import PartitionSpec as P
from jax.experimental import pallas as pl
from jax.experimental.pallas import tpu as pltpu

PATCH = 128
SHIFTS = 65
RADIUS = 32
WIN = 192
CAP = 2
ITERS_R = 3


SHARPNESS = 256.0
SPRING_RATE = 0.25
FLOW_RATE = 0.5
FLOW_UNIT = 8.0
EPSILON = 1e-05

HALF = PATCH // 2


def flow_kernel(tf_ref, w_ref, out_ref, wlo, whi, corr):
    wf = w_ref[0].astype(jnp.float32)
    wlo[...] = wf[:, 0:PATCH]
    whi[...] = jnp.zeros(whi.shape, jnp.float32)
    whi[:, 0:WIN - HALF] = wf[:, HALF:WIN]
    tfv = tf_ref[0].astype(jnp.float32)
    t_cat = jnp.concatenate([tf_ref[0, 0:HALF, :], tf_ref[0, HALF:PATCH, :]], axis=1)
    corr[...] = jnp.zeros(corr.shape, jnp.float32)

    def step(dy, carry):
        w_cat = jnp.concatenate(
            [whi[pl.ds(dy, PATCH), :], wlo[pl.ds(dy, PATCH), :]], axis=0
        ).astype(jnp.bfloat16)
        m = jnp.dot(t_cat, w_cat, preferred_element_type=jnp.float32)
        r = pltpu.roll(m, 0, axis=1, stride=1, stride_axis=0)
        corr[pl.ds(dy, 1), :] = jnp.sum(r, axis=0, keepdims=True)
        return carry

    lax.fori_loop(0, SHIFTS, step, 0, unroll=SHIFTS)

    c = corr[...]
    rows = lax.broadcasted_iota(jnp.int32, c.shape, 0)
    lanes = lax.broadcasted_iota(jnp.int32, c.shape, 1)
    valid = (rows < SHIFTS) & (lanes >= HALF - 1)
    e_t = jnp.sum(tfv * tfv, keepdims=True) / float(PATCH * PATCH)
    e_w = jnp.sum(wf * wf, keepdims=True) / float(WIN * WIN)
    denom = float(PATCH * PATCH) * jnp.sqrt((e_t + EPSILON) * (e_w + EPSILON))
    scores = SHARPNESS * c / denom
    scores = jnp.where(valid, scores, -jnp.inf)
    mx = jnp.max(scores, keepdims=True)
    e = jnp.where(valid, jnp.exp(scores - mx), 0.0)
    w = e / jnp.sum(e, keepdims=True)
    sy = (rows - RADIUS).astype(jnp.float32)
    sx = (lanes - (HALF - 1) - RADIUS).astype(jnp.float32)
    fy = jnp.sum(w * sy, keepdims=True) / FLOW_UNIT
    fx = jnp.sum(w * sx, keepdims=True) / FLOW_UNIT
    orow = lax.broadcasted_iota(jnp.int32, (8, 128), 0)
    out_ref[0] = jnp.where(orow == 0, fy, jnp.where(orow == 1, fx, 0.0))


def flows_of(tflipped, windows):
    n = tflipped.shape[0]
    out = pl.pallas_call(
        flow_kernel,
        grid=(n,),
        in_specs=[pl.BlockSpec((1, PATCH, PATCH), lambda i: (i, 0, 0)),
                  pl.BlockSpec((1, WIN, WIN), lambda i: (i, 0, 0))],
        out_specs=pl.BlockSpec((1, 8, 128), lambda i: (i, 0, 0)),
        out_shape=jax.ShapeDtypeStruct((n, 8, 128), jnp.float32),
        scratch_shapes=[pltpu.VMEM((WIN, PATCH), jnp.float32),
                        pltpu.VMEM((WIN, PATCH), jnp.float32),
                        pltpu.VMEM((72, PATCH), jnp.float32)],
    )(tflipped, windows)
    return out[:, 0:2, 0].T


def padded_2(cells, sides, width):
    for axis, dim in sides:
        count = lax.axis_size(axis)
        ends = count - 1
        head = lax.slice_in_dim(cells, 0, width, axis=dim)
        tail = lax.slice_in_dim(cells, cells.shape[dim] - width, cells.shape[dim], axis=dim)
        cells = jnp.concatenate(
            [
                lax.ppermute(tail, axis, [(i, (i + 1) % count) for i in range(ends)]),
                cells,
                lax.ppermute(head, axis, [((i + 1) % count, i) for i in range(ends)]),
            ],
            axis=dim,
        )
    return cells


def relax_sweep(padded, mask_pad, target, count):
    centre = padded[:, 1:-1, 1:-1]
    mask_c = mask_pad[1:-1, 1:-1]
    height = centre.shape[1]
    width = centre.shape[2]
    spring = jnp.zeros_like(centre)
    for row_step, col_step in ((0, 1), (2, 1), (1, 0), (1, 2)):
        nearby = padded[:, row_step : row_step + height, col_step : col_step + width]
        mask_n = mask_pad[row_step : row_step + height, col_step : col_step + width]
        spring = spring + mask_c * mask_n * (nearby - centre)
    return centre + SPRING_RATE * spring + FLOW_RATE * (target - count * centre)


def one_hot(starts, size, extent, flip=False):
    offs = jnp.arange(size, dtype=jnp.int32)
    if flip:
        offs = size - 1 - offs
    want = starts[:, None, None] + offs[None, :, None]
    return (want == jnp.arange(extent, dtype=jnp.int32)[None, None, :]).astype(jnp.bfloat16)


def shards(
    section_a, section_b, template_corner, template_slot, window_corner, window_slot, node_mask
):
    tile_size = section_a.shape[0]
    slot_count = lax.axis_size("tx") * CAP
    slot_ids = jnp.arange(slot_count, dtype=jnp.int32)
    owner_picker = template_slot[0][:, None] == slot_ids[None, :]
    source_picker = window_slot[0][:, None] == slot_ids[None, :]
    f32 = jnp.float32

    col_pick = one_hot(template_corner[1, 0], PATCH, section_a.shape[1], flip=True)
    row_pick = one_hot(template_corner[0, 0], PATCH, section_a.shape[0])
    by_col = jnp.einsum("krc,ac->kra", col_pick, section_a, preferred_element_type=f32)
    tflipped = jnp.einsum(
        "kra,kia->kri", by_col.astype(jnp.bfloat16), row_pick, preferred_element_type=f32
    ).astype(jnp.bfloat16)
    outgoing = jnp.einsum(
        "ks,kri->sri", owner_picker.astype(jnp.bfloat16), tflipped, preferred_element_type=f32
    ).astype(jnp.bfloat16)

    n_tx = lax.axis_size("tx")
    n_ty = lax.axis_size("ty")
    me_x = lax.axis_index("tx")
    tx_ids = jnp.arange(n_tx, dtype=jnp.int32)
    to_left = (tx_ids == me_x - 1)[:, None]
    to_right = (tx_ids == me_x + 1)[:, None]

    def side_payload(left, right):
        lf = left.reshape(1, -1)
        rf = right.reshape(1, -1)
        return jnp.where(to_left, lf, jnp.where(to_right, rf, jnp.zeros_like(lf)))

    def side_arrivals(got, shape):
        left = lax.dynamic_index_in_dim(got, jnp.maximum(me_x - 1, 0), axis=0, keepdims=False)
        right = lax.dynamic_index_in_dim(got, jnp.minimum(me_x + 1, n_tx - 1), axis=0, keepdims=False)
        left = jnp.where(me_x >= 1, left, jnp.zeros_like(left)).reshape(shape)
        right = jnp.where(me_x + 1 < n_tx, right, jnp.zeros_like(right)).reshape(shape)
        return left, right

    def rows_exchange(cells, width):
        count = n_ty
        height = cells.shape[-2]
        head = cells[..., 0:width, :]
        tail = cells[..., height - width : height, :]
        above = lax.ppermute(tail, "ty", [(i, i + 1) for i in range(count - 1)])
        below = lax.ppermute(head, "ty", [(i + 1, i) for i in range(count - 1)])
        return above, below

    node_rows, node_cols = node_mask.shape
    centre_y = (window_corner[0, 0] + PATCH // 2) * node_rows // tile_size
    centre_x = (window_corner[1, 0] + PATCH // 2) * node_cols // tile_size
    attach = (centre_y[:, None, None] == jnp.arange(node_rows, dtype=jnp.int32)[None, :, None]) & (
        centre_x[:, None, None] == jnp.arange(node_cols, dtype=jnp.int32)[None, None, :]
    )
    count = jnp.sum(attach.astype(f32), axis=0)
    mask = node_mask.astype(f32)
    w = ITERS_R
    arrived = lax.all_to_all(outgoing, "tx", split_axis=0, concat_axis=0, tiled=True)
    b_tall = padded_2(section_b, (("ty", 0),), RADIUS)
    b_wide = padded_2(b_tall, (("tx", 1),), RADIUS)

    wrow_pick = one_hot(window_corner[0, 0], WIN, b_wide.shape[0])
    wcol_pick = one_hot(window_corner[1, 0], WIN, b_wide.shape[1])
    by_row = jnp.einsum("mra,ac->mrc", wrow_pick, b_wide, preferred_element_type=f32)
    windows = jnp.einsum(
        "mrc,msc->mrs", by_row.astype(jnp.bfloat16), wcol_pick, preferred_element_type=f32
    ).astype(jnp.bfloat16)
    matched = jnp.einsum(
        "ms,sri->mri", source_picker.astype(jnp.bfloat16), arrived, preferred_element_type=f32
    ).astype(jnp.bfloat16)

    flows = flows_of(matched, windows)
    source_flow = -flows

    target = jnp.sum(jnp.where(attach[None], source_flow[:, :, None, None], 0.0), axis=1)
    fields = jnp.concatenate([target, count[None], mask[None]], axis=0)
    returned = jnp.sum(jnp.where(source_picker[None], flows[:, :, None], 0.0), axis=1)
    lane = 128
    sides = side_payload(fields[:, :, 0:w], fields[:, :, node_cols - w :])
    flows_out = returned.reshape(2, n_tx, CAP).transpose(1, 0, 2).reshape(n_tx, -1)
    side_len = sides.shape[1]
    chunk = -(-(side_len + flows_out.shape[1]) // lane) * lane
    back = jnp.concatenate(
        [sides, flows_out, jnp.zeros((n_tx, chunk - side_len - flows_out.shape[1]), f32)], axis=1
    ).reshape(n_tx, chunk // lane, lane)
    came = lax.all_to_all(back, "tx", split_axis=0, concat_axis=0, tiled=True).reshape(n_tx, chunk)
    landed = came[:, side_len : side_len + 2 * CAP].reshape(n_tx, 2, CAP).transpose(1, 0, 2).reshape(2, -1)
    owner_flow = jnp.sum(jnp.where(owner_picker[None], landed[:, None, :], 0.0), axis=2)
    f_left, f_right = side_arrivals(came[:, 0:side_len], (fields.shape[0], node_rows, w))
    fields_tx = jnp.concatenate([f_left, fields, f_right], axis=2)
    f_above, f_below = rows_exchange(fields_tx, w)
    wide = jnp.concatenate([f_above, fields_tx, f_below], axis=1)

    displace = jnp.zeros((2,) + wide.shape[1:], f32)
    for sweep in range(ITERS_R):
        lo_m, hi_m = sweep, wide.shape[1] - sweep
        lo_t, hi_t = sweep + 1, wide.shape[1] - sweep - 1
        displace = relax_sweep(
            displace,
            wide[3, lo_m:hi_m, lo_m:hi_m],
            wide[0:2, lo_t:hi_t, lo_t:hi_t],
            wide[2, lo_t:hi_t, lo_t:hi_t],
        )
    return (owner_flow[:, None, :], source_flow[:, None, :], displace)


def solution(mesh):
    placed = (
        P("ty", "tx"),
        P("ty", "tx"),
        P(None, "ty", "tx"),
        P("ty", "tx"),
        P(None, "ty", "tx"),
        P("ty", "tx"),
        P("ty", "tx"),
    )
    return jax.shard_map(
        shards,
        mesh=mesh,
        in_specs=placed,
        out_specs=(P(None, "ty", "tx"), P(None, "ty", "tx"), P(None, "ty", "tx")),
        check_vma=False,
    )
```

```python
import jax
import jax.numpy as jnp
from jax import lax
from jax.sharding import PartitionSpec as P
from jax.experimental import pallas as pl
from jax.experimental.pallas import tpu as pltpu

PATCH = 128
SHIFTS = 65
RADIUS = 32
WIN = 192
CAP = 2
ITERS_R = 3


SHARPNESS = 256.0
SPRING_RATE = 0.25
FLOW_RATE = 0.5
FLOW_UNIT = 8.0
EPSILON = 1e-05

HALF = PATCH // 2


def flow_kernel(tf_ref, w_ref, out_ref, wlo, whi, corr):
    wf = w_ref[0].astype(jnp.float32)
    wlo[...] = wf[:, 0:PATCH]
    whi[...] = jnp.zeros(whi.shape, jnp.float32)
    whi[:, 0:WIN - HALF] = wf[:, HALF:WIN]
    tfv = tf_ref[0].astype(jnp.float32)
    t_cat = jnp.concatenate([tf_ref[0, 0:HALF, :], tf_ref[0, HALF:PATCH, :]], axis=1)
    corr[...] = jnp.zeros(corr.shape, jnp.float32)

    def step(dy, carry):
        w_cat = jnp.concatenate(
            [whi[pl.ds(dy, PATCH), :], wlo[pl.ds(dy, PATCH), :]], axis=0
        ).astype(jnp.bfloat16)
        m = jnp.dot(t_cat, w_cat, preferred_element_type=jnp.float32)
        r = pltpu.roll(m, 0, axis=1, stride=1, stride_axis=0)
        corr[pl.ds(dy, 1), :] = jnp.sum(r, axis=0, keepdims=True)
        return carry

    lax.fori_loop(0, SHIFTS, step, 0, unroll=SHIFTS)

    c = corr[...]
    rows = lax.broadcasted_iota(jnp.int32, c.shape, 0)
    lanes = lax.broadcasted_iota(jnp.int32, c.shape, 1)
    valid = (rows < SHIFTS) & (lanes >= HALF - 1)
    e_t = jnp.sum(tfv * tfv, keepdims=True) / float(PATCH * PATCH)
    e_w = jnp.sum(wf * wf, keepdims=True) / float(WIN * WIN)
    denom = float(PATCH * PATCH) * jnp.sqrt((e_t + EPSILON) * (e_w + EPSILON))
    scores = SHARPNESS * c / denom
    scores = jnp.where(valid, scores, -jnp.inf)
    mx = jnp.max(scores, keepdims=True)
    e = jnp.where(valid, jnp.exp(scores - mx), 0.0)
    w = e / jnp.sum(e, keepdims=True)
    sy = (rows - RADIUS).astype(jnp.float32)
    sx = (lanes - (HALF - 1) - RADIUS).astype(jnp.float32)
    fy = jnp.sum(w * sy, keepdims=True) / FLOW_UNIT
    fx = jnp.sum(w * sx, keepdims=True) / FLOW_UNIT
    orow = lax.broadcasted_iota(jnp.int32, (8, 128), 0)
    out_ref[0] = jnp.where(orow == 0, fy, jnp.where(orow == 1, fx, 0.0))


def flows_of(tflipped, windows):
    n = tflipped.shape[0]
    out = pl.pallas_call(
        flow_kernel,
        grid=(n,),
        in_specs=[pl.BlockSpec((1, PATCH, PATCH), lambda i: (i, 0, 0)),
                  pl.BlockSpec((1, WIN, WIN), lambda i: (i, 0, 0))],
        out_specs=pl.BlockSpec((1, 8, 128), lambda i: (i, 0, 0)),
        out_shape=jax.ShapeDtypeStruct((n, 8, 128), jnp.float32),
        scratch_shapes=[pltpu.VMEM((WIN, PATCH), jnp.float32),
                        pltpu.VMEM((WIN, PATCH), jnp.float32),
                        pltpu.VMEM((72, PATCH), jnp.float32)],
    )(tflipped, windows)
    return out[:, 0:2, 0].T


def padded_2(cells, sides, width):
    for axis, dim in sides:
        count = lax.axis_size(axis)
        ends = count - 1
        head = lax.slice_in_dim(cells, 0, width, axis=dim)
        tail = lax.slice_in_dim(cells, cells.shape[dim] - width, cells.shape[dim], axis=dim)
        cells = jnp.concatenate(
            [
                lax.ppermute(tail, axis, [(i, (i + 1) % count) for i in range(ends)]),
                cells,
                lax.ppermute(head, axis, [((i + 1) % count, i) for i in range(ends)]),
            ],
            axis=dim,
        )
    return cells


def relax_sweep(padded, mask_pad, target, count):
    centre = padded[:, 1:-1, 1:-1]
    mask_c = mask_pad[1:-1, 1:-1]
    height = centre.shape[1]
    width = centre.shape[2]
    spring = jnp.zeros_like(centre)
    for row_step, col_step in ((0, 1), (2, 1), (1, 0), (1, 2)):
        nearby = padded[:, row_step : row_step + height, col_step : col_step + width]
        mask_n = mask_pad[row_step : row_step + height, col_step : col_step + width]
        spring = spring + mask_c * mask_n * (nearby - centre)
    return centre + SPRING_RATE * spring + FLOW_RATE * (target - count * centre)


def one_hot(starts, size, extent, flip=False):
    offs = jnp.arange(size, dtype=jnp.int32)
    if flip:
        offs = size - 1 - offs
    want = starts[:, None, None] + offs[None, :, None]
    return (want == jnp.arange(extent, dtype=jnp.int32)[None, None, :]).astype(jnp.bfloat16)


def shards(
    section_a, section_b, template_corner, template_slot, window_corner, window_slot, node_mask
):
    tile_size = section_a.shape[0]
    slot_count = lax.axis_size("tx") * CAP
    slot_ids = jnp.arange(slot_count, dtype=jnp.int32)
    owner_picker = template_slot[0][:, None] == slot_ids[None, :]
    source_picker = window_slot[0][:, None] == slot_ids[None, :]
    f32 = jnp.float32

    col_pick = one_hot(template_corner[1, 0], PATCH, section_a.shape[1], flip=True)
    row_pick = one_hot(template_corner[0, 0], PATCH, section_a.shape[0])
    by_col = jnp.einsum("krc,ac->kra", col_pick, section_a, preferred_element_type=f32)
    tflipped = jnp.einsum(
        "kra,kia->kri", by_col.astype(jnp.bfloat16), row_pick, preferred_element_type=f32
    ).astype(jnp.bfloat16)
    outgoing = jnp.einsum(
        "ks,kri->sri", owner_picker.astype(jnp.bfloat16), tflipped, preferred_element_type=f32
    ).astype(jnp.bfloat16)

    n_tx = lax.axis_size("tx")
    n_ty = lax.axis_size("ty")
    me_x = lax.axis_index("tx")
    tx_ids = jnp.arange(n_tx, dtype=jnp.int32)
    to_left = (tx_ids == me_x - 1)[:, None]
    to_right = (tx_ids == me_x + 1)[:, None]

    def side_payload(left, right):
        lf = left.reshape(1, -1)
        rf = right.reshape(1, -1)
        return jnp.where(to_left, lf, jnp.where(to_right, rf, jnp.zeros_like(lf)))

    def side_arrivals(got, shape):
        left = lax.dynamic_index_in_dim(got, jnp.maximum(me_x - 1, 0), axis=0, keepdims=False)
        right = lax.dynamic_index_in_dim(got, jnp.minimum(me_x + 1, n_tx - 1), axis=0, keepdims=False)
        left = jnp.where(me_x >= 1, left, jnp.zeros_like(left)).reshape(shape)
        right = jnp.where(me_x + 1 < n_tx, right, jnp.zeros_like(right)).reshape(shape)
        return left, right

    def rows_exchange(cells, width):
        count = n_ty
        height = cells.shape[-2]
        head = cells[..., 0:width, :]
        tail = cells[..., height - width : height, :]
        above = lax.ppermute(tail, "ty", [(i, i + 1) for i in range(count - 1)])
        below = lax.ppermute(head, "ty", [(i + 1, i) for i in range(count - 1)])
        return above, below

    node_rows, node_cols = node_mask.shape
    centre_y = (window_corner[0, 0] + PATCH // 2) * node_rows // tile_size
    centre_x = (window_corner[1, 0] + PATCH // 2) * node_cols // tile_size
    attach = (centre_y[:, None, None] == jnp.arange(node_rows, dtype=jnp.int32)[None, :, None]) & (
        centre_x[:, None, None] == jnp.arange(node_cols, dtype=jnp.int32)[None, None, :]
    )
    count = jnp.sum(attach.astype(f32), axis=0)
    mask = node_mask.astype(f32)
    w = ITERS_R
    arrived = lax.all_to_all(outgoing, "tx", split_axis=0, concat_axis=0, tiled=True)
    b_tall = padded_2(section_b, (("ty", 0),), RADIUS)
    tall_cols = b_tall.shape[1]
    rim_left = lax.ppermute(
        b_tall[:, tall_cols - RADIUS :], "tx", [(i, i + 1) for i in range(n_tx - 1)]
    )
    rim_right = lax.ppermute(b_tall[:, 0:RADIUS], "tx", [(i + 1, i) for i in range(n_tx - 1)])
    wrow_pick = one_hot(window_corner[0, 0], WIN, b_tall.shape[0])
    wcol_pick = one_hot(window_corner[1, 0], WIN, tall_cols + 2 * RADIUS)
    wcol_mid = wcol_pick[:, :, RADIUS : RADIUS + tall_cols]
    wcol_side = jnp.concatenate(
        [wcol_pick[:, :, 0:RADIUS], wcol_pick[:, :, RADIUS + tall_cols :]], axis=2
    )
    by_row_mid = jnp.einsum("mra,ac->mrc", wrow_pick, b_tall, preferred_element_type=f32)
    win_mid = jnp.einsum(
        "mrc,msc->mrs", by_row_mid.astype(jnp.bfloat16), wcol_mid, preferred_element_type=f32
    )
    win_mid = lax.optimization_barrier(win_mid)
    rims = jnp.concatenate([rim_left, rim_right], axis=1)
    by_row_side = jnp.einsum("mra,ac->mrc", wrow_pick, rims, preferred_element_type=f32)
    win_side = jnp.einsum(
        "mrc,msc->mrs", by_row_side.astype(jnp.bfloat16), wcol_side, preferred_element_type=f32
    )
    windows = (win_mid + win_side).astype(jnp.bfloat16)
    matched = jnp.einsum(
        "ms,sri->mri", source_picker.astype(jnp.bfloat16), arrived, preferred_element_type=f32
    ).astype(jnp.bfloat16)

    flows = flows_of(matched, windows)
    source_flow = -flows

    target = jnp.sum(jnp.where(attach[None], source_flow[:, :, None, None], 0.0), axis=1)
    fields = jnp.concatenate([target, count[None], mask[None]], axis=0)
    returned = jnp.sum(jnp.where(source_picker[None], flows[:, :, None], 0.0), axis=1)
    lane = 128
    sides = side_payload(fields[:, :, 0:w], fields[:, :, node_cols - w :])
    flows_out = returned.reshape(2, n_tx, CAP).transpose(1, 0, 2).reshape(n_tx, -1)
    side_len = sides.shape[1]
    chunk = -(-(side_len + flows_out.shape[1]) // lane) * lane
    back = jnp.concatenate(
        [sides, flows_out, jnp.zeros((n_tx, chunk - side_len - flows_out.shape[1]), f32)], axis=1
    ).reshape(n_tx, chunk // lane, lane)
    came = lax.all_to_all(back, "tx", split_axis=0, concat_axis=0, tiled=True).reshape(n_tx, chunk)
    landed = came[:, side_len : side_len + 2 * CAP].reshape(n_tx, 2, CAP).transpose(1, 0, 2).reshape(2, -1)
    owner_flow = jnp.sum(jnp.where(owner_picker[None], landed[:, None, :], 0.0), axis=2)
    f_left, f_right = side_arrivals(came[:, 0:side_len], (fields.shape[0], node_rows, w))
    fields_tx = jnp.concatenate([f_left, fields, f_right], axis=2)
    f_above, f_below = rows_exchange(fields_tx, w)
    wide = jnp.concatenate([f_above, fields_tx, f_below], axis=1)

    displace = jnp.zeros((2,) + wide.shape[1:], f32)
    for sweep in range(ITERS_R):
        lo_m, hi_m = sweep, wide.shape[1] - sweep
        lo_t, hi_t = sweep + 1, wide.shape[1] - sweep - 1
        displace = relax_sweep(
            displace,
            wide[3, lo_m:hi_m, lo_m:hi_m],
            wide[0:2, lo_t:hi_t, lo_t:hi_t],
            wide[2, lo_t:hi_t, lo_t:hi_t],
        )
    return (owner_flow[:, None, :], source_flow[:, None, :], displace)


def solution(mesh):
    placed = (
        P("ty", "tx"),
        P("ty", "tx"),
        P(None, "ty", "tx"),
        P("ty", "tx"),
        P(None, "ty", "tx"),
        P("ty", "tx"),
        P("ty", "tx"),
    )
    return jax.shard_map(
        shards,
        mesh=mesh,
        in_specs=placed,
        out_specs=(P(None, "ty", "tx"), P(None, "ty", "tx"), P(None, "ty", "tx")),
        check_vma=False,
    )
```

```python
import jax
import jax.numpy as jnp
from jax import lax
from jax.sharding import PartitionSpec as P
from jax.experimental import pallas as pl
from jax.experimental.pallas import tpu as pltpu

PATCH = 128
SHIFTS = 65
RADIUS = 32
WIN = 192
CAP = 2
ITERS_R = 3


SHARPNESS = 256.0
SPRING_RATE = 0.25
FLOW_RATE = 0.5
FLOW_UNIT = 8.0
EPSILON = 1e-05

HALF = PATCH // 2
PER = 2


def flow_kernel(tf_ref, w_ref, out_ref, wlo, whi, corr):
    cats = []
    for q in range(PER):
        wf = w_ref[q].astype(jnp.float32)
        wlo[q] = wf[:, 0:PATCH]
        whi[q] = jnp.zeros(whi.shape[1:], jnp.float32)
        whi[q, :, 0:WIN - HALF] = wf[:, HALF:WIN]
        cats.append(jnp.concatenate([tf_ref[q, 0:HALF, :], tf_ref[q, HALF:PATCH, :]], axis=1))
        corr[q] = jnp.zeros(corr.shape[1:], jnp.float32)
    for dy in range(SHIFTS):
        for q in range(PER):
            w_cat = jnp.concatenate(
                [whi[q, dy : dy + PATCH, :], wlo[q, dy : dy + PATCH, :]], axis=0
            ).astype(jnp.bfloat16)
            m = jnp.dot(cats[q], w_cat, preferred_element_type=jnp.float32)
            r = pltpu.roll(m, 0, axis=1, stride=1, stride_axis=0)
            corr[q, dy : dy + 1, :] = jnp.sum(r, axis=0, keepdims=True)
    for q in range(PER):
        _epilogue(tf_ref, w_ref, out_ref, corr, q)


def _epilogue(tf_ref, w_ref, out_ref, corr, q):
    wf = w_ref[q].astype(jnp.float32)
    tfv = tf_ref[q].astype(jnp.float32)
    c = corr[q]
    rows = lax.broadcasted_iota(jnp.int32, c.shape, 0)
    lanes = lax.broadcasted_iota(jnp.int32, c.shape, 1)
    valid = (rows < SHIFTS) & (lanes >= HALF - 1)
    e_t = jnp.sum(tfv * tfv, keepdims=True) / float(PATCH * PATCH)
    e_w = jnp.sum(wf * wf, keepdims=True) / float(WIN * WIN)
    denom = float(PATCH * PATCH) * jnp.sqrt((e_t + EPSILON) * (e_w + EPSILON))
    scores = SHARPNESS * c / denom
    scores = jnp.where(valid, scores, -jnp.inf)
    mx = jnp.max(scores, keepdims=True)
    e = jnp.where(valid, jnp.exp(scores - mx), 0.0)
    w = e / jnp.sum(e, keepdims=True)
    sy = (rows - RADIUS).astype(jnp.float32)
    sx = (lanes - (HALF - 1) - RADIUS).astype(jnp.float32)
    fy = jnp.sum(w * sy, keepdims=True) / FLOW_UNIT
    fx = jnp.sum(w * sx, keepdims=True) / FLOW_UNIT
    orow = lax.broadcasted_iota(jnp.int32, (8, 128), 0)
    out_ref[q] = jnp.where(orow == 0, fy, jnp.where(orow == 1, fx, 0.0))

def flows_of(tflipped, windows):
    n = tflipped.shape[0]
    out = pl.pallas_call(
        flow_kernel,
        grid=(n // PER,),
        in_specs=[pl.BlockSpec((PER, PATCH, PATCH), lambda i: (i, 0, 0)),
                  pl.BlockSpec((PER, WIN, WIN), lambda i: (i, 0, 0))],
        out_specs=pl.BlockSpec((PER, 8, 128), lambda i: (i, 0, 0)),
        out_shape=jax.ShapeDtypeStruct((n, 8, 128), jnp.float32),
        scratch_shapes=[pltpu.VMEM((PER, WIN, PATCH), jnp.float32),
                        pltpu.VMEM((PER, WIN, PATCH), jnp.float32),
                        pltpu.VMEM((PER, 72, PATCH), jnp.float32)],
    )(tflipped, windows)
    return out[:, 0:2, 0].T


def padded_2(cells, sides, width):
    for axis, dim in sides:
        count = lax.axis_size(axis)
        ends = count - 1
        head = lax.slice_in_dim(cells, 0, width, axis=dim)
        tail = lax.slice_in_dim(cells, cells.shape[dim] - width, cells.shape[dim], axis=dim)
        cells = jnp.concatenate(
            [
                lax.ppermute(tail, axis, [(i, (i + 1) % count) for i in range(ends)]),
                cells,
                lax.ppermute(head, axis, [((i + 1) % count, i) for i in range(ends)]),
            ],
            axis=dim,
        )
    return cells


def halo(cells, width):
    n_ty = lax.axis_size("ty")
    n_tx = lax.axis_size("tx")
    height, breadth = cells.shape[-2], cells.shape[-1]
    pieces = {}
    for dy in (-1, 0, 1):
        for dx in (-1, 0, 1):
            if dy == 0 and dx == 0:
                pieces[(dy, dx)] = cells
                continue
            rows = {-1: (height - width, height), 0: (0, height), 1: (0, width)}[dy]
            cols = {-1: (breadth - width, breadth), 0: (0, breadth), 1: (0, width)}[dx]
            part = cells[..., rows[0] : rows[1], cols[0] : cols[1]]
            pairs = []
            for i in range(n_ty):
                for j in range(n_tx):
                    si, sj = i + dy, j + dx
                    if 0 <= si < n_ty and 0 <= sj < n_tx:
                        pairs.append((si * n_tx + sj, i * n_tx + j))
            pieces[(dy, dx)] = lax.ppermute(part, ("ty", "tx"), pairs)
    bands = [
        jnp.concatenate([pieces[(dy, -1)], pieces[(dy, 0)], pieces[(dy, 1)]], axis=-1)
        for dy in (-1, 0, 1)
    ]
    return jnp.concatenate(bands, axis=-2)


def relax_sweep(padded, mask_pad, target, count):
    centre = padded[:, 1:-1, 1:-1]
    mask_c = mask_pad[1:-1, 1:-1]
    height = centre.shape[1]
    width = centre.shape[2]
    spring = jnp.zeros_like(centre)
    for row_step, col_step in ((0, 1), (2, 1), (1, 0), (1, 2)):
        nearby = padded[:, row_step : row_step + height, col_step : col_step + width]
        mask_n = mask_pad[row_step : row_step + height, col_step : col_step + width]
        spring = spring + mask_c * mask_n * (nearby - centre)
    return centre + SPRING_RATE * spring + FLOW_RATE * (target - count * centre)


def one_hot(starts, size, extent, flip=False):
    offs = jnp.arange(size, dtype=jnp.int32)
    if flip:
        offs = size - 1 - offs
    want = starts[:, None, None] + offs[None, :, None]
    return (want == jnp.arange(extent, dtype=jnp.int32)[None, None, :]).astype(jnp.bfloat16)


def shards(
    section_a, section_b, template_corner, template_slot, window_corner, window_slot, node_mask
):
    tile_size = section_a.shape[0]
    slot_count = lax.axis_size("tx") * CAP
    slot_ids = jnp.arange(slot_count, dtype=jnp.int32)
    owner_picker = template_slot[0][:, None] == slot_ids[None, :]
    source_picker = window_slot[0][:, None] == slot_ids[None, :]
    f32 = jnp.float32

    col_pick = one_hot(template_corner[1, 0], PATCH, section_a.shape[1], flip=True)
    row_pick = one_hot(template_corner[0, 0], PATCH, section_a.shape[0])
    by_col = jnp.einsum("krc,ac->kra", col_pick, section_a, preferred_element_type=f32)
    tflipped = jnp.einsum(
        "kra,kia->kri", by_col.astype(jnp.bfloat16), row_pick, preferred_element_type=f32
    ).astype(jnp.bfloat16)
    outgoing = jnp.einsum(
        "ks,kri->sri", owner_picker.astype(jnp.bfloat16), tflipped, preferred_element_type=f32
    ).astype(jnp.bfloat16)

    n_tx = lax.axis_size("tx")
    n_ty = lax.axis_size("ty")
    me_x = lax.axis_index("tx")
    tx_ids = jnp.arange(n_tx, dtype=jnp.int32)
    to_left = (tx_ids == me_x - 1)[:, None]
    to_right = (tx_ids == me_x + 1)[:, None]

    def side_payload(left, right):
        lf = left.reshape(1, -1)
        rf = right.reshape(1, -1)
        return jnp.where(to_left, lf, jnp.where(to_right, rf, jnp.zeros_like(lf)))

    def side_arrivals(got, shape):
        left = lax.dynamic_index_in_dim(got, jnp.maximum(me_x - 1, 0), axis=0, keepdims=False)
        right = lax.dynamic_index_in_dim(got, jnp.minimum(me_x + 1, n_tx - 1), axis=0, keepdims=False)
        left = jnp.where(me_x >= 1, left, jnp.zeros_like(left)).reshape(shape)
        right = jnp.where(me_x + 1 < n_tx, right, jnp.zeros_like(right)).reshape(shape)
        return left, right

    def rows_exchange(cells, width):
        count = n_ty
        height = cells.shape[-2]
        head = cells[..., 0:width, :]
        tail = cells[..., height - width : height, :]
        above = lax.ppermute(tail, "ty", [(i, i + 1) for i in range(count - 1)])
        below = lax.ppermute(head, "ty", [(i + 1, i) for i in range(count - 1)])
        return above, below

    node_rows, node_cols = node_mask.shape
    centre_y = (window_corner[0, 0] + PATCH // 2) * node_rows // tile_size
    centre_x = (window_corner[1, 0] + PATCH // 2) * node_cols // tile_size
    attach = (centre_y[:, None, None] == jnp.arange(node_rows, dtype=jnp.int32)[None, :, None]) & (
        centre_x[:, None, None] == jnp.arange(node_cols, dtype=jnp.int32)[None, None, :]
    )
    count = jnp.sum(attach.astype(f32), axis=0)
    mask = node_mask.astype(f32)
    w = ITERS_R
    arrived = lax.all_to_all(outgoing, "tx", split_axis=0, concat_axis=0, tiled=True)
    b_wide = padded_2(section_b, (("ty", 0), ("tx", 1)), RADIUS)

    wrow_pick = one_hot(window_corner[0, 0], WIN, b_wide.shape[0])
    wcol_pick = one_hot(window_corner[1, 0], WIN, b_wide.shape[1])
    by_row = jnp.einsum("mra,ac->mrc", wrow_pick, b_wide, preferred_element_type=f32)
    windows = jnp.einsum(
        "mrc,msc->mrs", by_row.astype(jnp.bfloat16), wcol_pick, preferred_element_type=f32
    ).astype(jnp.bfloat16)
    matched = jnp.einsum(
        "ms,sri->mri", source_picker.astype(jnp.bfloat16), arrived, preferred_element_type=f32
    ).astype(jnp.bfloat16)

    flows = flows_of(matched, windows)
    source_flow = -flows

    target = jnp.sum(jnp.where(attach[None], source_flow[:, :, None, None], 0.0), axis=1)
    fields = jnp.concatenate([target, count[None], mask[None]], axis=0)
    returned = jnp.sum(jnp.where(source_picker[None], flows[:, :, None], 0.0), axis=1)
    lane = 128
    sides = side_payload(fields[:, :, 0:w], fields[:, :, node_cols - w :])
    flows_out = returned.reshape(2, n_tx, CAP).transpose(1, 0, 2).reshape(n_tx, -1)
    side_len = sides.shape[1]
    chunk = -(-(side_len + flows_out.shape[1]) // lane) * lane
    back = jnp.concatenate(
        [sides, flows_out, jnp.zeros((n_tx, chunk - side_len - flows_out.shape[1]), f32)], axis=1
    ).reshape(n_tx, chunk // lane, lane)
    came = lax.all_to_all(back, "tx", split_axis=0, concat_axis=0, tiled=True).reshape(n_tx, chunk)
    landed = came[:, side_len : side_len + 2 * CAP].reshape(n_tx, 2, CAP).transpose(1, 0, 2).reshape(2, -1)
    owner_flow = jnp.sum(jnp.where(owner_picker[None], landed[:, None, :], 0.0), axis=2)
    f_left, f_right = side_arrivals(came[:, 0:side_len], (fields.shape[0], node_rows, w))
    fields_tx = jnp.concatenate([f_left, fields, f_right], axis=2)
    f_above, f_below = rows_exchange(fields_tx, w)
    wide = jnp.concatenate([f_above, fields_tx, f_below], axis=1)

    displace = jnp.zeros((2,) + wide.shape[1:], f32)
    for sweep in range(ITERS_R):
        lo_m, hi_m = sweep, wide.shape[1] - sweep
        lo_t, hi_t = sweep + 1, wide.shape[1] - sweep - 1
        displace = relax_sweep(
            displace,
            wide[3, lo_m:hi_m, lo_m:hi_m],
            wide[0:2, lo_t:hi_t, lo_t:hi_t],
            wide[2, lo_t:hi_t, lo_t:hi_t],
        )
    return (owner_flow[:, None, :], source_flow[:, None, :], displace)


def solution(mesh):
    placed = (
        P("ty", "tx"),
        P("ty", "tx"),
        P(None, "ty", "tx"),
        P("ty", "tx"),
        P(None, "ty", "tx"),
        P("ty", "tx"),
        P("ty", "tx"),
    )
    return jax.shard_map(
        shards,
        mesh=mesh,
        in_specs=placed,
        out_specs=(P(None, "ty", "tx"), P(None, "ty", "tx"), P(None, "ty", "tx")),
        check_vma=False,
    )
```

```python
import jax
import jax.numpy as jnp
from jax import lax
from jax.sharding import PartitionSpec as P
from jax.experimental import pallas as pl
from jax.experimental.pallas import tpu as pltpu

PATCH = 128
SHIFTS = 65
RADIUS = 32
WIN = 192
CAP = 2
ITERS_R = 3


SHARPNESS = 256.0
SPRING_RATE = 0.25
FLOW_RATE = 0.5
FLOW_UNIT = 8.0
EPSILON = 1e-05

HALF = PATCH // 2
PER = 4


def flow_kernel(tf_ref, w_ref, out_ref, wlo, whi, corr):
    cats = []
    for q in range(PER):
        wf = w_ref[q].astype(jnp.float32)
        wlo[q] = wf[:, 0:PATCH]
        whi[q] = jnp.zeros(whi.shape[1:], jnp.float32)
        whi[q, :, 0:WIN - HALF] = wf[:, HALF:WIN]
        cats.append(jnp.concatenate([tf_ref[q, 0:HALF, :], tf_ref[q, HALF:PATCH, :]], axis=1))
        corr[q] = jnp.zeros(corr.shape[1:], jnp.float32)
    for dy in range(SHIFTS):
        for q in range(PER):
            w_cat = jnp.concatenate(
                [whi[q, dy : dy + PATCH, :], wlo[q, dy : dy + PATCH, :]], axis=0
            ).astype(jnp.bfloat16)
            m = jnp.dot(cats[q], w_cat, preferred_element_type=jnp.float32)
            r = pltpu.roll(m, 0, axis=1, stride=1, stride_axis=0)
            corr[q, dy : dy + 1, :] = jnp.sum(r, axis=0, keepdims=True)
    for q in range(PER):
        _epilogue(tf_ref, w_ref, out_ref, corr, q)


def _epilogue(tf_ref, w_ref, out_ref, corr, q):
    wf = w_ref[q].astype(jnp.float32)
    tfv = tf_ref[q].astype(jnp.float32)
    c = corr[q]
    rows = lax.broadcasted_iota(jnp.int32, c.shape, 0)
    lanes = lax.broadcasted_iota(jnp.int32, c.shape, 1)
    valid = (rows < SHIFTS) & (lanes >= HALF - 1)
    e_t = jnp.sum(tfv * tfv, keepdims=True) / float(PATCH * PATCH)
    e_w = jnp.sum(wf * wf, keepdims=True) / float(WIN * WIN)
    denom = float(PATCH * PATCH) * jnp.sqrt((e_t + EPSILON) * (e_w + EPSILON))
    scores = SHARPNESS * c / denom
    scores = jnp.where(valid, scores, -jnp.inf)
    mx = jnp.max(scores, keepdims=True)
    e = jnp.where(valid, jnp.exp(scores - mx), 0.0)
    w = e / jnp.sum(e, keepdims=True)
    sy = (rows - RADIUS).astype(jnp.float32)
    sx = (lanes - (HALF - 1) - RADIUS).astype(jnp.float32)
    fy = jnp.sum(w * sy, keepdims=True) / FLOW_UNIT
    fx = jnp.sum(w * sx, keepdims=True) / FLOW_UNIT
    orow = lax.broadcasted_iota(jnp.int32, (8, 128), 0)
    out_ref[q] = jnp.where(orow == 0, fy, jnp.where(orow == 1, fx, 0.0))

def flows_of(tflipped, windows):
    n = tflipped.shape[0]
    out = pl.pallas_call(
        flow_kernel,
        grid=(n // PER,),
        in_specs=[pl.BlockSpec((PER, PATCH, PATCH), lambda i: (i, 0, 0)),
                  pl.BlockSpec((PER, WIN, WIN), lambda i: (i, 0, 0))],
        out_specs=pl.BlockSpec((PER, 8, 128), lambda i: (i, 0, 0)),
        out_shape=jax.ShapeDtypeStruct((n, 8, 128), jnp.float32),
        scratch_shapes=[pltpu.VMEM((PER, WIN, PATCH), jnp.float32),
                        pltpu.VMEM((PER, WIN, PATCH), jnp.float32),
                        pltpu.VMEM((PER, 72, PATCH), jnp.float32)],
    )(tflipped, windows)
    return out[:, 0:2, 0].T


def padded_2(cells, sides, width):
    for axis, dim in sides:
        count = lax.axis_size(axis)
        ends = count - 1
        head = lax.slice_in_dim(cells, 0, width, axis=dim)
        tail = lax.slice_in_dim(cells, cells.shape[dim] - width, cells.shape[dim], axis=dim)
        cells = jnp.concatenate(
            [
                lax.ppermute(tail, axis, [(i, (i + 1) % count) for i in range(ends)]),
                cells,
                lax.ppermute(head, axis, [((i + 1) % count, i) for i in range(ends)]),
            ],
            axis=dim,
        )
    return cells


def halo(cells, width):
    n_ty = lax.axis_size("ty")
    n_tx = lax.axis_size("tx")
    height, breadth = cells.shape[-2], cells.shape[-1]
    pieces = {}
    for dy in (-1, 0, 1):
        for dx in (-1, 0, 1):
            if dy == 0 and dx == 0:
                pieces[(dy, dx)] = cells
                continue
            rows = {-1: (height - width, height), 0: (0, height), 1: (0, width)}[dy]
            cols = {-1: (breadth - width, breadth), 0: (0, breadth), 1: (0, width)}[dx]
            part = cells[..., rows[0] : rows[1], cols[0] : cols[1]]
            pairs = []
            for i in range(n_ty):
                for j in range(n_tx):
                    si, sj = i + dy, j + dx
                    if 0 <= si < n_ty and 0 <= sj < n_tx:
                        pairs.append((si * n_tx + sj, i * n_tx + j))
            pieces[(dy, dx)] = lax.ppermute(part, ("ty", "tx"), pairs)
    bands = [
        jnp.concatenate([pieces[(dy, -1)], pieces[(dy, 0)], pieces[(dy, 1)]], axis=-1)
        for dy in (-1, 0, 1)
    ]
    return jnp.concatenate(bands, axis=-2)


def relax_sweep(padded, mask_pad, target, count):
    centre = padded[:, 1:-1, 1:-1]
    mask_c = mask_pad[1:-1, 1:-1]
    height = centre.shape[1]
    width = centre.shape[2]
    spring = jnp.zeros_like(centre)
    for row_step, col_step in ((0, 1), (2, 1), (1, 0), (1, 2)):
        nearby = padded[:, row_step : row_step + height, col_step : col_step + width]
        mask_n = mask_pad[row_step : row_step + height, col_step : col_step + width]
        spring = spring + mask_c * mask_n * (nearby - centre)
    return centre + SPRING_RATE * spring + FLOW_RATE * (target - count * centre)


def one_hot(starts, size, extent, flip=False):
    offs = jnp.arange(size, dtype=jnp.int32)
    if flip:
        offs = size - 1 - offs
    want = starts[:, None, None] + offs[None, :, None]
    return (want == jnp.arange(extent, dtype=jnp.int32)[None, None, :]).astype(jnp.bfloat16)


def shards(
    section_a, section_b, template_corner, template_slot, window_corner, window_slot, node_mask
):
    tile_size = section_a.shape[0]
    slot_count = lax.axis_size("tx") * CAP
    slot_ids = jnp.arange(slot_count, dtype=jnp.int32)
    owner_picker = template_slot[0][:, None] == slot_ids[None, :]
    source_picker = window_slot[0][:, None] == slot_ids[None, :]
    f32 = jnp.float32

    col_pick = one_hot(template_corner[1, 0], PATCH, section_a.shape[1], flip=True)
    row_pick = one_hot(template_corner[0, 0], PATCH, section_a.shape[0])
    by_col = jnp.einsum("krc,ac->kra", col_pick, section_a, preferred_element_type=f32)
    tflipped = jnp.einsum(
        "kra,kia->kri", by_col.astype(jnp.bfloat16), row_pick, preferred_element_type=f32
    ).astype(jnp.bfloat16)
    outgoing = jnp.einsum(
        "ks,kri->sri", owner_picker.astype(jnp.bfloat16), tflipped, preferred_element_type=f32
    ).astype(jnp.bfloat16)

    n_tx = lax.axis_size("tx")
    n_ty = lax.axis_size("ty")
    me_x = lax.axis_index("tx")
    tx_ids = jnp.arange(n_tx, dtype=jnp.int32)
    to_left = (tx_ids == me_x - 1)[:, None]
    to_right = (tx_ids == me_x + 1)[:, None]

    def side_payload(left, right):
        lf = left.reshape(1, -1)
        rf = right.reshape(1, -1)
        return jnp.where(to_left, lf, jnp.where(to_right, rf, jnp.zeros_like(lf)))

    def side_arrivals(got, shape):
        left = lax.dynamic_index_in_dim(got, jnp.maximum(me_x - 1, 0), axis=0, keepdims=False)
        right = lax.dynamic_index_in_dim(got, jnp.minimum(me_x + 1, n_tx - 1), axis=0, keepdims=False)
        left = jnp.where(me_x >= 1, left, jnp.zeros_like(left)).reshape(shape)
        right = jnp.where(me_x + 1 < n_tx, right, jnp.zeros_like(right)).reshape(shape)
        return left, right

    def rows_exchange(cells, width):
        count = n_ty
        height = cells.shape[-2]
        head = cells[..., 0:width, :]
        tail = cells[..., height - width : height, :]
        above = lax.ppermute(tail, "ty", [(i, i + 1) for i in range(count - 1)])
        below = lax.ppermute(head, "ty", [(i + 1, i) for i in range(count - 1)])
        return above, below

    node_rows, node_cols = node_mask.shape
    centre_y = (window_corner[0, 0] + PATCH // 2) * node_rows // tile_size
    centre_x = (window_corner[1, 0] + PATCH // 2) * node_cols // tile_size
    attach = (centre_y[:, None, None] == jnp.arange(node_rows, dtype=jnp.int32)[None, :, None]) & (
        centre_x[:, None, None] == jnp.arange(node_cols, dtype=jnp.int32)[None, None, :]
    )
    count = jnp.sum(attach.astype(f32), axis=0)
    mask = node_mask.astype(f32)
    w = ITERS_R
    arrived = lax.all_to_all(outgoing, "tx", split_axis=0, concat_axis=0, tiled=True)
    b_wide = padded_2(section_b, (("ty", 0), ("tx", 1)), RADIUS)

    wrow_pick = one_hot(window_corner[0, 0], WIN, b_wide.shape[0])
    wcol_pick = one_hot(window_corner[1, 0], WIN, b_wide.shape[1])
    by_row = jnp.einsum("mra,ac->mrc", wrow_pick, b_wide, preferred_element_type=f32)
    windows = jnp.einsum(
        "mrc,msc->mrs", by_row.astype(jnp.bfloat16), wcol_pick, preferred_element_type=f32
    ).astype(jnp.bfloat16)
    matched = jnp.einsum(
        "ms,sri->mri", source_picker.astype(jnp.bfloat16), arrived, preferred_element_type=f32
    ).astype(jnp.bfloat16)

    flows = flows_of(matched, windows)
    source_flow = -flows

    target = jnp.sum(jnp.where(attach[None], source_flow[:, :, None, None], 0.0), axis=1)
    fields = jnp.concatenate([target, count[None], mask[None]], axis=0)
    returned = jnp.sum(jnp.where(source_picker[None], flows[:, :, None], 0.0), axis=1)
    lane = 128
    sides = side_payload(fields[:, :, 0:w], fields[:, :, node_cols - w :])
    flows_out = returned.reshape(2, n_tx, CAP).transpose(1, 0, 2).reshape(n_tx, -1)
    side_len = sides.shape[1]
    chunk = -(-(side_len + flows_out.shape[1]) // lane) * lane
    back = jnp.concatenate(
        [sides, flows_out, jnp.zeros((n_tx, chunk - side_len - flows_out.shape[1]), f32)], axis=1
    ).reshape(n_tx, chunk // lane, lane)
    came = lax.all_to_all(back, "tx", split_axis=0, concat_axis=0, tiled=True).reshape(n_tx, chunk)
    landed = came[:, side_len : side_len + 2 * CAP].reshape(n_tx, 2, CAP).transpose(1, 0, 2).reshape(2, -1)
    owner_flow = jnp.sum(jnp.where(owner_picker[None], landed[:, None, :], 0.0), axis=2)
    f_left, f_right = side_arrivals(came[:, 0:side_len], (fields.shape[0], node_rows, w))
    fields_tx = jnp.concatenate([f_left, fields, f_right], axis=2)
    f_above, f_below = rows_exchange(fields_tx, w)
    wide = jnp.concatenate([f_above, fields_tx, f_below], axis=1)

    displace = jnp.zeros((2,) + wide.shape[1:], f32)
    for sweep in range(ITERS_R):
        lo_m, hi_m = sweep, wide.shape[1] - sweep
        lo_t, hi_t = sweep + 1, wide.shape[1] - sweep - 1
        displace = relax_sweep(
            displace,
            wide[3, lo_m:hi_m, lo_m:hi_m],
            wide[0:2, lo_t:hi_t, lo_t:hi_t],
            wide[2, lo_t:hi_t, lo_t:hi_t],
        )
    return (owner_flow[:, None, :], source_flow[:, None, :], displace)


def solution(mesh):
    placed = (
        P("ty", "tx"),
        P("ty", "tx"),
        P(None, "ty", "tx"),
        P("ty", "tx"),
        P(None, "ty", "tx"),
        P("ty", "tx"),
        P("ty", "tx"),
    )
    return jax.shard_map(
        shards,
        mesh=mesh,
        in_specs=placed,
        out_specs=(P(None, "ty", "tx"), P(None, "ty", "tx"), P(None, "ty", "tx")),
        check_vma=False,
    )
```

```python
import jax
import jax.numpy as jnp
from jax import lax
from jax.sharding import PartitionSpec as P
from jax.experimental import pallas as pl
from jax.experimental.pallas import tpu as pltpu

PATCH = 128
SHIFTS = 65
RADIUS = 32
WIN = 192
CAP = 2
ITERS_R = 3


SHARPNESS = 256.0
SPRING_RATE = 0.25
FLOW_RATE = 0.5
FLOW_UNIT = 8.0
EPSILON = 1e-05

HALF = PATCH // 2
PER = 2


def flow_kernel(tf_ref, w_ref, out_ref, wlo, whi, corr):
    cats = []
    for q in range(PER):
        wf = w_ref[q].astype(jnp.float32)
        wlo[q] = wf[:, 0:PATCH]
        whi[q] = jnp.zeros(whi.shape[1:], jnp.float32)
        whi[q, :, 0:WIN - HALF] = wf[:, HALF:WIN]
        cats.append(jnp.concatenate([tf_ref[q, 0:HALF, :], tf_ref[q, HALF:PATCH, :]], axis=1))
        corr[q] = jnp.zeros(corr.shape[1:], jnp.float32)
    for dy in range(SHIFTS):
        for q in range(PER):
            w_cat = jnp.concatenate(
                [whi[q, dy : dy + PATCH, :], wlo[q, dy : dy + PATCH, :]], axis=0
            ).astype(jnp.bfloat16)
            m = jnp.dot(cats[q], w_cat, preferred_element_type=jnp.float32)
            r = pltpu.roll(m, 0, axis=1, stride=1, stride_axis=0)
            corr[q, dy : dy + 1, :] = jnp.sum(r, axis=0, keepdims=True)
    for q in range(PER):
        _epilogue(tf_ref, w_ref, out_ref, corr, q)


def _epilogue(tf_ref, w_ref, out_ref, corr, q):
    wf = w_ref[q].astype(jnp.float32)
    tfv = tf_ref[q].astype(jnp.float32)
    c = corr[q]
    rows = lax.broadcasted_iota(jnp.int32, c.shape, 0)
    lanes = lax.broadcasted_iota(jnp.int32, c.shape, 1)
    valid = (rows < SHIFTS) & (lanes >= HALF - 1)
    e_t = jnp.sum(tfv * tfv, keepdims=True) / float(PATCH * PATCH)
    e_w = jnp.sum(wf * wf, keepdims=True) / float(WIN * WIN)
    denom = float(PATCH * PATCH) * jnp.sqrt((e_t + EPSILON) * (e_w + EPSILON))
    scores = SHARPNESS * c / denom
    scores = jnp.where(valid, scores, -jnp.inf)
    mx = jnp.max(scores, keepdims=True)
    e = jnp.where(valid, jnp.exp(scores - mx), 0.0)
    w = e / jnp.sum(e, keepdims=True)
    sy = (rows - RADIUS).astype(jnp.float32)
    sx = (lanes - (HALF - 1) - RADIUS).astype(jnp.float32)
    fy = jnp.sum(w * sy, keepdims=True) / FLOW_UNIT
    fx = jnp.sum(w * sx, keepdims=True) / FLOW_UNIT
    orow = lax.broadcasted_iota(jnp.int32, (8, 128), 0)
    out_ref[q] = jnp.where(orow == 0, fy, jnp.where(orow == 1, fx, 0.0))

def flows_of(tflipped, windows):
    n = tflipped.shape[0]
    out = pl.pallas_call(
        flow_kernel,
        grid=(n // PER,),
        in_specs=[pl.BlockSpec((PER, PATCH, PATCH), lambda i: (i, 0, 0)),
                  pl.BlockSpec((PER, WIN, WIN), lambda i: (i, 0, 0))],
        out_specs=pl.BlockSpec((PER, 8, 128), lambda i: (i, 0, 0)),
        out_shape=jax.ShapeDtypeStruct((n, 8, 128), jnp.float32),
        scratch_shapes=[pltpu.VMEM((PER, WIN, PATCH), jnp.float32),
                        pltpu.VMEM((PER, WIN, PATCH), jnp.float32),
                        pltpu.VMEM((PER, 72, PATCH), jnp.float32)],
    )(tflipped, windows)
    return out[:, 0:2, 0].T


def padded_2(cells, sides, width):
    for axis, dim in sides:
        count = lax.axis_size(axis)
        ends = count - 1
        head = lax.slice_in_dim(cells, 0, width, axis=dim)
        tail = lax.slice_in_dim(cells, cells.shape[dim] - width, cells.shape[dim], axis=dim)
        cells = jnp.concatenate(
            [
                lax.ppermute(tail, axis, [(i, (i + 1) % count) for i in range(ends)]),
                cells,
                lax.ppermute(head, axis, [((i + 1) % count, i) for i in range(ends)]),
            ],
            axis=dim,
        )
    return cells


def halo(cells, width):
    n_ty = lax.axis_size("ty")
    n_tx = lax.axis_size("tx")
    height, breadth = cells.shape[-2], cells.shape[-1]
    pieces = {}
    for dy in (-1, 0, 1):
        for dx in (-1, 0, 1):
            if dy == 0 and dx == 0:
                pieces[(dy, dx)] = cells
                continue
            rows = {-1: (height - width, height), 0: (0, height), 1: (0, width)}[dy]
            cols = {-1: (breadth - width, breadth), 0: (0, breadth), 1: (0, width)}[dx]
            part = cells[..., rows[0] : rows[1], cols[0] : cols[1]]
            pairs = []
            for i in range(n_ty):
                for j in range(n_tx):
                    si, sj = i + dy, j + dx
                    if 0 <= si < n_ty and 0 <= sj < n_tx:
                        pairs.append((si * n_tx + sj, i * n_tx + j))
            pieces[(dy, dx)] = lax.ppermute(part, ("ty", "tx"), pairs)
    bands = [
        jnp.concatenate([pieces[(dy, -1)], pieces[(dy, 0)], pieces[(dy, 1)]], axis=-1)
        for dy in (-1, 0, 1)
    ]
    return jnp.concatenate(bands, axis=-2)


def relax_sweep(padded, mask_pad, target, count):
    centre = padded[:, 1:-1, 1:-1]
    mask_c = mask_pad[1:-1, 1:-1]
    height = centre.shape[1]
    width = centre.shape[2]
    spring = jnp.zeros_like(centre)
    for row_step, col_step in ((0, 1), (2, 1), (1, 0), (1, 2)):
        nearby = padded[:, row_step : row_step + height, col_step : col_step + width]
        mask_n = mask_pad[row_step : row_step + height, col_step : col_step + width]
        spring = spring + mask_c * mask_n * (nearby - centre)
    return centre + SPRING_RATE * spring + FLOW_RATE * (target - count * centre)


def one_hot(starts, size, extent, flip=False):
    offs = jnp.arange(size, dtype=jnp.int32)
    if flip:
        offs = size - 1 - offs
    want = starts[:, None, None] + offs[None, :, None]
    return (want == jnp.arange(extent, dtype=jnp.int32)[None, None, :]).astype(jnp.bfloat16)


def shards(
    section_a, section_b, template_corner, template_slot, window_corner, window_slot, node_mask
):
    tile_size = section_a.shape[0]
    slot_count = lax.axis_size("tx") * CAP
    slot_ids = jnp.arange(slot_count, dtype=jnp.int32)
    owner_picker = template_slot[0][:, None] == slot_ids[None, :]
    source_picker = window_slot[0][:, None] == slot_ids[None, :]
    f32 = jnp.float32

    col_pick = one_hot(template_corner[1, 0], PATCH, section_a.shape[1], flip=True)
    row_pick = one_hot(template_corner[0, 0], PATCH, section_a.shape[0])
    by_col = jnp.einsum("krc,ac->kra", col_pick, section_a, preferred_element_type=f32)
    tflipped = jnp.einsum(
        "kra,kia->kri", by_col.astype(jnp.bfloat16), row_pick, preferred_element_type=f32
    ).astype(jnp.bfloat16)
    outgoing = jnp.einsum(
        "ks,kri->sri", owner_picker.astype(jnp.bfloat16), tflipped, preferred_element_type=f32
    ).astype(jnp.bfloat16)

    n_tx = lax.axis_size("tx")
    n_ty = lax.axis_size("ty")
    me_x = lax.axis_index("tx")
    tx_ids = jnp.arange(n_tx, dtype=jnp.int32)
    to_left = (tx_ids == me_x - 1)[:, None]
    to_right = (tx_ids == me_x + 1)[:, None]

    def side_payload(left, right):
        lf = left.reshape(1, -1)
        rf = right.reshape(1, -1)
        return jnp.where(to_left, lf, jnp.where(to_right, rf, jnp.zeros_like(lf)))

    def side_arrivals(got, shape):
        left = lax.dynamic_index_in_dim(got, jnp.maximum(me_x - 1, 0), axis=0, keepdims=False)
        right = lax.dynamic_index_in_dim(got, jnp.minimum(me_x + 1, n_tx - 1), axis=0, keepdims=False)
        left = jnp.where(me_x >= 1, left, jnp.zeros_like(left)).reshape(shape)
        right = jnp.where(me_x + 1 < n_tx, right, jnp.zeros_like(right)).reshape(shape)
        return left, right

    def rows_exchange(cells, width):
        count = n_ty
        height = cells.shape[-2]
        head = cells[..., 0:width, :]
        tail = cells[..., height - width : height, :]
        above = lax.ppermute(tail, "ty", [(i, i + 1) for i in range(count - 1)])
        below = lax.ppermute(head, "ty", [(i + 1, i) for i in range(count - 1)])
        return above, below

    node_rows, node_cols = node_mask.shape
    centre_y = (window_corner[0, 0] + PATCH // 2) * node_rows // tile_size
    centre_x = (window_corner[1, 0] + PATCH // 2) * node_cols // tile_size
    attach = (centre_y[:, None, None] == jnp.arange(node_rows, dtype=jnp.int32)[None, :, None]) & (
        centre_x[:, None, None] == jnp.arange(node_cols, dtype=jnp.int32)[None, None, :]
    )
    count = jnp.sum(attach.astype(f32), axis=0)
    mask = node_mask.astype(f32)
    w = ITERS_R
    arrived = lax.all_to_all(outgoing, "tx", split_axis=0, concat_axis=0, tiled=True)
    b_tall = padded_2(section_b, (("ty", 0),), RADIUS)
    b_wide = padded_2(b_tall.T, (("tx", 0),), RADIUS).T

    wrow_pick = one_hot(window_corner[0, 0], WIN, b_wide.shape[0])
    wcol_pick = one_hot(window_corner[1, 0], WIN, b_wide.shape[1])
    by_row = jnp.einsum("mra,ac->mrc", wrow_pick, b_wide, preferred_element_type=f32)
    windows = jnp.einsum(
        "mrc,msc->mrs", by_row.astype(jnp.bfloat16), wcol_pick, preferred_element_type=f32
    ).astype(jnp.bfloat16)
    matched = jnp.einsum(
        "ms,sri->mri", source_picker.astype(jnp.bfloat16), arrived, preferred_element_type=f32
    ).astype(jnp.bfloat16)

    flows = flows_of(matched, windows)
    source_flow = -flows

    target = jnp.sum(jnp.where(attach[None], source_flow[:, :, None, None], 0.0), axis=1)
    fields = jnp.concatenate([target, count[None], mask[None]], axis=0)
    returned = jnp.sum(jnp.where(source_picker[None], flows[:, :, None], 0.0), axis=1)
    lane = 128
    sides = side_payload(fields[:, :, 0:w], fields[:, :, node_cols - w :])
    flows_out = returned.reshape(2, n_tx, CAP).transpose(1, 0, 2).reshape(n_tx, -1)
    side_len = sides.shape[1]
    chunk = -(-(side_len + flows_out.shape[1]) // lane) * lane
    back = jnp.concatenate(
        [sides, flows_out, jnp.zeros((n_tx, chunk - side_len - flows_out.shape[1]), f32)], axis=1
    ).reshape(n_tx, chunk // lane, lane)
    came = lax.all_to_all(back, "tx", split_axis=0, concat_axis=0, tiled=True).reshape(n_tx, chunk)
    landed = came[:, side_len : side_len + 2 * CAP].reshape(n_tx, 2, CAP).transpose(1, 0, 2).reshape(2, -1)
    owner_flow = jnp.sum(jnp.where(owner_picker[None], landed[:, None, :], 0.0), axis=2)
    f_left, f_right = side_arrivals(came[:, 0:side_len], (fields.shape[0], node_rows, w))
    fields_tx = jnp.concatenate([f_left, fields, f_right], axis=2)
    f_above, f_below = rows_exchange(fields_tx, w)
    wide = jnp.concatenate([f_above, fields_tx, f_below], axis=1)

    displace = jnp.zeros((2,) + wide.shape[1:], f32)
    for sweep in range(ITERS_R):
        lo_m, hi_m = sweep, wide.shape[1] - sweep
        lo_t, hi_t = sweep + 1, wide.shape[1] - sweep - 1
        displace = relax_sweep(
            displace,
            wide[3, lo_m:hi_m, lo_m:hi_m],
            wide[0:2, lo_t:hi_t, lo_t:hi_t],
            wide[2, lo_t:hi_t, lo_t:hi_t],
        )
    return (owner_flow[:, None, :], source_flow[:, None, :], displace)


def solution(mesh):
    placed = (
        P("ty", "tx"),
        P("ty", "tx"),
        P(None, "ty", "tx"),
        P("ty", "tx"),
        P(None, "ty", "tx"),
        P("ty", "tx"),
        P("ty", "tx"),
    )
    return jax.shard_map(
        shards,
        mesh=mesh,
        in_specs=placed,
        out_specs=(P(None, "ty", "tx"), P(None, "ty", "tx"), P(None, "ty", "tx")),
        check_vma=False,
    )
```

```python
import jax
import jax.numpy as jnp
from jax import lax
from jax.sharding import PartitionSpec as P
from jax.experimental import pallas as pl
from jax.experimental.pallas import tpu as pltpu

PATCH = 128
SHIFTS = 65
RADIUS = 32
WIN = 192
CAP = 2
ITERS_R = 3


SHARPNESS = 256.0
SPRING_RATE = 0.25
FLOW_RATE = 0.5
FLOW_UNIT = 8.0
EPSILON = 1e-05

HALF = PATCH // 2
PER = 2


def flow_kernel(tf_ref, w_ref, out_ref, wlo, whi, corr):
    cats = []
    for q in range(PER):
        wf = w_ref[q].astype(jnp.float32)
        wlo[q] = wf[:, 0:PATCH]
        whi[q] = jnp.zeros(whi.shape[1:], jnp.float32)
        whi[q, :, 0:WIN - HALF] = wf[:, HALF:WIN]
        cats.append(jnp.concatenate([tf_ref[q, 0:HALF, :], tf_ref[q, HALF:PATCH, :]], axis=1))
        corr[q] = jnp.zeros(corr.shape[1:], jnp.float32)
    for dy in range(SHIFTS):
        for q in range(PER):
            w_cat = jnp.concatenate(
                [whi[q, dy : dy + PATCH, :], wlo[q, dy : dy + PATCH, :]], axis=0
            ).astype(jnp.bfloat16)
            m = jnp.dot(cats[q], w_cat, preferred_element_type=jnp.float32)
            r = pltpu.roll(m, 0, axis=1, stride=1, stride_axis=0)
            corr[q, dy : dy + 1, :] = jnp.sum(r, axis=0, keepdims=True)
    for q in range(PER):
        _epilogue(tf_ref, w_ref, out_ref, corr, q)


def _epilogue(tf_ref, w_ref, out_ref, corr, q):
    wf = w_ref[q].astype(jnp.float32)
    tfv = tf_ref[q].astype(jnp.float32)
    c = corr[q]
    rows = lax.broadcasted_iota(jnp.int32, c.shape, 0)
    lanes = lax.broadcasted_iota(jnp.int32, c.shape, 1)
    valid = (rows < SHIFTS) & (lanes >= HALF - 1)
    e_t = jnp.sum(tfv * tfv, keepdims=True) / float(PATCH * PATCH)
    e_w = jnp.sum(wf * wf, keepdims=True) / float(WIN * WIN)
    denom = float(PATCH * PATCH) * jnp.sqrt((e_t + EPSILON) * (e_w + EPSILON))
    scores = SHARPNESS * c / denom
    scores = jnp.where(valid, scores, -jnp.inf)
    mx = jnp.max(scores, keepdims=True)
    e = jnp.where(valid, jnp.exp(scores - mx), 0.0)
    w = e / jnp.sum(e, keepdims=True)
    sy = (rows - RADIUS).astype(jnp.float32)
    sx = (lanes - (HALF - 1) - RADIUS).astype(jnp.float32)
    fy = jnp.sum(w * sy, keepdims=True) / FLOW_UNIT
    fx = jnp.sum(w * sx, keepdims=True) / FLOW_UNIT
    orow = lax.broadcasted_iota(jnp.int32, (8, 128), 0)
    out_ref[q] = jnp.where(orow == 0, fy, jnp.where(orow == 1, fx, 0.0))

def flows_of(tflipped, windows):
    n = tflipped.shape[0]
    out = pl.pallas_call(
        flow_kernel,
        grid=(n // PER,),
        in_specs=[pl.BlockSpec((PER, PATCH, PATCH), lambda i: (i, 0, 0)),
                  pl.BlockSpec((PER, WIN, WIN), lambda i: (i, 0, 0))],
        out_specs=pl.BlockSpec((PER, 8, 128), lambda i: (i, 0, 0)),
        out_shape=jax.ShapeDtypeStruct((n, 8, 128), jnp.float32),
        scratch_shapes=[pltpu.VMEM((PER, WIN, PATCH), jnp.float32),
                        pltpu.VMEM((PER, WIN, PATCH), jnp.float32),
                        pltpu.VMEM((PER, 72, PATCH), jnp.float32)],
    )(tflipped, windows)
    return out[:, 0:2, 0].T


def padded_2(cells, sides, width):
    for axis, dim in sides:
        count = lax.axis_size(axis)
        ends = count - 1
        head = lax.slice_in_dim(cells, 0, width, axis=dim)
        tail = lax.slice_in_dim(cells, cells.shape[dim] - width, cells.shape[dim], axis=dim)
        cells = jnp.concatenate(
            [
                lax.ppermute(tail, axis, [(i, (i + 1) % count) for i in range(ends)]),
                cells,
                lax.ppermute(head, axis, [((i + 1) % count, i) for i in range(ends)]),
            ],
            axis=dim,
        )
    return cells


def halo(cells, width):
    n_ty = lax.axis_size("ty")
    n_tx = lax.axis_size("tx")
    height, breadth = cells.shape[-2], cells.shape[-1]
    pieces = {}
    for dy in (-1, 0, 1):
        for dx in (-1, 0, 1):
            if dy == 0 and dx == 0:
                pieces[(dy, dx)] = cells
                continue
            rows = {-1: (height - width, height), 0: (0, height), 1: (0, width)}[dy]
            cols = {-1: (breadth - width, breadth), 0: (0, breadth), 1: (0, width)}[dx]
            part = cells[..., rows[0] : rows[1], cols[0] : cols[1]]
            pairs = []
            for i in range(n_ty):
                for j in range(n_tx):
                    si, sj = i + dy, j + dx
                    if 0 <= si < n_ty and 0 <= sj < n_tx:
                        pairs.append((si * n_tx + sj, i * n_tx + j))
            pieces[(dy, dx)] = lax.ppermute(part, ("ty", "tx"), pairs)
    bands = [
        jnp.concatenate([pieces[(dy, -1)], pieces[(dy, 0)], pieces[(dy, 1)]], axis=-1)
        for dy in (-1, 0, 1)
    ]
    return jnp.concatenate(bands, axis=-2)


def relax_sweep(padded, mask_pad, target, count):
    centre = padded[:, 1:-1, 1:-1]
    mask_c = mask_pad[1:-1, 1:-1]
    height = centre.shape[1]
    width = centre.shape[2]
    spring = jnp.zeros_like(centre)
    for row_step, col_step in ((0, 1), (2, 1), (1, 0), (1, 2)):
        nearby = padded[:, row_step : row_step + height, col_step : col_step + width]
        mask_n = mask_pad[row_step : row_step + height, col_step : col_step + width]
        spring = spring + mask_c * mask_n * (nearby - centre)
    return centre + SPRING_RATE * spring + FLOW_RATE * (target - count * centre)


def one_hot(starts, size, extent, flip=False):
    offs = jnp.arange(size, dtype=jnp.int32)
    if flip:
        offs = size - 1 - offs
    want = starts[:, None, None] + offs[None, :, None]
    return (want == jnp.arange(extent, dtype=jnp.int32)[None, None, :]).astype(jnp.bfloat16)


def shards(
    section_a, section_b, template_corner, template_slot, window_corner, window_slot, node_mask
):
    tile_size = section_a.shape[0]
    slot_count = lax.axis_size("tx") * CAP
    slot_ids = jnp.arange(slot_count, dtype=jnp.int32)
    owner_picker = template_slot[0][:, None] == slot_ids[None, :]
    source_picker = window_slot[0][:, None] == slot_ids[None, :]
    f32 = jnp.float32

    col_pick = one_hot(template_corner[1, 0], PATCH, section_a.shape[1], flip=True)
    row_pick = one_hot(template_corner[0, 0], PATCH, section_a.shape[0])
    by_col = jnp.einsum("krc,ac->kra", col_pick, section_a, preferred_element_type=f32)
    tflipped = jnp.einsum(
        "kra,kia->kri", by_col.astype(jnp.bfloat16), row_pick, preferred_element_type=f32
    ).astype(jnp.bfloat16)
    outgoing = jnp.einsum(
        "ks,kri->sri", owner_picker.astype(jnp.bfloat16), tflipped, preferred_element_type=f32
    ).astype(jnp.bfloat16)

    n_tx = lax.axis_size("tx")
    n_ty = lax.axis_size("ty")
    me_x = lax.axis_index("tx")
    tx_ids = jnp.arange(n_tx, dtype=jnp.int32)
    to_left = (tx_ids == me_x - 1)[:, None]
    to_right = (tx_ids == me_x + 1)[:, None]

    def side_payload(left, right):
        lf = left.reshape(1, -1)
        rf = right.reshape(1, -1)
        return jnp.where(to_left, lf, jnp.where(to_right, rf, jnp.zeros_like(lf)))

    def side_arrivals(got, shape):
        left = lax.dynamic_index_in_dim(got, jnp.maximum(me_x - 1, 0), axis=0, keepdims=False)
        right = lax.dynamic_index_in_dim(got, jnp.minimum(me_x + 1, n_tx - 1), axis=0, keepdims=False)
        left = jnp.where(me_x >= 1, left, jnp.zeros_like(left)).reshape(shape)
        right = jnp.where(me_x + 1 < n_tx, right, jnp.zeros_like(right)).reshape(shape)
        return left, right

    def rows_exchange(cells, width):
        count = n_ty
        height = cells.shape[-2]
        head = cells[..., 0:width, :]
        tail = cells[..., height - width : height, :]
        above = lax.ppermute(tail, "ty", [(i, i + 1) for i in range(count - 1)])
        below = lax.ppermute(head, "ty", [(i + 1, i) for i in range(count - 1)])
        return above, below

    node_rows, node_cols = node_mask.shape
    centre_y = (window_corner[0, 0] + PATCH // 2) * node_rows // tile_size
    centre_x = (window_corner[1, 0] + PATCH // 2) * node_cols // tile_size
    attach = (centre_y[:, None, None] == jnp.arange(node_rows, dtype=jnp.int32)[None, :, None]) & (
        centre_x[:, None, None] == jnp.arange(node_cols, dtype=jnp.int32)[None, None, :]
    )
    count = jnp.sum(attach.astype(f32), axis=0)
    mask = node_mask.astype(f32)
    w = ITERS_R
    arrived = lax.all_to_all(outgoing, "tx", split_axis=0, concat_axis=0, tiled=True)
    b_tall = padded_2(section_b, (("ty", 0),), RADIUS)
    b_wide = padded_2(b_tall.T, (("tx", 0),), RADIUS).T

    wrow_pick = one_hot(window_corner[0, 0], WIN, b_wide.shape[0])
    wcol_pick = one_hot(window_corner[1, 0], WIN, b_wide.shape[1])
    by_row = jnp.einsum("mra,ac->mrc", wrow_pick, b_wide, preferred_element_type=f32)
    windows = jnp.einsum(
        "mrc,msc->mrs", by_row.astype(jnp.bfloat16), wcol_pick, preferred_element_type=f32
    ).astype(jnp.bfloat16)
    matched = jnp.einsum(
        "ms,sri->mri", source_picker.astype(jnp.bfloat16), arrived, preferred_element_type=f32
    ).astype(jnp.bfloat16)

    flows = flows_of(matched, windows)
    source_flow = -flows

    target = jnp.sum(jnp.where(attach[None], source_flow[:, :, None, None], 0.0), axis=1)
    fields = jnp.concatenate([target, count[None], mask[None]], axis=0)
    returned = jnp.sum(jnp.where(source_picker[None], flows[:, :, None], 0.0), axis=1)
    f_above, f_below = rows_exchange(fields, w)
    fields_ty = jnp.concatenate([f_above, fields, f_below], axis=1)
    lane = 128
    sides = side_payload(fields_ty[:, :, 0:w], fields_ty[:, :, node_cols - w :])
    flows_out = returned.reshape(2, n_tx, CAP).transpose(1, 0, 2).reshape(n_tx, -1)
    side_len = sides.shape[1]
    chunk = -(-(side_len + flows_out.shape[1]) // lane) * lane
    back = jnp.concatenate(
        [sides, flows_out, jnp.zeros((n_tx, chunk - side_len - flows_out.shape[1]), f32)], axis=1
    ).reshape(n_tx, chunk // lane, lane)
    came = lax.all_to_all(back, "tx", split_axis=0, concat_axis=0, tiled=True).reshape(n_tx, chunk)
    landed = came[:, side_len : side_len + 2 * CAP].reshape(n_tx, 2, CAP).transpose(1, 0, 2).reshape(2, -1)
    owner_flow = jnp.sum(jnp.where(owner_picker[None], landed[:, None, :], 0.0), axis=2)
    f_left, f_right = side_arrivals(came[:, 0:side_len], (fields.shape[0], fields_ty.shape[1], w))
    wide = jnp.concatenate([f_left, fields_ty, f_right], axis=2)

    displace = jnp.zeros((2,) + wide.shape[1:], f32)
    for sweep in range(ITERS_R):
        lo_m, hi_m = sweep, wide.shape[1] - sweep
        lo_t, hi_t = sweep + 1, wide.shape[1] - sweep - 1
        displace = relax_sweep(
            displace,
            wide[3, lo_m:hi_m, lo_m:hi_m],
            wide[0:2, lo_t:hi_t, lo_t:hi_t],
            wide[2, lo_t:hi_t, lo_t:hi_t],
        )
    return (owner_flow[:, None, :], source_flow[:, None, :], displace)


def solution(mesh):
    placed = (
        P("ty", "tx"),
        P("ty", "tx"),
        P(None, "ty", "tx"),
        P("ty", "tx"),
        P(None, "ty", "tx"),
        P("ty", "tx"),
        P("ty", "tx"),
    )
    return jax.shard_map(
        shards,
        mesh=mesh,
        in_specs=placed,
        out_specs=(P(None, "ty", "tx"), P(None, "ty", "tx"), P(None, "ty", "tx")),
        check_vma=False,
    )
```

```python
import jax
import jax.numpy as jnp
from jax import lax
from jax.sharding import PartitionSpec as P
from jax.experimental import pallas as pl
from jax.experimental.pallas import tpu as pltpu

PATCH = 128
SHIFTS = 65
RADIUS = 32
WIN = 192
CAP = 2
ITERS_R = 3


SHARPNESS = 256.0
SPRING_RATE = 0.25
FLOW_RATE = 0.5
FLOW_UNIT = 8.0
EPSILON = 1e-05

HALF = PATCH // 2
PER = 2


def flow_kernel(tf_ref, w_ref, out_ref, wlo, whi, corr):
    cats = []
    for q in range(PER):
        wf = w_ref[q].astype(jnp.float32)
        wlo[q] = wf[:, 0:PATCH]
        whi[q] = jnp.zeros(whi.shape[1:], jnp.float32)
        whi[q, :, 0:WIN - HALF] = wf[:, HALF:WIN]
        cats.append(jnp.concatenate([tf_ref[q, 0:HALF, :], tf_ref[q, HALF:PATCH, :]], axis=1))
        corr[q] = jnp.zeros(corr.shape[1:], jnp.float32)
    for dy in range(SHIFTS):
        for q in range(PER):
            w_cat = jnp.concatenate(
                [whi[q, dy : dy + PATCH, :], wlo[q, dy : dy + PATCH, :]], axis=0
            ).astype(jnp.bfloat16)
            m = jnp.dot(cats[q], w_cat, preferred_element_type=jnp.float32)
            r = pltpu.roll(m, 0, axis=1, stride=1, stride_axis=0)
            corr[q, dy : dy + 1, :] = jnp.sum(r, axis=0, keepdims=True)
    for q in range(PER):
        _epilogue(tf_ref, w_ref, out_ref, corr, q)


def _epilogue(tf_ref, w_ref, out_ref, corr, q):
    wf = w_ref[q].astype(jnp.float32)
    tfv = tf_ref[q].astype(jnp.float32)
    c = corr[q]
    rows = lax.broadcasted_iota(jnp.int32, c.shape, 0)
    lanes = lax.broadcasted_iota(jnp.int32, c.shape, 1)
    valid = (rows < SHIFTS) & (lanes >= HALF - 1)
    e_t = jnp.sum(tfv * tfv, keepdims=True) / float(PATCH * PATCH)
    e_w = jnp.sum(wf * wf, keepdims=True) / float(WIN * WIN)
    denom = float(PATCH * PATCH) * jnp.sqrt((e_t + EPSILON) * (e_w + EPSILON))
    scores = SHARPNESS * c / denom
    scores = jnp.where(valid, scores, -jnp.inf)
    mx = jnp.max(scores, keepdims=True)
    e = jnp.where(valid, jnp.exp(scores - mx), 0.0)
    w = e / jnp.sum(e, keepdims=True)
    sy = (rows - RADIUS).astype(jnp.float32)
    sx = (lanes - (HALF - 1) - RADIUS).astype(jnp.float32)
    fy = jnp.sum(w * sy, keepdims=True) / FLOW_UNIT
    fx = jnp.sum(w * sx, keepdims=True) / FLOW_UNIT
    orow = lax.broadcasted_iota(jnp.int32, (8, 128), 0)
    out_ref[q] = jnp.where(orow == 0, fy, jnp.where(orow == 1, fx, 0.0))

def flows_of(tflipped, windows):
    n = tflipped.shape[0]
    out = pl.pallas_call(
        flow_kernel,
        grid=(n // PER,),
        in_specs=[pl.BlockSpec((PER, PATCH, PATCH), lambda i: (i, 0, 0)),
                  pl.BlockSpec((PER, WIN, WIN), lambda i: (i, 0, 0))],
        out_specs=pl.BlockSpec((PER, 8, 128), lambda i: (i, 0, 0)),
        out_shape=jax.ShapeDtypeStruct((n, 8, 128), jnp.float32),
        scratch_shapes=[pltpu.VMEM((PER, WIN, PATCH), jnp.float32),
                        pltpu.VMEM((PER, WIN, PATCH), jnp.float32),
                        pltpu.VMEM((PER, 72, PATCH), jnp.float32)],
    )(tflipped, windows)
    return out[:, 0:2, 0].T


def padded_2(cells, sides, width):
    for axis, dim in sides:
        count = lax.axis_size(axis)
        ends = count - 1
        head = lax.slice_in_dim(cells, 0, width, axis=dim)
        tail = lax.slice_in_dim(cells, cells.shape[dim] - width, cells.shape[dim], axis=dim)
        cells = jnp.concatenate(
            [
                lax.ppermute(tail, axis, [(i, (i + 1) % count) for i in range(ends)]),
                cells,
                lax.ppermute(head, axis, [((i + 1) % count, i) for i in range(ends)]),
            ],
            axis=dim,
        )
    return cells


def halo(cells, width):
    n_ty = lax.axis_size("ty")
    n_tx = lax.axis_size("tx")
    height, breadth = cells.shape[-2], cells.shape[-1]
    pieces = {}
    for dy in (-1, 0, 1):
        for dx in (-1, 0, 1):
            if dy == 0 and dx == 0:
                pieces[(dy, dx)] = cells
                continue
            rows = {-1: (height - width, height), 0: (0, height), 1: (0, width)}[dy]
            cols = {-1: (breadth - width, breadth), 0: (0, breadth), 1: (0, width)}[dx]
            part = cells[..., rows[0] : rows[1], cols[0] : cols[1]]
            pairs = []
            for i in range(n_ty):
                for j in range(n_tx):
                    si, sj = i + dy, j + dx
                    if 0 <= si < n_ty and 0 <= sj < n_tx:
                        pairs.append((si * n_tx + sj, i * n_tx + j))
            pieces[(dy, dx)] = lax.ppermute(part, ("ty", "tx"), pairs)
    bands = [
        jnp.concatenate([pieces[(dy, -1)], pieces[(dy, 0)], pieces[(dy, 1)]], axis=-1)
        for dy in (-1, 0, 1)
    ]
    return jnp.concatenate(bands, axis=-2)


def relax_sweep(padded, mask_pad, target, count):
    centre = padded[:, 1:-1, 1:-1]
    mask_c = mask_pad[1:-1, 1:-1]
    height = centre.shape[1]
    width = centre.shape[2]
    spring = jnp.zeros_like(centre)
    for row_step, col_step in ((0, 1), (2, 1), (1, 0), (1, 2)):
        nearby = padded[:, row_step : row_step + height, col_step : col_step + width]
        mask_n = mask_pad[row_step : row_step + height, col_step : col_step + width]
        spring = spring + mask_c * mask_n * (nearby - centre)
    return centre + SPRING_RATE * spring + FLOW_RATE * (target - count * centre)


def one_hot(starts, size, extent, flip=False):
    offs = jnp.arange(size, dtype=jnp.int32)
    if flip:
        offs = size - 1 - offs
    want = starts[:, None, None] + offs[None, :, None]
    return (want == jnp.arange(extent, dtype=jnp.int32)[None, None, :]).astype(jnp.bfloat16)


def shards(
    section_a, section_b, template_corner, template_slot, window_corner, window_slot, node_mask
):
    tile_size = section_a.shape[0]
    slot_count = lax.axis_size("tx") * CAP
    slot_ids = jnp.arange(slot_count, dtype=jnp.int32)
    owner_picker = template_slot[0][:, None] == slot_ids[None, :]
    source_picker = window_slot[0][:, None] == slot_ids[None, :]
    f32 = jnp.float32

    col_pick = one_hot(template_corner[1, 0], PATCH, section_a.shape[1], flip=True)
    row_pick = one_hot(template_corner[0, 0], PATCH, section_a.shape[0])
    by_col = jnp.einsum("krc,ac->kra", col_pick, section_a, preferred_element_type=f32)
    tflipped = jnp.einsum(
        "kra,kia->kri", by_col.astype(jnp.bfloat16), row_pick, preferred_element_type=f32
    ).astype(jnp.bfloat16)
    outgoing = jnp.einsum(
        "ks,kri->sri", owner_picker.astype(jnp.bfloat16), tflipped, preferred_element_type=f32
    ).astype(jnp.bfloat16)

    n_tx = lax.axis_size("tx")
    n_ty = lax.axis_size("ty")
    me_x = lax.axis_index("tx")
    tx_ids = jnp.arange(n_tx, dtype=jnp.int32)
    to_left = (tx_ids == me_x - 1)[:, None]
    to_right = (tx_ids == me_x + 1)[:, None]

    def side_payload(left, right):
        lf = left.reshape(1, -1)
        rf = right.reshape(1, -1)
        return jnp.where(to_left, lf, jnp.where(to_right, rf, jnp.zeros_like(lf)))

    def side_arrivals(got, shape):
        left = lax.dynamic_index_in_dim(got, jnp.maximum(me_x - 1, 0), axis=0, keepdims=False)
        right = lax.dynamic_index_in_dim(got, jnp.minimum(me_x + 1, n_tx - 1), axis=0, keepdims=False)
        left = jnp.where(me_x >= 1, left, jnp.zeros_like(left)).reshape(shape)
        right = jnp.where(me_x + 1 < n_tx, right, jnp.zeros_like(right)).reshape(shape)
        return left, right

    def rows_exchange(cells, width):
        count = n_ty
        height = cells.shape[-2]
        head = cells[..., 0:width, :]
        tail = cells[..., height - width : height, :]
        above = lax.ppermute(tail, "ty", [(i, i + 1) for i in range(count - 1)])
        below = lax.ppermute(head, "ty", [(i + 1, i) for i in range(count - 1)])
        return above, below

    node_rows, node_cols = node_mask.shape
    centre_y = (window_corner[0, 0] + PATCH // 2) * node_rows // tile_size
    centre_x = (window_corner[1, 0] + PATCH // 2) * node_cols // tile_size
    attach = (centre_y[:, None, None] == jnp.arange(node_rows, dtype=jnp.int32)[None, :, None]) & (
        centre_x[:, None, None] == jnp.arange(node_cols, dtype=jnp.int32)[None, None, :]
    )
    count = jnp.sum(attach.astype(f32), axis=0)
    mask = node_mask.astype(f32)
    w = ITERS_R
    arrived = lax.all_to_all(outgoing, "tx", split_axis=0, concat_axis=0, tiled=True)
    b_tall = padded_2(section_b, (("ty", 0),), RADIUS)
    b_wide = padded_2(b_tall.T, (("tx", 0),), RADIUS).T

    wrow_pick = one_hot(window_corner[0, 0], WIN, b_wide.shape[0])
    wcol_pick = one_hot(window_corner[1, 0], WIN, b_wide.shape[1])
    by_col = jnp.einsum("ac,msc->mas", b_wide, wcol_pick, preferred_element_type=f32)
    windows = jnp.einsum(
        "mra,mas->mrs", wrow_pick, by_col.astype(jnp.bfloat16), preferred_element_type=f32
    ).astype(jnp.bfloat16)
    matched = jnp.einsum(
        "ms,sri->mri", source_picker.astype(jnp.bfloat16), arrived, preferred_element_type=f32
    ).astype(jnp.bfloat16)

    flows = flows_of(matched, windows)
    source_flow = -flows

    target = jnp.sum(jnp.where(attach[None], source_flow[:, :, None, None], 0.0), axis=1)
    fields = jnp.concatenate([target, count[None], mask[None]], axis=0)
    returned = jnp.sum(jnp.where(source_picker[None], flows[:, :, None], 0.0), axis=1)
    lane = 128
    sides = side_payload(fields[:, :, 0:w], fields[:, :, node_cols - w :])
    flows_out = returned.reshape(2, n_tx, CAP).transpose(1, 0, 2).reshape(n_tx, -1)
    side_len = sides.shape[1]
    chunk = -(-(side_len + flows_out.shape[1]) // lane) * lane
    back = jnp.concatenate(
        [sides, flows_out, jnp.zeros((n_tx, chunk - side_len - flows_out.shape[1]), f32)], axis=1
    ).reshape(n_tx, chunk // lane, lane)
    came = lax.all_to_all(back, "tx", split_axis=0, concat_axis=0, tiled=True).reshape(n_tx, chunk)
    landed = came[:, side_len : side_len + 2 * CAP].reshape(n_tx, 2, CAP).transpose(1, 0, 2).reshape(2, -1)
    owner_flow = jnp.sum(jnp.where(owner_picker[None], landed[:, None, :], 0.0), axis=2)
    f_left, f_right = side_arrivals(came[:, 0:side_len], (fields.shape[0], node_rows, w))
    fields_tx = jnp.concatenate([f_left, fields, f_right], axis=2)
    f_above, f_below = rows_exchange(fields_tx, w)
    wide = jnp.concatenate([f_above, fields_tx, f_below], axis=1)

    displace = jnp.zeros((2,) + wide.shape[1:], f32)
    for sweep in range(ITERS_R):
        lo_m, hi_m = sweep, wide.shape[1] - sweep
        lo_t, hi_t = sweep + 1, wide.shape[1] - sweep - 1
        displace = relax_sweep(
            displace,
            wide[3, lo_m:hi_m, lo_m:hi_m],
            wide[0:2, lo_t:hi_t, lo_t:hi_t],
            wide[2, lo_t:hi_t, lo_t:hi_t],
        )
    return (owner_flow[:, None, :], source_flow[:, None, :], displace)


def solution(mesh):
    placed = (
        P("ty", "tx"),
        P("ty", "tx"),
        P(None, "ty", "tx"),
        P("ty", "tx"),
        P(None, "ty", "tx"),
        P("ty", "tx"),
        P("ty", "tx"),
    )
    return jax.shard_map(
        shards,
        mesh=mesh,
        in_specs=placed,
        out_specs=(P(None, "ty", "tx"), P(None, "ty", "tx"), P(None, "ty", "tx")),
        check_vma=False,
    )
```

```python
import jax
import jax.numpy as jnp
from jax import lax
from jax.sharding import PartitionSpec as P
from jax.experimental import pallas as pl
from jax.experimental.pallas import tpu as pltpu

PATCH = 128
SHIFTS = 65
RADIUS = 32
WIN = 192
CAP = 2
ITERS_R = 3


SHARPNESS = 256.0
SPRING_RATE = 0.25
FLOW_RATE = 0.5
FLOW_UNIT = 8.0
EPSILON = 1e-05

HALF = PATCH // 2
PER = 2


def flow_kernel(tf_ref, w_ref, out_ref, wlo, whi, corr):
    cats = []
    for q in range(PER):
        wf = w_ref[q].astype(jnp.float32)
        wlo[q] = wf[:, 0:PATCH]
        whi[q] = jnp.zeros(whi.shape[1:], jnp.float32)
        whi[q, :, 0:WIN - HALF] = wf[:, HALF:WIN]
        cats.append(jnp.concatenate([tf_ref[q, 0:HALF, :], tf_ref[q, HALF:PATCH, :]], axis=1))
        corr[q] = jnp.zeros(corr.shape[1:], jnp.float32)
    for dy in range(SHIFTS):
        for q in range(PER):
            w_cat = jnp.concatenate(
                [whi[q, dy : dy + PATCH, :], wlo[q, dy : dy + PATCH, :]], axis=0
            ).astype(jnp.bfloat16)
            m = jnp.dot(cats[q], w_cat, preferred_element_type=jnp.float32)
            r = pltpu.roll(m, 0, axis=1, stride=1, stride_axis=0)
            corr[q, dy : dy + 1, :] = jnp.sum(r, axis=0, keepdims=True)
    for q in range(PER):
        _epilogue(tf_ref, w_ref, out_ref, corr, q)


def _epilogue(tf_ref, w_ref, out_ref, corr, q):
    wf = w_ref[q].astype(jnp.float32)
    tfv = tf_ref[q].astype(jnp.float32)
    c = corr[q]
    rows = lax.broadcasted_iota(jnp.int32, c.shape, 0)
    lanes = lax.broadcasted_iota(jnp.int32, c.shape, 1)
    valid = (rows < SHIFTS) & (lanes >= HALF - 1)
    e_t = jnp.sum(tfv * tfv, keepdims=True) / float(PATCH * PATCH)
    e_w = jnp.sum(wf * wf, keepdims=True) / float(WIN * WIN)
    denom = float(PATCH * PATCH) * jnp.sqrt((e_t + EPSILON) * (e_w + EPSILON))
    scores = SHARPNESS * c / denom
    scores = jnp.where(valid, scores, -jnp.inf)
    mx = jnp.max(scores, keepdims=True)
    e = jnp.where(valid, jnp.exp(scores - mx), 0.0)
    w = e / jnp.sum(e, keepdims=True)
    sy = (rows - RADIUS).astype(jnp.float32)
    sx = (lanes - (HALF - 1) - RADIUS).astype(jnp.float32)
    fy = jnp.sum(w * sy, keepdims=True) / FLOW_UNIT
    fx = jnp.sum(w * sx, keepdims=True) / FLOW_UNIT
    orow = lax.broadcasted_iota(jnp.int32, (8, 128), 0)
    out_ref[q] = jnp.where(orow == 0, fy, jnp.where(orow == 1, fx, 0.0))

def flows_of(tflipped, windows):
    n = tflipped.shape[0]
    out = pl.pallas_call(
        flow_kernel,
        grid=(n // PER,),
        in_specs=[pl.BlockSpec((PER, PATCH, PATCH), lambda i: (i, 0, 0)),
                  pl.BlockSpec((PER, WIN, WIN), lambda i: (i, 0, 0))],
        out_specs=pl.BlockSpec((PER, 8, 128), lambda i: (i, 0, 0)),
        out_shape=jax.ShapeDtypeStruct((n, 8, 128), jnp.float32),
        scratch_shapes=[pltpu.VMEM((PER, WIN, PATCH), jnp.float32),
                        pltpu.VMEM((PER, WIN, PATCH), jnp.float32),
                        pltpu.VMEM((PER, 72, PATCH), jnp.float32)],
    )(tflipped, windows)
    return out[:, 0:2, 0].T


def padded_2(cells, sides, width):
    for axis, dim in sides:
        count = lax.axis_size(axis)
        ends = count - 1
        head = lax.slice_in_dim(cells, 0, width, axis=dim)
        tail = lax.slice_in_dim(cells, cells.shape[dim] - width, cells.shape[dim], axis=dim)
        cells = jnp.concatenate(
            [
                lax.ppermute(tail, axis, [(i, (i + 1) % count) for i in range(ends)]),
                cells,
                lax.ppermute(head, axis, [((i + 1) % count, i) for i in range(ends)]),
            ],
            axis=dim,
        )
    return cells


def halo(cells, width):
    n_ty = lax.axis_size("ty")
    n_tx = lax.axis_size("tx")
    height, breadth = cells.shape[-2], cells.shape[-1]
    pieces = {}
    for dy in (-1, 0, 1):
        for dx in (-1, 0, 1):
            if dy == 0 and dx == 0:
                pieces[(dy, dx)] = cells
                continue
            rows = {-1: (height - width, height), 0: (0, height), 1: (0, width)}[dy]
            cols = {-1: (breadth - width, breadth), 0: (0, breadth), 1: (0, width)}[dx]
            part = cells[..., rows[0] : rows[1], cols[0] : cols[1]]
            pairs = []
            for i in range(n_ty):
                for j in range(n_tx):
                    si, sj = i + dy, j + dx
                    if 0 <= si < n_ty and 0 <= sj < n_tx:
                        pairs.append((si * n_tx + sj, i * n_tx + j))
            pieces[(dy, dx)] = lax.ppermute(part, ("ty", "tx"), pairs)
    bands = [
        jnp.concatenate([pieces[(dy, -1)], pieces[(dy, 0)], pieces[(dy, 1)]], axis=-1)
        for dy in (-1, 0, 1)
    ]
    return jnp.concatenate(bands, axis=-2)


def relax_sweep(padded, mask_pad, target, count):
    centre = padded[:, 1:-1, 1:-1]
    mask_c = mask_pad[1:-1, 1:-1]
    height = centre.shape[1]
    width = centre.shape[2]
    spring = jnp.zeros_like(centre)
    for row_step, col_step in ((0, 1), (2, 1), (1, 0), (1, 2)):
        nearby = padded[:, row_step : row_step + height, col_step : col_step + width]
        mask_n = mask_pad[row_step : row_step + height, col_step : col_step + width]
        spring = spring + mask_c * mask_n * (nearby - centre)
    return centre + SPRING_RATE * spring + FLOW_RATE * (target - count * centre)


def one_hot(starts, size, extent, flip=False):
    offs = jnp.arange(size, dtype=jnp.int32)
    if flip:
        offs = size - 1 - offs
    want = starts[:, None, None] + offs[None, :, None]
    return (want == jnp.arange(extent, dtype=jnp.int32)[None, None, :]).astype(jnp.bfloat16)


def shards(
    section_a, section_b, template_corner, template_slot, window_corner, window_slot, node_mask
):
    tile_size = section_a.shape[0]
    slot_count = lax.axis_size("tx") * CAP
    slot_ids = jnp.arange(slot_count, dtype=jnp.int32)
    owner_picker = template_slot[0][:, None] == slot_ids[None, :]
    source_picker = window_slot[0][:, None] == slot_ids[None, :]
    f32 = jnp.float32

    slot_has = jnp.any(owner_picker, axis=0)
    no_col = section_a.shape[1] + PATCH
    slot_top = jnp.sum(jnp.where(owner_picker, template_corner[0, 0][:, None], 0), axis=0)
    slot_left = jnp.sum(jnp.where(owner_picker, template_corner[1, 0][:, None], 0), axis=0)
    slot_left = jnp.where(slot_has, slot_left, no_col)
    col_pick = one_hot(slot_left, PATCH, section_a.shape[1], flip=True)
    row_pick = one_hot(slot_top, PATCH, section_a.shape[0])
    by_col = jnp.einsum("src,ac->sra", col_pick, section_a, preferred_element_type=f32)
    outgoing = jnp.einsum(
        "sra,sia->sri", by_col.astype(jnp.bfloat16), row_pick, preferred_element_type=f32
    ).astype(jnp.bfloat16)

    n_tx = lax.axis_size("tx")
    n_ty = lax.axis_size("ty")
    me_x = lax.axis_index("tx")
    tx_ids = jnp.arange(n_tx, dtype=jnp.int32)
    to_left = (tx_ids == me_x - 1)[:, None]
    to_right = (tx_ids == me_x + 1)[:, None]

    def side_payload(left, right):
        lf = left.reshape(1, -1)
        rf = right.reshape(1, -1)
        return jnp.where(to_left, lf, jnp.where(to_right, rf, jnp.zeros_like(lf)))

    def side_arrivals(got, shape):
        left = lax.dynamic_index_in_dim(got, jnp.maximum(me_x - 1, 0), axis=0, keepdims=False)
        right = lax.dynamic_index_in_dim(got, jnp.minimum(me_x + 1, n_tx - 1), axis=0, keepdims=False)
        left = jnp.where(me_x >= 1, left, jnp.zeros_like(left)).reshape(shape)
        right = jnp.where(me_x + 1 < n_tx, right, jnp.zeros_like(right)).reshape(shape)
        return left, right

    def rows_exchange(cells, width):
        count = n_ty
        height = cells.shape[-2]
        head = cells[..., 0:width, :]
        tail = cells[..., height - width : height, :]
        above = lax.ppermute(tail, "ty", [(i, i + 1) for i in range(count - 1)])
        below = lax.ppermute(head, "ty", [(i + 1, i) for i in range(count - 1)])
        return above, below

    node_rows, node_cols = node_mask.shape
    centre_y = (window_corner[0, 0] + PATCH // 2) * node_rows // tile_size
    centre_x = (window_corner[1, 0] + PATCH // 2) * node_cols // tile_size
    attach = (centre_y[:, None, None] == jnp.arange(node_rows, dtype=jnp.int32)[None, :, None]) & (
        centre_x[:, None, None] == jnp.arange(node_cols, dtype=jnp.int32)[None, None, :]
    )
    count = jnp.sum(attach.astype(f32), axis=0)
    mask = node_mask.astype(f32)
    w = ITERS_R
    arrived = lax.all_to_all(outgoing, "tx", split_axis=0, concat_axis=0, tiled=True)
    b_tall = padded_2(section_b, (("ty", 0),), RADIUS)
    b_wide = padded_2(b_tall.T, (("tx", 0),), RADIUS).T

    wrow_pick = one_hot(window_corner[0, 0], WIN, b_wide.shape[0])
    wcol_pick = one_hot(window_corner[1, 0], WIN, b_wide.shape[1])
    by_row = jnp.einsum("mra,ac->mrc", wrow_pick, b_wide, preferred_element_type=f32)
    windows = jnp.einsum(
        "mrc,msc->mrs", by_row.astype(jnp.bfloat16), wcol_pick, preferred_element_type=f32
    ).astype(jnp.bfloat16)
    matched = jnp.einsum(
        "ms,sri->mri", source_picker.astype(jnp.bfloat16), arrived, preferred_element_type=f32
    ).astype(jnp.bfloat16)

    flows = flows_of(matched, windows)
    source_flow = -flows

    target = jnp.sum(jnp.where(attach[None], source_flow[:, :, None, None], 0.0), axis=1)
    fields = jnp.concatenate([target, count[None], mask[None]], axis=0)
    returned = jnp.sum(jnp.where(source_picker[None], flows[:, :, None], 0.0), axis=1)
    lane = 128
    sides = side_payload(fields[:, :, 0:w], fields[:, :, node_cols - w :])
    flows_out = returned.reshape(2, n_tx, CAP).transpose(1, 0, 2).reshape(n_tx, -1)
    side_len = sides.shape[1]
    chunk = -(-(side_len + flows_out.shape[1]) // lane) * lane
    back = jnp.concatenate(
        [sides, flows_out, jnp.zeros((n_tx, chunk - side_len - flows_out.shape[1]), f32)], axis=1
    ).reshape(n_tx, chunk // lane, lane)
    came = lax.all_to_all(back, "tx", split_axis=0, concat_axis=0, tiled=True).reshape(n_tx, chunk)
    landed = came[:, side_len : side_len + 2 * CAP].reshape(n_tx, 2, CAP).transpose(1, 0, 2).reshape(2, -1)
    owner_flow = jnp.sum(jnp.where(owner_picker[None], landed[:, None, :], 0.0), axis=2)
    f_left, f_right = side_arrivals(came[:, 0:side_len], (fields.shape[0], node_rows, w))
    fields_tx = jnp.concatenate([f_left, fields, f_right], axis=2)
    f_above, f_below = rows_exchange(fields_tx, w)
    wide = jnp.concatenate([f_above, fields_tx, f_below], axis=1)

    displace = jnp.zeros((2,) + wide.shape[1:], f32)
    for sweep in range(ITERS_R):
        lo_m, hi_m = sweep, wide.shape[1] - sweep
        lo_t, hi_t = sweep + 1, wide.shape[1] - sweep - 1
        displace = relax_sweep(
            displace,
            wide[3, lo_m:hi_m, lo_m:hi_m],
            wide[0:2, lo_t:hi_t, lo_t:hi_t],
            wide[2, lo_t:hi_t, lo_t:hi_t],
        )
    return (owner_flow[:, None, :], source_flow[:, None, :], displace)


def solution(mesh):
    placed = (
        P("ty", "tx"),
        P("ty", "tx"),
        P(None, "ty", "tx"),
        P("ty", "tx"),
        P(None, "ty", "tx"),
        P("ty", "tx"),
        P("ty", "tx"),
    )
    return jax.shard_map(
        shards,
        mesh=mesh,
        in_specs=placed,
        out_specs=(P(None, "ty", "tx"), P(None, "ty", "tx"), P(None, "ty", "tx")),
        check_vma=False,
    )
```

```python
import jax
import jax.numpy as jnp
from jax import lax
from jax.sharding import PartitionSpec as P
from jax.experimental import pallas as pl
from jax.experimental.pallas import tpu as pltpu

PATCH = 128
SHIFTS = 65
RADIUS = 32
WIN = 192
CAP = 2
ITERS_R = 3


SHARPNESS = 256.0
SPRING_RATE = 0.25
FLOW_RATE = 0.5
FLOW_UNIT = 8.0
EPSILON = 1e-05

HALF = PATCH // 2
PER = 4


def flow_kernel(tf_ref, w_ref, out_ref, wlo, whi, corr):
    cats = []
    for q in range(PER):
        wf = w_ref[q].astype(jnp.float32)
        wlo[q] = wf[:, 0:PATCH]
        whi[q] = jnp.zeros(whi.shape[1:], jnp.float32)
        whi[q, :, 0:WIN - HALF] = wf[:, HALF:WIN]
        cats.append(jnp.concatenate([tf_ref[q, 0:HALF, :], tf_ref[q, HALF:PATCH, :]], axis=1))
        corr[q] = jnp.zeros(corr.shape[1:], jnp.float32)
    for dy in range(SHIFTS):
        for q in range(PER):
            w_cat = jnp.concatenate(
                [whi[q, dy : dy + PATCH, :], wlo[q, dy : dy + PATCH, :]], axis=0
            ).astype(jnp.bfloat16)
            m = jnp.dot(cats[q], w_cat, preferred_element_type=jnp.float32)
            r = pltpu.roll(m, 0, axis=1, stride=1, stride_axis=0)
            corr[q, dy : dy + 1, :] = jnp.sum(r, axis=0, keepdims=True)
    for q in range(PER):
        _epilogue(tf_ref, w_ref, out_ref, corr, q)


def _epilogue(tf_ref, w_ref, out_ref, corr, q):
    wf = w_ref[q].astype(jnp.float32)
    tfv = tf_ref[q].astype(jnp.float32)
    c = corr[q]
    rows = lax.broadcasted_iota(jnp.int32, c.shape, 0)
    lanes = lax.broadcasted_iota(jnp.int32, c.shape, 1)
    valid = (rows < SHIFTS) & (lanes >= HALF - 1)
    e_t = jnp.sum(tfv * tfv, keepdims=True) / float(PATCH * PATCH)
    e_w = jnp.sum(wf * wf, keepdims=True) / float(WIN * WIN)
    denom = float(PATCH * PATCH) * jnp.sqrt((e_t + EPSILON) * (e_w + EPSILON))
    scores = SHARPNESS * c / denom
    scores = jnp.where(valid, scores, -jnp.inf)
    mx = jnp.max(scores, keepdims=True)
    e = jnp.where(valid, jnp.exp(scores - mx), 0.0)
    w = e / jnp.sum(e, keepdims=True)
    sy = (rows - RADIUS).astype(jnp.float32)
    sx = (lanes - (HALF - 1) - RADIUS).astype(jnp.float32)
    fy = jnp.sum(w * sy, keepdims=True) / FLOW_UNIT
    fx = jnp.sum(w * sx, keepdims=True) / FLOW_UNIT
    orow = lax.broadcasted_iota(jnp.int32, (8, 128), 0)
    out_ref[q] = jnp.where(orow == 0, fy, jnp.where(orow == 1, fx, 0.0))

def flows_of(tflipped, windows):
    n = tflipped.shape[0]
    out = pl.pallas_call(
        flow_kernel,
        grid=(n // PER,),
        in_specs=[pl.BlockSpec((PER, PATCH, PATCH), lambda i: (i, 0, 0)),
                  pl.BlockSpec((PER, WIN, WIN), lambda i: (i, 0, 0))],
        out_specs=pl.BlockSpec((PER, 8, 128), lambda i: (i, 0, 0)),
        out_shape=jax.ShapeDtypeStruct((n, 8, 128), jnp.float32),
        scratch_shapes=[pltpu.VMEM((PER, WIN, PATCH), jnp.float32),
                        pltpu.VMEM((PER, WIN, PATCH), jnp.float32),
                        pltpu.VMEM((PER, 72, PATCH), jnp.float32)],
    )(tflipped, windows)
    return out[:, 0:2, 0].T


def padded_2(cells, sides, width):
    for axis, dim in sides:
        count = lax.axis_size(axis)
        ends = count - 1
        head = lax.slice_in_dim(cells, 0, width, axis=dim)
        tail = lax.slice_in_dim(cells, cells.shape[dim] - width, cells.shape[dim], axis=dim)
        cells = jnp.concatenate(
            [
                lax.ppermute(tail, axis, [(i, (i + 1) % count) for i in range(ends)]),
                cells,
                lax.ppermute(head, axis, [((i + 1) % count, i) for i in range(ends)]),
            ],
            axis=dim,
        )
    return cells


def halo(cells, width):
    n_ty = lax.axis_size("ty")
    n_tx = lax.axis_size("tx")
    height, breadth = cells.shape[-2], cells.shape[-1]
    pieces = {}
    for dy in (-1, 0, 1):
        for dx in (-1, 0, 1):
            if dy == 0 and dx == 0:
                pieces[(dy, dx)] = cells
                continue
            rows = {-1: (height - width, height), 0: (0, height), 1: (0, width)}[dy]
            cols = {-1: (breadth - width, breadth), 0: (0, breadth), 1: (0, width)}[dx]
            part = cells[..., rows[0] : rows[1], cols[0] : cols[1]]
            pairs = []
            for i in range(n_ty):
                for j in range(n_tx):
                    si, sj = i + dy, j + dx
                    if 0 <= si < n_ty and 0 <= sj < n_tx:
                        pairs.append((si * n_tx + sj, i * n_tx + j))
            pieces[(dy, dx)] = lax.ppermute(part, ("ty", "tx"), pairs)
    bands = [
        jnp.concatenate([pieces[(dy, -1)], pieces[(dy, 0)], pieces[(dy, 1)]], axis=-1)
        for dy in (-1, 0, 1)
    ]
    return jnp.concatenate(bands, axis=-2)


def relax_sweep(padded, mask_pad, target, count):
    centre = padded[:, 1:-1, 1:-1]
    mask_c = mask_pad[1:-1, 1:-1]
    height = centre.shape[1]
    width = centre.shape[2]
    spring = jnp.zeros_like(centre)
    for row_step, col_step in ((0, 1), (2, 1), (1, 0), (1, 2)):
        nearby = padded[:, row_step : row_step + height, col_step : col_step + width]
        mask_n = mask_pad[row_step : row_step + height, col_step : col_step + width]
        spring = spring + mask_c * mask_n * (nearby - centre)
    return centre + SPRING_RATE * spring + FLOW_RATE * (target - count * centre)


def one_hot(starts, size, extent, flip=False):
    offs = jnp.arange(size, dtype=jnp.int32)
    if flip:
        offs = size - 1 - offs
    want = starts[:, None, None] + offs[None, :, None]
    return (want == jnp.arange(extent, dtype=jnp.int32)[None, None, :]).astype(jnp.bfloat16)


def shards(
    section_a, section_b, template_corner, template_slot, window_corner, window_slot, node_mask
):
    tile_size = section_a.shape[0]
    slot_count = lax.axis_size("tx") * CAP
    slot_ids = jnp.arange(slot_count, dtype=jnp.int32)
    owner_picker = template_slot[0][:, None] == slot_ids[None, :]
    source_picker = window_slot[0][:, None] == slot_ids[None, :]
    f32 = jnp.float32

    col_pick = one_hot(template_corner[1, 0], PATCH, section_a.shape[1], flip=True)
    row_pick = one_hot(template_corner[0, 0], PATCH, section_a.shape[0])
    by_col = jnp.einsum("krc,ac->kra", col_pick, section_a, preferred_element_type=f32)
    tflipped = jnp.einsum(
        "kra,kia->kri", by_col.astype(jnp.bfloat16), row_pick, preferred_element_type=f32
    ).astype(jnp.bfloat16)
    outgoing = jnp.einsum(
        "ks,kri->sri", owner_picker.astype(jnp.bfloat16), tflipped, preferred_element_type=f32
    ).astype(jnp.bfloat16)

    n_tx = lax.axis_size("tx")
    n_ty = lax.axis_size("ty")
    me_x = lax.axis_index("tx")
    tx_ids = jnp.arange(n_tx, dtype=jnp.int32)
    to_left = (tx_ids == me_x - 1)[:, None]
    to_right = (tx_ids == me_x + 1)[:, None]

    def side_payload(left, right):
        lf = left.reshape(1, -1)
        rf = right.reshape(1, -1)
        return jnp.where(to_left, lf, jnp.where(to_right, rf, jnp.zeros_like(lf)))

    def side_arrivals(got, shape):
        left = lax.dynamic_index_in_dim(got, jnp.maximum(me_x - 1, 0), axis=0, keepdims=False)
        right = lax.dynamic_index_in_dim(got, jnp.minimum(me_x + 1, n_tx - 1), axis=0, keepdims=False)
        left = jnp.where(me_x >= 1, left, jnp.zeros_like(left)).reshape(shape)
        right = jnp.where(me_x + 1 < n_tx, right, jnp.zeros_like(right)).reshape(shape)
        return left, right

    def rows_exchange(cells, width):
        count = n_ty
        height = cells.shape[-2]
        head = cells[..., 0:width, :]
        tail = cells[..., height - width : height, :]
        above = lax.ppermute(tail, "ty", [(i, i + 1) for i in range(count - 1)])
        below = lax.ppermute(head, "ty", [(i + 1, i) for i in range(count - 1)])
        return above, below

    node_rows, node_cols = node_mask.shape
    centre_y = (window_corner[0, 0] + PATCH // 2) * node_rows // tile_size
    centre_x = (window_corner[1, 0] + PATCH // 2) * node_cols // tile_size
    attach = (centre_y[:, None, None] == jnp.arange(node_rows, dtype=jnp.int32)[None, :, None]) & (
        centre_x[:, None, None] == jnp.arange(node_cols, dtype=jnp.int32)[None, None, :]
    )
    count = jnp.sum(attach.astype(f32), axis=0)
    mask = node_mask.astype(f32)
    w = ITERS_R
    arrived = lax.all_to_all(outgoing, "tx", split_axis=0, concat_axis=0, tiled=True)
    b_tall = padded_2(section_b, (("ty", 0),), RADIUS)
    b_wide = padded_2(b_tall.T, (("tx", 0),), RADIUS).T

    wrow_pick = one_hot(window_corner[0, 0], WIN, b_wide.shape[0])
    wcol_pick = one_hot(window_corner[1, 0], WIN, b_wide.shape[1])
    by_row = jnp.einsum("mra,ac->mrc", wrow_pick, b_wide, preferred_element_type=f32)
    windows = jnp.einsum(
        "mrc,msc->mrs", by_row.astype(jnp.bfloat16), wcol_pick, preferred_element_type=f32
    ).astype(jnp.bfloat16)
    matched = jnp.einsum(
        "ms,sri->mri", source_picker.astype(jnp.bfloat16), arrived, preferred_element_type=f32
    ).astype(jnp.bfloat16)

    flows = flows_of(matched, windows)
    source_flow = -flows

    target = jnp.sum(jnp.where(attach[None], source_flow[:, :, None, None], 0.0), axis=1)
    fields = jnp.concatenate([target, count[None], mask[None]], axis=0)
    returned = jnp.sum(jnp.where(source_picker[None], flows[:, :, None], 0.0), axis=1)
    lane = 128
    sides = side_payload(fields[:, :, 0:w], fields[:, :, node_cols - w :])
    flows_out = returned.reshape(2, n_tx, CAP).transpose(1, 0, 2).reshape(n_tx, -1)
    side_len = sides.shape[1]
    chunk = -(-(side_len + flows_out.shape[1]) // lane) * lane
    back = jnp.concatenate(
        [sides, flows_out, jnp.zeros((n_tx, chunk - side_len - flows_out.shape[1]), f32)], axis=1
    ).reshape(n_tx, chunk // lane, lane)
    came = lax.all_to_all(back, "tx", split_axis=0, concat_axis=0, tiled=True).reshape(n_tx, chunk)
    landed = came[:, side_len : side_len + 2 * CAP].reshape(n_tx, 2, CAP).transpose(1, 0, 2).reshape(2, -1)
    owner_flow = jnp.sum(jnp.where(owner_picker[None], landed[:, None, :], 0.0), axis=2)
    f_left, f_right = side_arrivals(came[:, 0:side_len], (fields.shape[0], node_rows, w))
    fields_tx = jnp.concatenate([f_left, fields, f_right], axis=2)
    f_above, f_below = rows_exchange(fields_tx, w)
    wide = jnp.concatenate([f_above, fields_tx, f_below], axis=1)

    displace = jnp.zeros((2,) + wide.shape[1:], f32)
    for sweep in range(ITERS_R):
        lo_m, hi_m = sweep, wide.shape[1] - sweep
        lo_t, hi_t = sweep + 1, wide.shape[1] - sweep - 1
        displace = relax_sweep(
            displace,
            wide[3, lo_m:hi_m, lo_m:hi_m],
            wide[0:2, lo_t:hi_t, lo_t:hi_t],
            wide[2, lo_t:hi_t, lo_t:hi_t],
        )
    return (owner_flow[:, None, :], source_flow[:, None, :], displace)


def solution(mesh):
    placed = (
        P("ty", "tx"),
        P("ty", "tx"),
        P(None, "ty", "tx"),
        P("ty", "tx"),
        P(None, "ty", "tx"),
        P("ty", "tx"),
        P("ty", "tx"),
    )
    return jax.shard_map(
        shards,
        mesh=mesh,
        in_specs=placed,
        out_specs=(P(None, "ty", "tx"), P(None, "ty", "tx"), P(None, "ty", "tx")),
        check_vma=False,
    )
```

```python
import jax
import jax.numpy as jnp
from jax import lax
from jax.sharding import PartitionSpec as P
from jax.experimental import pallas as pl
from jax.experimental.pallas import tpu as pltpu

PATCH = 128
SHIFTS = 65
RADIUS = 32
WIN = 192
CAP = 2
ITERS_R = 3


SHARPNESS = 256.0
SPRING_RATE = 0.25
FLOW_RATE = 0.5
FLOW_UNIT = 8.0
EPSILON = 1e-05

HALF = PATCH // 2
PER = 8


def flow_kernel(tf_ref, w_ref, out_ref, wlo, whi, corr):
    cats = []
    for q in range(PER):
        wf = w_ref[q].astype(jnp.float32)
        wlo[q] = wf[:, 0:PATCH]
        whi[q] = jnp.zeros(whi.shape[1:], jnp.float32)
        whi[q, :, 0:WIN - HALF] = wf[:, HALF:WIN]
        cats.append(jnp.concatenate([tf_ref[q, 0:HALF, :], tf_ref[q, HALF:PATCH, :]], axis=1))
        corr[q] = jnp.zeros(corr.shape[1:], jnp.float32)
    for dy in range(SHIFTS):
        for q in range(PER):
            w_cat = jnp.concatenate(
                [whi[q, dy : dy + PATCH, :], wlo[q, dy : dy + PATCH, :]], axis=0
            ).astype(jnp.bfloat16)
            m = jnp.dot(cats[q], w_cat, preferred_element_type=jnp.float32)
            r = pltpu.roll(m, 0, axis=1, stride=1, stride_axis=0)
            corr[q, dy : dy + 1, :] = jnp.sum(r, axis=0, keepdims=True)
    for q in range(PER):
        _epilogue(tf_ref, w_ref, out_ref, corr, q)


def _epilogue(tf_ref, w_ref, out_ref, corr, q):
    wf = w_ref[q].astype(jnp.float32)
    tfv = tf_ref[q].astype(jnp.float32)
    c = corr[q]
    rows = lax.broadcasted_iota(jnp.int32, c.shape, 0)
    lanes = lax.broadcasted_iota(jnp.int32, c.shape, 1)
    valid = (rows < SHIFTS) & (lanes >= HALF - 1)
    e_t = jnp.sum(tfv * tfv, keepdims=True) / float(PATCH * PATCH)
    e_w = jnp.sum(wf * wf, keepdims=True) / float(WIN * WIN)
    denom = float(PATCH * PATCH) * jnp.sqrt((e_t + EPSILON) * (e_w + EPSILON))
    scores = SHARPNESS * c / denom
    scores = jnp.where(valid, scores, -jnp.inf)
    mx = jnp.max(scores, keepdims=True)
    e = jnp.where(valid, jnp.exp(scores - mx), 0.0)
    w = e / jnp.sum(e, keepdims=True)
    sy = (rows - RADIUS).astype(jnp.float32)
    sx = (lanes - (HALF - 1) - RADIUS).astype(jnp.float32)
    fy = jnp.sum(w * sy, keepdims=True) / FLOW_UNIT
    fx = jnp.sum(w * sx, keepdims=True) / FLOW_UNIT
    orow = lax.broadcasted_iota(jnp.int32, (8, 128), 0)
    out_ref[q] = jnp.where(orow == 0, fy, jnp.where(orow == 1, fx, 0.0))

def flows_of(tflipped, windows):
    n = tflipped.shape[0]
    out = pl.pallas_call(
        flow_kernel,
        grid=(n // PER,),
        in_specs=[pl.BlockSpec((PER, PATCH, PATCH), lambda i: (i, 0, 0)),
                  pl.BlockSpec((PER, WIN, WIN), lambda i: (i, 0, 0))],
        out_specs=pl.BlockSpec((PER, 8, 128), lambda i: (i, 0, 0)),
        out_shape=jax.ShapeDtypeStruct((n, 8, 128), jnp.float32),
        scratch_shapes=[pltpu.VMEM((PER, WIN, PATCH), jnp.float32),
                        pltpu.VMEM((PER, WIN, PATCH), jnp.float32),
                        pltpu.VMEM((PER, 72, PATCH), jnp.float32)],
    )(tflipped, windows)
    return out[:, 0:2, 0].T


def padded_2(cells, sides, width):
    for axis, dim in sides:
        count = lax.axis_size(axis)
        ends = count - 1
        head = lax.slice_in_dim(cells, 0, width, axis=dim)
        tail = lax.slice_in_dim(cells, cells.shape[dim] - width, cells.shape[dim], axis=dim)
        cells = jnp.concatenate(
            [
                lax.ppermute(tail, axis, [(i, (i + 1) % count) for i in range(ends)]),
                cells,
                lax.ppermute(head, axis, [((i + 1) % count, i) for i in range(ends)]),
            ],
            axis=dim,
        )
    return cells


def halo(cells, width):
    n_ty = lax.axis_size("ty")
    n_tx = lax.axis_size("tx")
    height, breadth = cells.shape[-2], cells.shape[-1]
    pieces = {}
    for dy in (-1, 0, 1):
        for dx in (-1, 0, 1):
            if dy == 0 and dx == 0:
                pieces[(dy, dx)] = cells
                continue
            rows = {-1: (height - width, height), 0: (0, height), 1: (0, width)}[dy]
            cols = {-1: (breadth - width, breadth), 0: (0, breadth), 1: (0, width)}[dx]
            part = cells[..., rows[0] : rows[1], cols[0] : cols[1]]
            pairs = []
            for i in range(n_ty):
                for j in range(n_tx):
                    si, sj = i + dy, j + dx
                    if 0 <= si < n_ty and 0 <= sj < n_tx:
                        pairs.append((si * n_tx + sj, i * n_tx + j))
            pieces[(dy, dx)] = lax.ppermute(part, ("ty", "tx"), pairs)
    bands = [
        jnp.concatenate([pieces[(dy, -1)], pieces[(dy, 0)], pieces[(dy, 1)]], axis=-1)
        for dy in (-1, 0, 1)
    ]
    return jnp.concatenate(bands, axis=-2)


def relax_sweep(padded, mask_pad, target, count):
    centre = padded[:, 1:-1, 1:-1]
    mask_c = mask_pad[1:-1, 1:-1]
    height = centre.shape[1]
    width = centre.shape[2]
    spring = jnp.zeros_like(centre)
    for row_step, col_step in ((0, 1), (2, 1), (1, 0), (1, 2)):
        nearby = padded[:, row_step : row_step + height, col_step : col_step + width]
        mask_n = mask_pad[row_step : row_step + height, col_step : col_step + width]
        spring = spring + mask_c * mask_n * (nearby - centre)
    return centre + SPRING_RATE * spring + FLOW_RATE * (target - count * centre)


def one_hot(starts, size, extent, flip=False):
    offs = jnp.arange(size, dtype=jnp.int32)
    if flip:
        offs = size - 1 - offs
    want = starts[:, None, None] + offs[None, :, None]
    return (want == jnp.arange(extent, dtype=jnp.int32)[None, None, :]).astype(jnp.bfloat16)


def shards(
    section_a, section_b, template_corner, template_slot, window_corner, window_slot, node_mask
):
    tile_size = section_a.shape[0]
    slot_count = lax.axis_size("tx") * CAP
    slot_ids = jnp.arange(slot_count, dtype=jnp.int32)
    owner_picker = template_slot[0][:, None] == slot_ids[None, :]
    source_picker = window_slot[0][:, None] == slot_ids[None, :]
    f32 = jnp.float32

    col_pick = one_hot(template_corner[1, 0], PATCH, section_a.shape[1], flip=True)
    row_pick = one_hot(template_corner[0, 0], PATCH, section_a.shape[0])
    by_col = jnp.einsum("krc,ac->kra", col_pick, section_a, preferred_element_type=f32)
    tflipped = jnp.einsum(
        "kra,kia->kri", by_col.astype(jnp.bfloat16), row_pick, preferred_element_type=f32
    ).astype(jnp.bfloat16)
    outgoing = jnp.einsum(
        "ks,kri->sri", owner_picker.astype(jnp.bfloat16), tflipped, preferred_element_type=f32
    ).astype(jnp.bfloat16)

    n_tx = lax.axis_size("tx")
    n_ty = lax.axis_size("ty")
    me_x = lax.axis_index("tx")
    tx_ids = jnp.arange(n_tx, dtype=jnp.int32)
    to_left = (tx_ids == me_x - 1)[:, None]
    to_right = (tx_ids == me_x + 1)[:, None]

    def side_payload(left, right):
        lf = left.reshape(1, -1)
        rf = right.reshape(1, -1)
        return jnp.where(to_left, lf, jnp.where(to_right, rf, jnp.zeros_like(lf)))

    def side_arrivals(got, shape):
        left = lax.dynamic_index_in_dim(got, jnp.maximum(me_x - 1, 0), axis=0, keepdims=False)
        right = lax.dynamic_index_in_dim(got, jnp.minimum(me_x + 1, n_tx - 1), axis=0, keepdims=False)
        left = jnp.where(me_x >= 1, left, jnp.zeros_like(left)).reshape(shape)
        right = jnp.where(me_x + 1 < n_tx, right, jnp.zeros_like(right)).reshape(shape)
        return left, right

    def rows_exchange(cells, width):
        count = n_ty
        height = cells.shape[-2]
        head = cells[..., 0:width, :]
        tail = cells[..., height - width : height, :]
        above = lax.ppermute(tail, "ty", [(i, i + 1) for i in range(count - 1)])
        below = lax.ppermute(head, "ty", [(i + 1, i) for i in range(count - 1)])
        return above, below

    node_rows, node_cols = node_mask.shape
    centre_y = (window_corner[0, 0] + PATCH // 2) * node_rows // tile_size
    centre_x = (window_corner[1, 0] + PATCH // 2) * node_cols // tile_size
    attach = (centre_y[:, None, None] == jnp.arange(node_rows, dtype=jnp.int32)[None, :, None]) & (
        centre_x[:, None, None] == jnp.arange(node_cols, dtype=jnp.int32)[None, None, :]
    )
    count = jnp.sum(attach.astype(f32), axis=0)
    mask = node_mask.astype(f32)
    w = ITERS_R
    arrived = lax.all_to_all(outgoing, "tx", split_axis=0, concat_axis=0, tiled=True)
    b_tall = padded_2(section_b, (("ty", 0),), RADIUS)
    b_wide = padded_2(b_tall.T, (("tx", 0),), RADIUS).T

    wrow_pick = one_hot(window_corner[0, 0], WIN, b_wide.shape[0])
    wcol_pick = one_hot(window_corner[1, 0], WIN, b_wide.shape[1])
    by_row = jnp.einsum("mra,ac->mrc", wrow_pick, b_wide, preferred_element_type=f32)
    windows = jnp.einsum(
        "mrc,msc->mrs", by_row.astype(jnp.bfloat16), wcol_pick, preferred_element_type=f32
    ).astype(jnp.bfloat16)
    matched = jnp.einsum(
        "ms,sri->mri", source_picker.astype(jnp.bfloat16), arrived, preferred_element_type=f32
    ).astype(jnp.bfloat16)

    flows = flows_of(matched, windows)
    source_flow = -flows

    target = jnp.sum(jnp.where(attach[None], source_flow[:, :, None, None], 0.0), axis=1)
    fields = jnp.concatenate([target, count[None], mask[None]], axis=0)
    returned = jnp.sum(jnp.where(source_picker[None], flows[:, :, None], 0.0), axis=1)
    lane = 128
    sides = side_payload(fields[:, :, 0:w], fields[:, :, node_cols - w :])
    flows_out = returned.reshape(2, n_tx, CAP).transpose(1, 0, 2).reshape(n_tx, -1)
    side_len = sides.shape[1]
    chunk = -(-(side_len + flows_out.shape[1]) // lane) * lane
    back = jnp.concatenate(
        [sides, flows_out, jnp.zeros((n_tx, chunk - side_len - flows_out.shape[1]), f32)], axis=1
    ).reshape(n_tx, chunk // lane, lane)
    came = lax.all_to_all(back, "tx", split_axis=0, concat_axis=0, tiled=True).reshape(n_tx, chunk)
    landed = came[:, side_len : side_len + 2 * CAP].reshape(n_tx, 2, CAP).transpose(1, 0, 2).reshape(2, -1)
    owner_flow = jnp.sum(jnp.where(owner_picker[None], landed[:, None, :], 0.0), axis=2)
    f_left, f_right = side_arrivals(came[:, 0:side_len], (fields.shape[0], node_rows, w))
    fields_tx = jnp.concatenate([f_left, fields, f_right], axis=2)
    f_above, f_below = rows_exchange(fields_tx, w)
    wide = jnp.concatenate([f_above, fields_tx, f_below], axis=1)

    displace = jnp.zeros((2,) + wide.shape[1:], f32)
    for sweep in range(ITERS_R):
        lo_m, hi_m = sweep, wide.shape[1] - sweep
        lo_t, hi_t = sweep + 1, wide.shape[1] - sweep - 1
        displace = relax_sweep(
            displace,
            wide[3, lo_m:hi_m, lo_m:hi_m],
            wide[0:2, lo_t:hi_t, lo_t:hi_t],
            wide[2, lo_t:hi_t, lo_t:hi_t],
        )
    return (owner_flow[:, None, :], source_flow[:, None, :], displace)


def solution(mesh):
    placed = (
        P("ty", "tx"),
        P("ty", "tx"),
        P(None, "ty", "tx"),
        P("ty", "tx"),
        P(None, "ty", "tx"),
        P("ty", "tx"),
        P("ty", "tx"),
    )
    return jax.shard_map(
        shards,
        mesh=mesh,
        in_specs=placed,
        out_specs=(P(None, "ty", "tx"), P(None, "ty", "tx"), P(None, "ty", "tx")),
        check_vma=False,
    )
```
